256 devices in a mesh: curve: 16 (over y, x), line: 16 (over z, core).
Axes of the slice: x: 4, y: 4, z: 8, core: 2. Of those that a mesh axis runs over, the one named last changes fastest.
Arguments:
- scaled_distributions: float32 [16, 16, 6, 27, 512], P('curve', 'line'), may hold values from 0.1 to 2.5, as said below
- remaining_brick_places: int32 [16, 16, 6], P('curve', 'line'), may hold values from -1 to 7, as said below
- retained_wavenumbers: int32 [8], replicated, may hold values from 1 to 16, as said below
- regional_amplitudes: float32 [3, 2, 512, 16], P(None, None, 'curve'), may hold values from -0.12 to 0.12
- relaxation_frequencies: float32 [27], replicated, may hold values from 0.6 to 1.8
Outputs:
- new_populations: float32 [16, 16, 6, 27, 512], P('curve', 'line')
The draws below stay inside these ranges and needn't reach their ends.
Inputs may be any that keep to these rules, and one draw needn't show every extreme that they name: `scaled_distributions`: positive values. `remaining_brick_places`: distinct tile positions (row of the block times 4 plus its column) of one device's surviving blocks, -1 in empty slots, which may stand anywhere; at least half of each device's slots are used, and on some device all 6 are. `retained_wavenumbers`: distinct mode numbers; 16 is always among them.
All inputs are finite; a program needn't handle non-finite values.
Results may differ from the reference program's by a relative error of at most 0.0003.
Values sent between devices are 32-bit elements; how exact they have to be, the bound alone decides.
No kernel may reach another device: no remote copies, remote signals or barrier semaphores. Data moves between devices by JAX's collectives and lax.ppermute only.
A program may use at most 64 MiB of HBM per device.

```python
import jax
import jax.numpy as jnp
import numpy as np
from jax import lax

BE = 16
LEVELS = 2
TX = 4
TY = 2
KEEP = 8
KMAX = 16
MAX_SEATS_CHIP = 6
GRID_SITES_EACH = 512
NX = 1024
NY = 512
N_CURVE = 16
N_LINE = 16


def draw_scaled_distributions(key, part):
    lead_shape = (N_CURVE, N_LINE, MAX_SEATS_CHIP, 1, GRID_SITES_EACH)
    line_place = jnp.arange(N_LINE, dtype=jnp.float32).reshape(1, N_LINE, 1, 1, 1)
    phases = jax.random.uniform(jax.random.fold_in(key, 1), (N_CURVE, 1, 1, 1, 1), jnp.float32, 0.0, 6.2831855)
    wave_angle = 6.2831855 * (line_place + 0.5) / N_LINE + phases
    density_low = 0.9
    density_high = 1.1
    noise_size = 0.25
    wind_x = 0.03 * jnp.sin(wave_angle) + jax.random.uniform(jax.random.fold_in(key, 2), lead_shape, jnp.float32, -0.03, 0.03)
    wind_y = 0.03 * jnp.cos(wave_angle) + jax.random.uniform(jax.random.fold_in(key, 3), lead_shape, jnp.float32, -0.03, 0.03)
    wind_z = jax.random.uniform(jax.random.fold_in(key, 4), lead_shape, jnp.float32, -0.015, 0.015)
    density = jax.random.uniform(jax.random.fold_in(key, 5), lead_shape, jnp.float32, density_low, density_high)
    noise_draw = jax.random.uniform(jax.random.fold_in(key, 6), (N_CURVE, N_LINE, MAX_SEATS_CHIP, 27, GRID_SITES_EACH), jnp.float32, -1.0, 1.0)
    numbers = jnp.arange(27, dtype=jnp.int32)
    speed_x = (numbers // 9 - 1).astype(jnp.float32).reshape(1, 1, 1, 27, 1)
    speed_y = (numbers // 3 % 3 - 1).astype(jnp.float32).reshape(1, 1, 1, 27, 1)
    speed_z = (numbers % 3 - 1).astype(jnp.float32).reshape(1, 1, 1, 27, 1)
    drift = 3.0 * (speed_x * wind_x + speed_y * wind_y + speed_z * wind_z)
    return density * (1.0 + drift + noise_size * noise_draw)


def draw_remaining_brick_places(key, part):
    chip_tally = N_CURVE * N_LINE
    tile_count = TX * TY
    device_keys = jax.random.split(jax.random.fold_in(key, 21), chip_tally)
    tile_sequence = jax.vmap(lambda single: jax.random.permutation(single, tile_count))(device_keys)[:, :MAX_SEATS_CHIP]
    rank_keys = jax.random.split(jax.random.fold_in(key, 22), chip_tally)
    slot_positions = jax.vmap(lambda single: jax.random.permutation(single, MAX_SEATS_CHIP))(rank_keys)
    block_counts = MAX_SEATS_CHIP - jax.random.randint(jax.random.fold_in(key, 23), (chip_tally,), 0, MAX_SEATS_CHIP // 2 + 1)
    fullest = jax.random.randint(jax.random.fold_in(key, 24), (), 0, chip_tally)
    block_counts = jnp.where(jnp.arange(chip_tally) == fullest, MAX_SEATS_CHIP, block_counts)
    kept_block_ids = jnp.where(slot_positions < block_counts[:, None], tile_sequence, -1)
    return kept_block_ids.reshape(N_CURVE, N_LINE, MAX_SEATS_CHIP).astype(jnp.int32)


def draw_retained_wavenumbers(key, part):
    others = jax.random.permutation(jax.random.fold_in(key, 31), KMAX - 1)[:KEEP - 1] + 1
    return jnp.concatenate([jnp.array([KMAX], dtype=jnp.int32), others.astype(jnp.int32)])


def level_of(stream_key, extent, pieces, least, top_value):
    gain, own = 1.0, jax.random.fold_in(stream_key, 6)
    for axis_at, blocks in pieces:
        heights = jnp.exp(jax.random.uniform(jax.random.fold_in(own, axis_at), (blocks,), jnp.float32, least / len(pieces), top_value / len(pieces)))
        gain = gain * jnp.repeat(heights, extent[axis_at] // blocks).reshape([-1 if axis == axis_at else 1 for axis in range(len(extent))])
    return gain


def centred(stream_key, dims, spread, limit, pieces=(), kind=jnp.bfloat16):
    result = jax.random.normal(stream_key, dims, jnp.float32) * spread
    if len(pieces) > 0:
        result = level_of(stream_key, dims, pieces, -0.22, 0.18) * result
    return jnp.clip(result, min=-limit, max=limit).astype(kind)


def setup_inputs(seed: int = 0) -> dict:
    key_list = jax.random.split(jax.random.key(seed), 6)
    return {
        "scaled_distributions": draw_scaled_distributions(jax.random.fold_in(key_list[5], 71), 0),
        "remaining_brick_places": draw_remaining_brick_places(jax.random.fold_in(key_list[5], 71), 0),
        "retained_wavenumbers": draw_retained_wavenumbers(jax.random.fold_in(key_list[5], 71), 0),
        "regional_amplitudes": centred(key_list[3], (3, LEVELS, NY, 2 * KEEP), 0.04, 0.12, ((2, 16),), jnp.float32),
        "relaxation_frequencies": jnp.clip(jax.random.uniform(key_list[4], (27,), jnp.float32, 0.6, 1.8), 0.6, 1.8),
    }


NUDGE_GAIN = 0.5
TWO_PI = 6.283185307179586
HIGHEST = lax.Precision.HIGHEST


def lattice_tables():
    one_weights = np.array([1.0 / 6.0, 2.0 / 3.0, 1.0 / 6.0])
    speeds = np.array([[along_x - 1, along_y - 1, along_z - 1] for along_x in range(3) for along_y in range(3) for along_z in range(3)])
    weights = np.array([one_weights[along_x] * one_weights[along_y] * one_weights[along_z] for along_x in range(3) for along_y in range(3) for along_z in range(3)])
    vander = np.array([[1.0, 1.0, 1.0], [-1.0, 0.0, 1.0], [1.0, 0.0, 1.0]])
    undo_vander = np.array([[0.0, -0.5, 0.5], [1.0, 0.0, -1.0], [0.0, 0.5, 0.5]])
    moment_matrix = np.kron(vander, np.kron(vander, vander))
    inverse = np.kron(undo_vander, np.kron(undo_vander, undo_vander))
    forward = jnp.asarray(moment_matrix * weights[None, :], dtype=jnp.float32)
    backward = jnp.asarray(inverse / weights[:, None], dtype=jnp.float32)
    return forward, backward, speeds


def mode_basis_at(mode_ids, positions, length):
    phase_ids = (positions[:, None] * mode_ids[None, :]) % length
    angles = phase_ids.astype(jnp.float32) * (TWO_PI / length)
    return jnp.concatenate([jnp.cos(angles), jnp.sin(angles)], axis=1)


def cell_moments(device_pops, forward):
    return jnp.einsum('ij,bjc->bic', forward, device_pops, precision=HIGHEST)


def velocity_from(moments):
    return jnp.stack([moments[:, 9], moments[:, 3], moments[:, 1]], axis=1) / moments[:, 0][:, None]


def collide(moments, device_nudge, backward, relaxation_frequencies):
    density = moments[:, 0]
    shifted = velocity_from(moments) + device_nudge
    powers = jnp.stack([jnp.ones_like(shifted), shifted, shifted * shifted + 1.0 / 3.0], axis=1)
    equilibrium = density[:, None, None, None, :] * powers[:, :, None, None, 0] * powers[:, None, :, None, 1] * powers[:, None, None, :, 2]
    equilibrium = equilibrium.reshape(moments.shape)
    relaxed = moments - relaxation_frequencies[None, :, None] * (moments - equilibrium)
    return jnp.einsum('ij,bjc->bic', backward, relaxed, precision=HIGHEST)


def grid_pointers(remaining_brick_places):
    curve_ids = jnp.arange(N_CURVE, dtype=jnp.int32)[:, None, None]
    line_ids = jnp.arange(N_LINE, dtype=jnp.int32)[None, :, None]
    occupied_seats = remaining_brick_places >= 0
    bounded_labels = jnp.maximum(remaining_brick_places, 0)
    row_base = (curve_ids * TY + bounded_labels // TX) * BE
    col_base = (line_ids * TX + bounded_labels % TX) * BE
    within = jnp.arange(BE, dtype=jnp.int32)
    horizontal_label = row_base[..., None, None] + within[:, None]
    vertical_label = col_base[..., None, None] + within[None, :]
    return horizontal_label, vertical_label, occupied_seats


def seats_onto_full(packed_arrangement, remaining_brick_places):
    horizontal_label, vertical_label, occupied_seats = grid_pointers(remaining_brick_places)
    channels = packed_arrangement.shape[3]
    values = packed_arrangement.reshape(N_CURVE, N_LINE, MAX_SEATS_CHIP, channels, LEVELS, BE, BE).transpose(3, 4, 0, 1, 2, 5, 6)
    rows_drop = jnp.where(occupied_seats[..., None, None], horizontal_label, NY + BE)
    full_arrangement = jnp.zeros((channels, LEVELS, NY, NX), packed_arrangement.dtype)
    return full_arrangement.at[:, :, rows_drop, vertical_label].set(values, mode="drop")


def full_onto_seats(full_arrangement, remaining_brick_places):
    horizontal_label, vertical_label, occupied_seats = grid_pointers(remaining_brick_places)
    channels = full_arrangement.shape[0]
    picked = full_arrangement[:, :, horizontal_label, vertical_label]
    picked = picked.transpose(2, 3, 4, 0, 1, 5, 6).reshape(N_CURVE, N_LINE, MAX_SEATS_CHIP, channels, GRID_SITES_EACH)
    return picked * occupied_seats[..., None, None].astype(full_arrangement.dtype)


def reference(scaled_distributions, remaining_brick_places, retained_wavenumbers, regional_amplitudes, relaxation_frequencies):
    forward, backward, speeds = lattice_tables()
    chip_tally = N_CURVE * N_LINE
    flat_pops = scaled_distributions.reshape(chip_tally, MAX_SEATS_CHIP, 27, GRID_SITES_EACH)
    stream_speed_vector = lax.map(lambda device_pops: velocity_from(cell_moments(device_pops, forward)), flat_pops)
    breeze_region = seats_onto_full(stream_speed_vector.reshape(N_CURVE, N_LINE, MAX_SEATS_CHIP, 3, GRID_SITES_EACH), remaining_brick_places)
    mode_basis = mode_basis_at(retained_wavenumbers, jnp.arange(NX, dtype=jnp.int32), NX)
    coefficients = jnp.einsum('klyx,xm->klym', breeze_region, mode_basis, precision=HIGHEST)
    misfit = regional_amplitudes - (2.0 / NX) * coefficients
    forcing_adjustment = NUDGE_GAIN * jnp.einsum('klym,xm->klyx', misfit, mode_basis, precision=HIGHEST)
    forced_sites = full_onto_seats(forcing_adjustment, remaining_brick_places).reshape(chip_tally, MAX_SEATS_CHIP, 3, GRID_SITES_EACH)
    relaxed_populace = lax.map(lambda pair_args: collide(cell_moments(pair_args[0], forward), pair_args[1], backward, relaxation_frequencies), (flat_pops, forced_sites))
    relaxed_populace = relaxed_populace.reshape(N_CURVE, N_LINE, MAX_SEATS_CHIP, 27, GRID_SITES_EACH)
    liquid_region = seats_onto_full(jnp.ones((N_CURVE, N_LINE, MAX_SEATS_CHIP, 1, GRID_SITES_EACH), jnp.float32), remaining_brick_places)[0, 0]
    solid_grid = liquid_region < 0.5
    portion_catalog = []
    for discrete_heading in range(27):
        carry_eastward = int(speeds[discrete_heading, 0])
        carry_northward = int(speeds[discrete_heading, 1])
        step_z = int(speeds[discrete_heading, 2])
        carried_sheet = jnp.roll(seats_onto_full(relaxed_populace[:, :, :, discrete_heading:discrete_heading + 1], remaining_brick_places)[0], (carry_northward, carry_eastward), axis=(1, 2))
        blocked = jnp.roll(solid_grid, (carry_northward, carry_eastward), axis=(0, 1))
        bounced_distributions = seats_onto_full(relaxed_populace[:, :, :, 26 - discrete_heading:27 - discrete_heading], remaining_brick_places)[0]
        if step_z == 0:
            source = carried_sheet
            block_both = jnp.stack([blocked, blocked])
        elif step_z == 1:
            source = jnp.stack([carried_sheet[0], carried_sheet[0]])
            block_both = jnp.stack([jnp.ones_like(blocked), blocked])
        else:
            mirror_sheet = jnp.roll(seats_onto_full(relaxed_populace[:, :, :, discrete_heading + 2:discrete_heading + 3], remaining_brick_places)[0], (carry_northward, carry_eastward), axis=(1, 2))
            source = jnp.stack([carried_sheet[1], mirror_sheet[1]])
            block_both = jnp.stack([blocked, blocked])
        update_outcome = jnp.where(block_both, bounced_distributions, source)
        portion_catalog.append(full_onto_seats(update_outcome[None], remaining_brick_places))
    return jnp.concatenate(portion_catalog, axis=3)
```

```python
import jax
import jax.numpy as jnp
import numpy as np
from jax import lax
from jax.sharding import PartitionSpec as P

BE = 16
TX = 4
TY = 2


NUDGE_GAIN = 0.5
TWO_PI = 6.283185307179586
HIGHEST = lax.Precision.HIGHEST


def with_halo(block, sides, width):
    for axis, dim in sides:
        count = lax.axis_size(axis)
        forward = [(i, i + 1) for i in range(count - 1)]
        forward.append((count - 1, 0))
        backward = [(target, source) for source, target in forward]
        low = lax.ppermute(
            lax.slice_in_dim(block, block.shape[dim] - width, None, axis=dim), axis, forward
        )
        high = lax.ppermute(lax.slice_in_dim(block, 0, width, axis=dim), axis, backward)
        block = jnp.concatenate([low, block, high], axis=dim)
    return block


def lattice_tables():
    one_weights = np.array([1.0 / 6.0, 2.0 / 3.0, 1.0 / 6.0])
    speeds = np.array(
        [
            [along_x - 1, along_y - 1, along_z - 1]
            for along_x in range(3)
            for along_y in range(3)
            for along_z in range(3)
        ]
    )
    weights = np.array(
        [
            one_weights[along_x] * one_weights[along_y] * one_weights[along_z]
            for along_x in range(3)
            for along_y in range(3)
            for along_z in range(3)
        ]
    )
    vander = np.array([[1.0, 1.0, 1.0], [-1.0, 0.0, 1.0], [1.0, 0.0, 1.0]])
    undo_vander = np.array([[0.0, -0.5, 0.5], [1.0, 0.0, -1.0], [0.0, 0.5, 0.5]])
    moment_matrix = np.kron(vander, np.kron(vander, vander))
    inverse = np.kron(undo_vander, np.kron(undo_vander, undo_vander))
    forward = jnp.asarray(moment_matrix * weights[None, :], dtype=jnp.float32)
    backward = jnp.asarray(inverse / weights[:, None], dtype=jnp.float32)
    return (forward, backward, speeds)


def mode_basis_at(mode_ids, positions, length):
    phase_ids = positions[:, None] * mode_ids[None, :] % length
    angles = phase_ids.astype(jnp.float32) * (TWO_PI / length)
    return jnp.concatenate([jnp.cos(angles), jnp.sin(angles)], axis=1)


def tile_velocity(moments, safe_density):
    return jnp.stack([moments[9], moments[3], moments[1]], axis=0) / safe_density[None]


def collide_tile(moments, velocity, nudge_tile, backward, relaxation_frequencies):
    density = moments[0]
    shifted = velocity + nudge_tile
    powers = jnp.stack([jnp.ones_like(shifted), shifted, shifted * shifted + 1.0 / 3.0], axis=0)
    equilibrium = (
        density[None, None, None]
        * powers[:, None, None, 0]
        * powers[None, :, None, 1]
        * powers[None, None, :, 2]
    )
    equilibrium = equilibrium.reshape(moments.shape)
    relaxed = moments - relaxation_frequencies[:, None, None, None] * (moments - equilibrium)
    return jnp.einsum("ij,jlrc->ilrc", backward, relaxed, precision=HIGHEST)


def slot_lookup(living_brick_keys, tile_blocks):
    positions = jnp.arange(tile_blocks, dtype=jnp.int32)
    matches = living_brick_keys[None, :] == positions[:, None]
    slot_numbers = jnp.arange(living_brick_keys.shape[0], dtype=jnp.int32)
    slot_of = jnp.sum(jnp.where(matches, slot_numbers[None, :], 0), axis=1)
    present = jnp.any(matches, axis=1)
    return (slot_of, present)


def compact_to_tile(packed_arrangement, slot_of, present, rows_blocks, cols_blocks, block_edge):
    channels = packed_arrangement.shape[1]
    levels = packed_arrangement.shape[2] // (block_edge * block_edge)
    picked = jnp.take(packed_arrangement, slot_of, axis=0) * present[:, None, None].astype(
        packed_arrangement.dtype
    )
    shaped = picked.reshape(rows_blocks, cols_blocks, channels, levels, block_edge, block_edge)
    return shaped.transpose(2, 3, 0, 4, 1, 5).reshape(
        channels, levels, rows_blocks * block_edge, cols_blocks * block_edge
    )


def tile_to_compact(tile_data, living_brick_keys, rows_blocks, cols_blocks, block_edge):
    channels = tile_data.shape[0]
    levels = tile_data.shape[1]
    shaped = tile_data.reshape(
        channels, levels, rows_blocks, block_edge, cols_blocks, block_edge
    ).transpose(2, 4, 0, 1, 3, 5)
    blocks = shaped.reshape(rows_blocks * cols_blocks, channels, levels * block_edge * block_edge)
    occupied_seats = living_brick_keys >= 0
    picked = jnp.take(blocks, jnp.maximum(living_brick_keys, 0), axis=0)
    return picked * occupied_seats[:, None, None].astype(tile_data.dtype)


def on_device(
    scaled_distributions,
    remaining_brick_places,
    retained_wavenumbers,
    regional_amplitudes,
    relaxation_frequencies,
):
    forward, backward, speeds = lattice_tables()
    slot_state = scaled_distributions[0, 0]
    living_brick_keys = remaining_brick_places[0, 0]
    rows_tile = TY * BE
    cols_tile = TX * BE
    slot_of, present = slot_lookup(living_brick_keys, TX * TY)
    fluid_map = present.reshape(TY, TX).astype(jnp.float32)
    fluid_map = jnp.repeat(jnp.repeat(fluid_map, BE, axis=0), BE, axis=1)
    solid_tile = 1.0 - fluid_map
    pops_tile = compact_to_tile(slot_state, slot_of, present, TY, TX, BE)
    moments = jnp.einsum("ij,jlrc->ilrc", forward, pops_tile, precision=HIGHEST)
    safe_density = jnp.where(fluid_map[None] > 0.5, moments[0], 1.0)
    wind_tile = tile_velocity(moments, safe_density)
    line_length = lax.axis_size("line") * cols_tile
    own_columns = lax.axis_index("line") * cols_tile + jnp.arange(cols_tile, dtype=jnp.int32)
    mode_basis = mode_basis_at(retained_wavenumbers, own_columns, line_length)
    partial = jnp.einsum("klrx,xm->klrm", wind_tile, mode_basis, precision=HIGHEST)
    coefficients = lax.psum(partial, "line")
    misfit = regional_amplitudes - 2.0 / line_length * coefficients
    nudge_tile = NUDGE_GAIN * jnp.einsum(
        "klrm,xm->klrx", misfit, mode_basis, precision=HIGHEST
    )
    post_tile = collide_tile(moments, wind_tile, nudge_tile, backward, relaxation_frequencies)
    levels = post_tile.shape[1]
    solid_plane = jnp.broadcast_to(solid_tile[None, None], (1, levels, rows_tile, cols_tile))
    extended = jnp.concatenate([post_tile, solid_plane], axis=0)
    padded = with_halo(extended, (("curve", 2), ("line", 3)), 1)
    pops_pad = padded[:27]
    solid_pad = padded[27, 0]
    read = []
    for discrete_heading in range(27):
        carry_eastward = int(speeds[discrete_heading, 0])
        carry_northward = int(speeds[discrete_heading, 1])
        step_z = int(speeds[discrete_heading, 2])
        rows_slice = slice(1 - carry_northward, 1 - carry_northward + rows_tile)
        cols_slice = slice(1 - carry_eastward, 1 - carry_eastward + cols_tile)
        carried_sheet = pops_pad[discrete_heading, :, rows_slice, cols_slice]
        blocked = solid_pad[rows_slice, cols_slice] > 0.5
        bounced_distributions = post_tile[26 - discrete_heading]
        if step_z == 0:
            source = carried_sheet
            block_both = jnp.stack([blocked, blocked])
        elif step_z == 1:
            source = jnp.stack([carried_sheet[0], carried_sheet[0]])
            block_both = jnp.stack([jnp.ones_like(blocked), blocked])
        else:
            mirror_sheet = pops_pad[discrete_heading + 2, 1, rows_slice, cols_slice]
            source = jnp.stack([carried_sheet[1], mirror_sheet])
            block_both = jnp.stack([blocked, blocked])
        read.append(jnp.where(block_both, bounced_distributions, source))
    read_tile = jnp.stack(read, axis=0)
    new_state = tile_to_compact(read_tile, living_brick_keys, TY, TX, BE)
    return new_state[None, None]


def solution(mesh):
    return jax.shard_map(
        on_device,
        mesh=mesh,
        in_specs=(
            P("curve", "line", None, None, None),
            P("curve", "line", None),
            P(),
            P(None, None, "curve", None),
            P(),
        ),
        out_specs=P("curve", "line", None, None, None),
        check_vma=False,
    )
```

```python
import jax
import jax.numpy as jnp
import numpy as np
from jax import lax
from jax.sharding import PartitionSpec as P

BE = 16
TX = 4
TY = 2


NUDGE_GAIN = 0.5
TWO_PI = 6.283185307179586
HIGHEST = lax.Precision.HIGHEST


def with_halo(block, sides, width):
    for axis, dim in sides:
        count = lax.axis_size(axis)
        forward = [(i, i + 1) for i in range(count - 1)]
        forward.append((count - 1, 0))
        backward = [(target, source) for source, target in forward]
        low = lax.ppermute(
            lax.slice_in_dim(block, block.shape[dim] - width, None, axis=dim), axis, forward
        )
        high = lax.ppermute(lax.slice_in_dim(block, 0, width, axis=dim), axis, backward)
        block = jnp.concatenate([low, block, high], axis=dim)
    return block


def butterfly_sum(value, axis):
    count = lax.axis_size(axis)
    stride = 1
    while stride < count:
        value = value + lax.ppermute(value, axis, [(i, i ^ stride) for i in range(count)])
        stride *= 2
    return value


def lattice_tables():
    one_weights = np.array([1.0 / 6.0, 2.0 / 3.0, 1.0 / 6.0])
    speeds = np.array(
        [
            [along_x - 1, along_y - 1, along_z - 1]
            for along_x in range(3)
            for along_y in range(3)
            for along_z in range(3)
        ]
    )
    weights = np.array(
        [
            one_weights[along_x] * one_weights[along_y] * one_weights[along_z]
            for along_x in range(3)
            for along_y in range(3)
            for along_z in range(3)
        ]
    )
    vander = np.array([[1.0, 1.0, 1.0], [-1.0, 0.0, 1.0], [1.0, 0.0, 1.0]])
    undo_vander = np.array([[0.0, -0.5, 0.5], [1.0, 0.0, -1.0], [0.0, 0.5, 0.5]])
    moment_matrix = np.kron(vander, np.kron(vander, vander))
    inverse = np.kron(undo_vander, np.kron(undo_vander, undo_vander))
    forward = jnp.asarray(moment_matrix * weights[None, :], dtype=jnp.float32)
    backward = jnp.asarray(inverse / weights[:, None], dtype=jnp.float32)
    return (forward, backward, speeds)


def mode_basis_at(mode_ids, positions, length):
    phase_ids = positions[:, None] * mode_ids[None, :] % length
    angles = phase_ids.astype(jnp.float32) * (TWO_PI / length)
    return jnp.concatenate([jnp.cos(angles), jnp.sin(angles)], axis=1)


def tile_velocity(moments, safe_density):
    return jnp.stack([moments[9], moments[3], moments[1]], axis=0) / safe_density[None]


def collide_tile(moments, velocity, nudge_tile, backward, relaxation_frequencies):
    density = moments[0]
    shifted = velocity + nudge_tile
    powers = jnp.stack([jnp.ones_like(shifted), shifted, shifted * shifted + 1.0 / 3.0], axis=0)
    equilibrium = (
        density[None, None, None]
        * powers[:, None, None, 0]
        * powers[None, :, None, 1]
        * powers[None, None, :, 2]
    )
    equilibrium = equilibrium.reshape(moments.shape)
    relaxed = moments - relaxation_frequencies[:, None, None, None] * (moments - equilibrium)
    return jnp.einsum("ij,jlrc->ilrc", backward, relaxed, precision=HIGHEST)


def slot_lookup(living_brick_keys, tile_blocks):
    positions = jnp.arange(tile_blocks, dtype=jnp.int32)
    matches = living_brick_keys[None, :] == positions[:, None]
    slot_numbers = jnp.arange(living_brick_keys.shape[0], dtype=jnp.int32)
    slot_of = jnp.sum(jnp.where(matches, slot_numbers[None, :], 0), axis=1)
    present = jnp.any(matches, axis=1)
    return (slot_of, present)


def compact_to_tile(packed_arrangement, slot_of, present, rows_blocks, cols_blocks, block_edge):
    channels = packed_arrangement.shape[1]
    levels = packed_arrangement.shape[2] // (block_edge * block_edge)
    picked = jnp.take(packed_arrangement, slot_of, axis=0) * present[:, None, None].astype(
        packed_arrangement.dtype
    )
    shaped = picked.reshape(rows_blocks, cols_blocks, channels, levels, block_edge, block_edge)
    return shaped.transpose(2, 3, 0, 4, 1, 5).reshape(
        channels, levels, rows_blocks * block_edge, cols_blocks * block_edge
    )


def tile_to_compact(tile_data, living_brick_keys, rows_blocks, cols_blocks, block_edge):
    channels = tile_data.shape[0]
    levels = tile_data.shape[1]
    shaped = tile_data.reshape(
        channels, levels, rows_blocks, block_edge, cols_blocks, block_edge
    ).transpose(2, 4, 0, 1, 3, 5)
    blocks = shaped.reshape(rows_blocks * cols_blocks, channels, levels * block_edge * block_edge)
    occupied_seats = living_brick_keys >= 0
    picked = jnp.take(blocks, jnp.maximum(living_brick_keys, 0), axis=0)
    return picked * occupied_seats[:, None, None].astype(tile_data.dtype)


def on_device(
    scaled_distributions,
    remaining_brick_places,
    retained_wavenumbers,
    regional_amplitudes,
    relaxation_frequencies,
):
    forward, backward, speeds = lattice_tables()
    slot_state = scaled_distributions[0, 0]
    living_brick_keys = remaining_brick_places[0, 0]
    rows_tile = TY * BE
    cols_tile = TX * BE
    slot_of, present = slot_lookup(living_brick_keys, TX * TY)
    fluid_map = present.reshape(TY, TX).astype(jnp.float32)
    fluid_map = jnp.repeat(jnp.repeat(fluid_map, BE, axis=0), BE, axis=1)
    solid_tile = 1.0 - fluid_map
    pops_tile = compact_to_tile(slot_state, slot_of, present, TY, TX, BE)
    moments = jnp.einsum("ij,jlrc->ilrc", forward, pops_tile, precision=HIGHEST)
    safe_density = jnp.where(fluid_map[None] > 0.5, moments[0], 1.0)
    wind_tile = tile_velocity(moments, safe_density)
    line_length = lax.axis_size("line") * cols_tile
    own_columns = lax.axis_index("line") * cols_tile + jnp.arange(cols_tile, dtype=jnp.int32)
    mode_basis = mode_basis_at(retained_wavenumbers, own_columns, line_length)
    partial = jnp.einsum("klrx,xm->klrm", wind_tile, mode_basis, precision=HIGHEST)
    coefficients = butterfly_sum(partial, "line")
    misfit = regional_amplitudes - 2.0 / line_length * coefficients
    nudge_tile = NUDGE_GAIN * jnp.einsum(
        "klrm,xm->klrx", misfit, mode_basis, precision=HIGHEST
    )
    post_tile = collide_tile(moments, wind_tile, nudge_tile, backward, relaxation_frequencies)
    levels = post_tile.shape[1]
    solid_plane = jnp.broadcast_to(solid_tile[None, None], (1, levels, rows_tile, cols_tile))
    extended = jnp.concatenate([post_tile, solid_plane], axis=0)
    padded = with_halo(extended, (("curve", 2), ("line", 3)), 1)
    pops_pad = padded[:27]
    solid_pad = padded[27, 0]
    read = []
    for discrete_heading in range(27):
        carry_eastward = int(speeds[discrete_heading, 0])
        carry_northward = int(speeds[discrete_heading, 1])
        step_z = int(speeds[discrete_heading, 2])
        rows_slice = slice(1 - carry_northward, 1 - carry_northward + rows_tile)
        cols_slice = slice(1 - carry_eastward, 1 - carry_eastward + cols_tile)
        carried_sheet = pops_pad[discrete_heading, :, rows_slice, cols_slice]
        blocked = solid_pad[rows_slice, cols_slice] > 0.5
        bounced_distributions = post_tile[26 - discrete_heading]
        if step_z == 0:
            source = carried_sheet
            block_both = jnp.stack([blocked, blocked])
        elif step_z == 1:
            source = jnp.stack([carried_sheet[0], carried_sheet[0]])
            block_both = jnp.stack([jnp.ones_like(blocked), blocked])
        else:
            mirror_sheet = pops_pad[discrete_heading + 2, 1, rows_slice, cols_slice]
            source = jnp.stack([carried_sheet[1], mirror_sheet])
            block_both = jnp.stack([blocked, blocked])
        read.append(jnp.where(block_both, bounced_distributions, source))
    read_tile = jnp.stack(read, axis=0)
    new_state = tile_to_compact(read_tile, living_brick_keys, TY, TX, BE)
    return new_state[None, None]


def solution(mesh):
    return jax.shard_map(
        on_device,
        mesh=mesh,
        in_specs=(
            P("curve", "line", None, None, None),
            P("curve", "line", None),
            P(),
            P(None, None, "curve", None),
            P(),
        ),
        out_specs=P("curve", "line", None, None, None),
        check_vma=False,
    )
```

```python
import jax
import jax.numpy as jnp
import numpy as np
from jax import lax
from jax.experimental import pallas as pl
from jax.experimental.pallas import tpu as pltpu
from jax.sharding import PartitionSpec as P

BE = 16
TX = 4
TY = 2


NUDGE_GAIN = 0.5
TWO_PI = 6.283185307179586
HIGHEST = lax.Precision.HIGHEST


def butterfly_sum(value, axis):
    count = lax.axis_size(axis)
    stride = 1
    while stride < count:
        value = value + lax.ppermute(value, axis, [(i, i ^ stride) for i in range(count)])
        stride *= 2
    return value


def ring_pairs(axis):
    count = lax.axis_size(axis)
    forward = [(i, (i + 1) % count) for i in range(count)]
    backward = [(target, source) for source, target in forward]
    return forward, backward


def lattice_tables():
    one_weights = np.array([1.0 / 6.0, 2.0 / 3.0, 1.0 / 6.0])
    speeds = np.array(
        [
            [along_x - 1, along_y - 1, along_z - 1]
            for along_x in range(3)
            for along_y in range(3)
            for along_z in range(3)
        ]
    )
    weights = np.array(
        [
            one_weights[along_x] * one_weights[along_y] * one_weights[along_z]
            for along_x in range(3)
            for along_y in range(3)
            for along_z in range(3)
        ]
    )
    vander = np.array([[1.0, 1.0, 1.0], [-1.0, 0.0, 1.0], [1.0, 0.0, 1.0]])
    undo_vander = np.array([[0.0, -0.5, 0.5], [1.0, 0.0, -1.0], [0.0, 0.5, 0.5]])
    moment_matrix = np.kron(vander, np.kron(vander, vander))
    inverse = np.kron(undo_vander, np.kron(undo_vander, undo_vander))
    forward = jnp.asarray(moment_matrix * weights[None, :], dtype=jnp.float32)
    backward = jnp.asarray(inverse / weights[:, None], dtype=jnp.float32)
    return (forward, backward, speeds)


def mode_basis_at(mode_ids, positions, length):
    phase_ids = positions[:, None] * mode_ids[None, :] % length
    angles = phase_ids.astype(jnp.float32) * (TWO_PI / length)
    return jnp.concatenate([jnp.cos(angles), jnp.sin(angles)], axis=1)


def collide_tile(moments, velocity, nudge_tile, backward, relaxation_frequencies):
    density = moments[0]
    shifted = velocity + nudge_tile
    powers = jnp.stack([jnp.ones_like(shifted), shifted, shifted * shifted + 1.0 / 3.0], axis=0)
    equilibrium = (
        density[None, None, None]
        * powers[:, None, None, 0]
        * powers[None, :, None, 1]
        * powers[None, None, :, 2]
    )
    equilibrium = equilibrium.reshape(moments.shape)
    relaxed = moments - relaxation_frequencies[:, None, None] * (moments - equilibrium)
    return jnp.einsum("ij,jrl->irl", backward, relaxed, precision=HIGHEST)


def stream_kernel(pad_ref, side_ref, out_ref):
    rows = out_ref.shape[1]
    lanes = out_ref.shape[2]
    half = lanes // 2
    _, _, speeds = lattice_tables()
    lane = lax.broadcasted_iota(jnp.int32, (rows, lanes), 1)
    upper = lane >= half
    column = lane % half
    solid_channel = pad_ref.shape[0] - 1

    def joined(channel, cx, cy):
        window = slice(1 - cy, 1 - cy + rows)
        plane = pad_ref[channel, window, :]
        if cx == 1:
            low = side_ref[channel, window, 0:1]
            high = side_ref[channel, window, 1:2]
            plane = jnp.where(lane == lanes - 1, low, jnp.where(lane == half - 1, high, plane))
        elif cx == -1:
            low = side_ref[channel, window, 2:3]
            high = side_ref[channel, window, 3:4]
            plane = jnp.where(lane == half, low, jnp.where(lane == 0, high, plane))
        return plane

    def moved(plane, shift):
        shift = shift % lanes
        if shift == 0:
            return plane
        return pltpu.roll(plane, shift, 1)

    blocked_of = {}
    for cx in (-1, 0, 1):
        for cy in (-1, 0, 1):
            blocked_of[(cx, cy)] = moved(joined(solid_channel, cx, cy), cx) > 0.5
    for heading in range(27):
        cx, cy, cz = (int(v) for v in speeds[heading])
        blocked = blocked_of[(cx, cy)]
        bounced = pad_ref[26 - heading, 1:1 + rows, :]
        if cz == 0:
            source = moved(joined(heading, cx, cy), cx)
        elif cz == 1:
            source = moved(joined(heading, cx, cy), half + cx)
            blocked = jnp.logical_or(blocked, jnp.logical_not(upper))
        else:
            source = jnp.where(
                upper,
                moved(joined(heading + 2, cx, cy), cx),
                moved(joined(heading, cx, cy), half + cx),
            )
        out_ref[heading] = jnp.where(blocked, bounced, source)


def stream(padded, sides):
    channels = padded.shape[0] - 1
    rows = padded.shape[1] - 2
    lanes = padded.shape[2]
    return pl.pallas_call(
        stream_kernel,
        out_shape=jax.ShapeDtypeStruct((channels, rows, lanes), jnp.float32),
        in_specs=[
            pl.BlockSpec(memory_space=pltpu.VMEM),
            pl.BlockSpec(memory_space=pltpu.VMEM),
        ],
        out_specs=pl.BlockSpec(memory_space=pltpu.VMEM),
    )(padded, sides)


def on_device(
    scaled_distributions,
    remaining_brick_places,
    retained_wavenumbers,
    regional_amplitudes,
    relaxation_frequencies,
):
    forward, backward, speeds = lattice_tables()
    slot_state = scaled_distributions[0, 0]
    living_brick_keys = remaining_brick_places[0, 0]
    seats = living_brick_keys.shape[0]
    channels = slot_state.shape[1]
    levels = slot_state.shape[2] // (BE * BE)
    rows_tile = TY * BE
    cols_tile = TX * BE
    lanes = levels * cols_tile
    positions = jnp.arange(TX * TY, dtype=jnp.int32)
    matches = living_brick_keys[None, :] == positions[:, None]
    slot_of = jnp.sum(jnp.where(matches, jnp.arange(seats, dtype=jnp.int32)[None, :], 0), axis=1)
    present = jnp.any(matches, axis=1)
    picked = jnp.take(slot_state, slot_of, axis=0) * present[:, None, None].astype(jnp.float32)
    pops_tile = (
        picked.reshape(TY, TX, channels, levels, BE, BE)
        .transpose(2, 0, 4, 3, 1, 5)
        .reshape(channels, rows_tile, lanes)
    )
    fluid_blocks = present.reshape(TY, TX).astype(jnp.float32)
    fluid_map = jnp.broadcast_to(
        fluid_blocks[:, None, None, :, None], (TY, BE, levels, TX, BE)
    ).reshape(rows_tile, lanes)
    moments = jnp.einsum("ij,jrl->irl", forward, pops_tile, precision=HIGHEST)
    safe_density = jnp.where(fluid_map > 0.5, moments[0], 1.0)
    wind_tile = jnp.stack([moments[9], moments[3], moments[1]], axis=0) / safe_density[None]
    line_length = lax.axis_size("line") * cols_tile
    own_columns = lax.axis_index("line") * cols_tile + jnp.arange(cols_tile, dtype=jnp.int32)
    mode_basis = mode_basis_at(retained_wavenumbers, own_columns, line_length)
    partial = jnp.einsum(
        "krzx,xm->kzrm", wind_tile.reshape(3, rows_tile, levels, cols_tile), mode_basis,
        precision=HIGHEST,
    )
    coefficients = butterfly_sum(partial, "line")
    misfit = regional_amplitudes - 2.0 / line_length * coefficients
    nudge_tile = NUDGE_GAIN * jnp.einsum(
        "kzrm,xm->krzx", misfit, mode_basis, precision=HIGHEST
    ).reshape(3, rows_tile, lanes)
    post_tile = collide_tile(moments, wind_tile, nudge_tile, backward, relaxation_frequencies)
    extended = jnp.concatenate([post_tile, (1.0 - fluid_map)[None]], axis=0)
    ahead, behind = ring_pairs("curve")
    below = lax.ppermute(extended[:, rows_tile - 1:], "curve", ahead)
    above = lax.ppermute(extended[:, :1], "curve", behind)
    padded = jnp.concatenate([below, extended, above], axis=1)
    ahead, behind = ring_pairs("line")
    half = cols_tile
    to_right = jnp.stack([padded[:, :, half - 1], padded[:, :, lanes - 1]], axis=2)
    to_left = jnp.stack([padded[:, :, 0], padded[:, :, half]], axis=2)
    from_left = lax.ppermute(to_right, "line", ahead)
    from_right = lax.ppermute(to_left, "line", behind)
    sides = jnp.concatenate([from_left, from_right], axis=2)
    read_tile = stream(padded, sides)
    blocks = (
        read_tile.reshape(channels, TY, BE, levels, TX, BE)
        .transpose(1, 4, 0, 3, 2, 5)
        .reshape(TY * TX, channels, levels * BE * BE)
    )
    occupied = living_brick_keys >= 0
    new_state = jnp.take(blocks, jnp.maximum(living_brick_keys, 0), axis=0)
    new_state = new_state * occupied[:, None, None].astype(jnp.float32)
    return new_state[None, None]


def solution(mesh):
    return jax.shard_map(
        on_device,
        mesh=mesh,
        in_specs=(
            P("curve", "line", None, None, None),
            P("curve", "line", None),
            P(),
            P(None, None, "curve", None),
            P(),
        ),
        out_specs=P("curve", "line", None, None, None),
        check_vma=False,
    )
```

```python
import jax
import jax.numpy as jnp
import numpy as np
from jax import lax
from jax.experimental import pallas as pl
from jax.experimental.pallas import tpu as pltpu
from jax.sharding import PartitionSpec as P

BE = 16
TX = 4
TY = 2


NUDGE_GAIN = 0.5
TWO_PI = 6.283185307179586
HIGHEST = lax.Precision.HIGHEST


def butterfly_sum(value, axis):
    count = lax.axis_size(axis)
    stride = 1
    while stride < count:
        value = value + lax.ppermute(value, axis, [(i, i ^ stride) for i in range(count)])
        stride *= 2
    return value


def ring_pairs(axis):
    count = lax.axis_size(axis)
    forward = [(i, (i + 1) % count) for i in range(count)]
    backward = [(target, source) for source, target in forward]
    return forward, backward


def lattice_tables():
    one_weights = np.array([1.0 / 6.0, 2.0 / 3.0, 1.0 / 6.0])
    speeds = np.array(
        [
            [along_x - 1, along_y - 1, along_z - 1]
            for along_x in range(3)
            for along_y in range(3)
            for along_z in range(3)
        ]
    )
    weights = np.array(
        [
            one_weights[along_x] * one_weights[along_y] * one_weights[along_z]
            for along_x in range(3)
            for along_y in range(3)
            for along_z in range(3)
        ]
    )
    vander = np.array([[1.0, 1.0, 1.0], [-1.0, 0.0, 1.0], [1.0, 0.0, 1.0]])
    undo_vander = np.array([[0.0, -0.5, 0.5], [1.0, 0.0, -1.0], [0.0, 0.5, 0.5]])
    moment_matrix = np.kron(vander, np.kron(vander, vander))
    inverse = np.kron(undo_vander, np.kron(undo_vander, undo_vander))
    forward = jnp.asarray(moment_matrix * weights[None, :], dtype=jnp.float32)
    backward = jnp.asarray(inverse / weights[:, None], dtype=jnp.float32)
    return (forward, backward, speeds)


def mode_basis_at(mode_ids, positions, length):
    phase_ids = positions[:, None] * mode_ids[None, :] % length
    angles = phase_ids.astype(jnp.float32) * (TWO_PI / length)
    return jnp.concatenate([jnp.cos(angles), jnp.sin(angles)], axis=1)


def collide_blocks(moments, velocity, nudge, backward, relaxation_frequencies):
    density = moments[0]
    shifted = velocity + nudge
    powers = jnp.stack([jnp.ones_like(shifted), shifted, shifted * shifted + 1.0 / 3.0], axis=0)
    equilibrium = (
        density[None, None, None]
        * powers[:, None, None, 0]
        * powers[None, :, None, 1]
        * powers[None, None, :, 2]
    )
    equilibrium = equilibrium.reshape(moments.shape)
    relaxed = moments - relaxation_frequencies[:, None, None, None] * (moments - equilibrium)
    return jnp.einsum("ij,jzpl->izpl", backward, relaxed, precision=HIGHEST)


def stream_kernel(pad_ref, side_ref, out_ref):
    blocks = out_ref.shape[2]
    cells = out_ref.shape[3]
    _, _, speeds = lattice_tables()
    lane = lax.broadcasted_iota(jnp.int32, (blocks, cells), 1)
    seat = lax.broadcasted_iota(jnp.int32, (blocks, cells), 0)
    q = lane % BE
    r = lane // BE
    px = seat % TX
    py = seat // TX
    solid_channel = pad_ref.shape[0] - 1
    base = 2 * blocks // 2

    def moved(plane, shift):
        shift = shift % cells
        if shift == 0:
            return plane
        return pltpu.roll(plane, shift, 1)

    def gathered(channel, level, cx, cy):
        shift = cy * BE + cx

        def window(dy, dx):
            start = base - TX * dy - dx
            plane = pad_ref[channel, level, start:start + blocks, :]
            if dx != 0:
                edge = TX - 1 if dx == -1 else 0
                first = (1 - dy) if dx == 1 else (TY + 3 - dy)
                plane = jnp.where(
                    seat == edge,
                    side_ref[channel, level, first:first + 1, :],
                    jnp.where(
                        seat == edge + TX,
                        side_ref[channel, level, first + 1:first + 2, :],
                        plane,
                    ),
                )
            return plane

        value = moved(window(0, 0), shift)
        if cy != 0:
            ycross = r == (0 if cy == 1 else BE - 1)
            value = jnp.where(ycross, moved(window(cy, 0), shift), value)
        if cx != 0:
            xcross = q == (0 if cx == 1 else BE - 1)
            xvalue = moved(window(0, cx), shift - BE * cx)
            if cy != 0:
                xvalue = jnp.where(ycross, moved(window(cy, cx), shift - BE * cx), xvalue)
            value = jnp.where(xcross, xvalue, value)
        return value

    blocked_of = {}
    for cx in (-1, 0, 1):
        for cy in (-1, 0, 1):
            blocked_of[(cx, cy)] = gathered(solid_channel, 0, cx, cy) > 0.5
    for heading in range(27):
        cx, cy, cz = (int(v) for v in speeds[heading])
        blocked = blocked_of[(cx, cy)]
        for level in range(2):
            bounced = pad_ref[26 - heading, level, base:base + blocks, :]
            if cz == 1 and level == 0:
                out_ref[heading, level] = bounced
                continue
            if cz == 0:
                source = gathered(heading, level, cx, cy)
            elif cz == 1:
                source = gathered(heading, 0, cx, cy)
            elif level == 0:
                source = gathered(heading, 1, cx, cy)
            else:
                source = gathered(heading + 2, 1, cx, cy)
            out_ref[heading, level] = jnp.where(blocked, bounced, source)


def stream(padded, sides):
    channels = padded.shape[0] - 1
    levels = padded.shape[1]
    cells = padded.shape[3]
    return pl.pallas_call(
        stream_kernel,
        out_shape=jax.ShapeDtypeStruct((channels, levels, TX * TY, cells), jnp.float32),
        in_specs=[
            pl.BlockSpec(memory_space=pltpu.VMEM),
            pl.BlockSpec(memory_space=pltpu.VMEM),
        ],
        out_specs=pl.BlockSpec(memory_space=pltpu.VMEM),
    )(padded, sides)


def on_device(
    scaled_distributions,
    remaining_brick_places,
    retained_wavenumbers,
    regional_amplitudes,
    relaxation_frequencies,
):
    forward, backward, speeds = lattice_tables()
    slot_state = scaled_distributions[0, 0]
    living_brick_keys = remaining_brick_places[0, 0]
    seats = living_brick_keys.shape[0]
    channels = slot_state.shape[1]
    cells = BE * BE
    levels = slot_state.shape[2] // cells
    blocks = TX * TY
    rows_tile = TY * BE
    cols_tile = TX * BE
    positions = jnp.arange(blocks, dtype=jnp.int32)
    matches = living_brick_keys[None, :] == positions[:, None]
    slot_of = jnp.sum(jnp.where(matches, jnp.arange(seats, dtype=jnp.int32)[None, :], 0), axis=1)
    present = jnp.any(matches, axis=1)
    fluid = present.astype(jnp.float32)
    picked = jnp.take(slot_state.reshape(seats, channels, levels, cells), slot_of, axis=0)
    pops = picked.transpose(1, 2, 0, 3) * fluid[None, None, :, None]
    moments = jnp.einsum("ij,jzpl->izpl", forward, pops, precision=HIGHEST)
    safe_density = jnp.where(present[None, :, None], moments[0], 1.0)
    wind = jnp.stack([moments[9], moments[3], moments[1]], axis=0) / safe_density[None]
    line_length = lax.axis_size("line") * cols_tile
    own_columns = lax.axis_index("line") * cols_tile + jnp.arange(cols_tile, dtype=jnp.int32)
    mode_basis = mode_basis_at(retained_wavenumbers, own_columns, line_length).reshape(TX, BE, -1)
    partial = jnp.einsum(
        "kzyxrq,xqm->kzyrm", wind.reshape(3, levels, TY, TX, BE, BE), mode_basis,
        precision=HIGHEST,
    ).reshape(3, levels, rows_tile, -1)
    coefficients = butterfly_sum(partial, "line")
    misfit = regional_amplitudes - 2.0 / line_length * coefficients
    nudge = NUDGE_GAIN * jnp.einsum(
        "kzyrm,xqm->kzyxrq", misfit.reshape(3, levels, TY, BE, -1), mode_basis,
        precision=HIGHEST,
    ).reshape(3, levels, blocks, cells)
    post = collide_blocks(moments, wind, nudge, backward, relaxation_frequencies)
    solid = jnp.broadcast_to((1.0 - fluid)[None, None, :, None], (1, levels, blocks, cells))
    extended = jnp.concatenate([post, solid], axis=0)
    ahead, behind = ring_pairs("curve")
    top_row = extended[:, :, blocks - TX:, cells - BE:]
    bottom_row = extended[:, :, :TX, :BE]
    below = lax.ppermute(top_row, "curve", ahead)
    above = lax.ppermute(bottom_row, "curve", behind)
    width = channels + 1
    spread_below = jnp.pad(below, ((0, 0), (0, 0), (0, 0), (cells - BE, 0)))
    spread_above = jnp.pad(above, ((0, 0), (0, 0), (0, 0), (0, cells - BE)))
    filler = jnp.zeros((width, levels, TX, cells), jnp.float32)
    padded = jnp.concatenate([filler, spread_below, extended, spread_above, filler], axis=2)
    ahead, behind = ring_pairs("line")
    by_rows = extended.reshape(width, levels, TY, TX, BE, BE)
    right_cols = by_rows[:, :, :, TX - 1, :, BE - 1]
    left_cols = by_rows[:, :, :, 0, :, 0]
    to_right = jnp.concatenate(
        [
            jnp.broadcast_to(below[:, :, TX - 1:, BE - 1:], (width, levels, 1, BE)),
            right_cols,
            jnp.broadcast_to(above[:, :, TX - 1:, BE - 1:], (width, levels, 1, BE)),
        ],
        axis=2,
    )
    to_left = jnp.concatenate(
        [
            jnp.broadcast_to(below[:, :, :1, :1], (width, levels, 1, BE)),
            left_cols,
            jnp.broadcast_to(above[:, :, :1, :1], (width, levels, 1, BE)),
        ],
        axis=2,
    )
    from_left = lax.ppermute(to_right, "line", ahead)
    from_right = lax.ppermute(to_left, "line", behind)
    sides = jnp.concatenate(
        [
            jnp.pad(from_left[..., None], ((0, 0), (0, 0), (0, 0), (0, 0), (BE - 1, 0))),
            jnp.pad(from_right[..., None], ((0, 0), (0, 0), (0, 0), (0, 0), (0, BE - 1))),
        ],
        axis=2,
    ).reshape(width, levels, 2 * (TY + 2), cells)
    result = stream(padded, sides)
    by_block = result.transpose(2, 0, 1, 3).reshape(blocks, channels, levels * cells)
    occupied = living_brick_keys >= 0
    new_state = jnp.take(by_block, jnp.maximum(living_brick_keys, 0), axis=0)
    new_state = new_state * occupied[:, None, None].astype(jnp.float32)
    return new_state[None, None]


def solution(mesh):
    return jax.shard_map(
        on_device,
        mesh=mesh,
        in_specs=(
            P("curve", "line", None, None, None),
            P("curve", "line", None),
            P(),
            P(None, None, "curve", None),
            P(),
        ),
        out_specs=P("curve", "line", None, None, None),
        check_vma=False,
    )
```

```python
import jax
import jax.numpy as jnp
import numpy as np
from jax import lax
from jax.experimental import pallas as pl
from jax.experimental.pallas import tpu as pltpu
from jax.sharding import PartitionSpec as P

BE = 16
TX = 4
TY = 2


NUDGE_GAIN = 0.5
TWO_PI = 6.283185307179586
HIGHEST = lax.Precision.HIGHEST


def butterfly_sum(value, axis):
    count = lax.axis_size(axis)
    stride = 1
    while stride < count:
        value = value + lax.ppermute(value, axis, [(i, i ^ stride) for i in range(count)])
        stride *= 2
    return value


def ring_pairs(axis):
    count = lax.axis_size(axis)
    forward = [(i, (i + 1) % count) for i in range(count)]
    backward = [(target, source) for source, target in forward]
    return forward, backward


def lattice_tables():
    one_weights = np.array([1.0 / 6.0, 2.0 / 3.0, 1.0 / 6.0])
    speeds = np.array(
        [
            [along_x - 1, along_y - 1, along_z - 1]
            for along_x in range(3)
            for along_y in range(3)
            for along_z in range(3)
        ]
    )
    weights = np.array(
        [
            one_weights[along_x] * one_weights[along_y] * one_weights[along_z]
            for along_x in range(3)
            for along_y in range(3)
            for along_z in range(3)
        ]
    )
    vander = np.array([[1.0, 1.0, 1.0], [-1.0, 0.0, 1.0], [1.0, 0.0, 1.0]])
    undo_vander = np.array([[0.0, -0.5, 0.5], [1.0, 0.0, -1.0], [0.0, 0.5, 0.5]])
    moment_matrix = np.kron(vander, np.kron(vander, vander))
    inverse = np.kron(undo_vander, np.kron(undo_vander, undo_vander))
    forward = jnp.asarray(moment_matrix * weights[None, :], dtype=jnp.float32)
    backward = jnp.asarray(inverse / weights[:, None], dtype=jnp.float32)
    return (forward, backward, speeds)


def mode_basis_at(mode_ids, positions, length):
    phase_ids = positions[:, None] * mode_ids[None, :] % length
    angles = phase_ids.astype(jnp.float32) * (TWO_PI / length)
    return jnp.concatenate([jnp.cos(angles), jnp.sin(angles)], axis=1)


def velocity_of(moments, solid):
    safe_density = jnp.where(solid > 0.5, 1.0, moments[0])
    return jnp.stack([moments[9], moments[3], moments[1]], axis=0) / safe_density[None]


def collide_cells(moments, velocity, nudge, backward, relaxation_frequencies):
    density = moments[0]
    shifted = velocity + nudge
    powers = jnp.stack([jnp.ones_like(shifted), shifted, shifted * shifted + 1.0 / 3.0], axis=0)
    equilibrium = (
        density[None, None, None]
        * powers[:, None, None, 0]
        * powers[None, :, None, 1]
        * powers[None, None, :, 2]
    )
    equilibrium = equilibrium.reshape(moments.shape)
    rates = relaxation_frequencies.reshape((-1,) + (1,) * (moments.ndim - 1))
    relaxed = moments - rates * (moments - equilibrium)
    return jnp.einsum("ij,j...->i...", backward, relaxed, precision=HIGHEST)


def stream_kernel(pad_ref, side_ref, out_ref):
    blocks = out_ref.shape[2]
    cells = out_ref.shape[3]
    _, _, speeds = lattice_tables()
    lane = lax.broadcasted_iota(jnp.int32, (blocks, cells), 1)
    seat = lax.broadcasted_iota(jnp.int32, (blocks, cells), 0)
    q = lane % BE
    r = lane // BE
    px = seat % TX
    py = seat // TX
    solid_channel = pad_ref.shape[0] - 1
    base = 2 * blocks // 2

    def moved(plane, shift):
        shift = shift % cells
        if shift == 0:
            return plane
        return pltpu.roll(plane, shift, 1)

    def gathered(channel, level, cx, cy):
        shift = cy * BE + cx

        def window(dy, dx):
            start = base - TX * dy - dx
            plane = pad_ref[channel, level, start:start + blocks, :]
            if dx != 0:
                edge = TX - 1 if dx == -1 else 0
                first = (1 - dy) if dx == 1 else (TY + 3 - dy)
                plane = jnp.where(
                    seat == edge,
                    side_ref[channel, level, first:first + 1, :],
                    jnp.where(
                        seat == edge + TX,
                        side_ref[channel, level, first + 1:first + 2, :],
                        plane,
                    ),
                )
            return plane

        value = moved(window(0, 0), shift)
        if cy != 0:
            ycross = r == (0 if cy == 1 else BE - 1)
            value = jnp.where(ycross, moved(window(cy, 0), shift), value)
        if cx != 0:
            xcross = q == (0 if cx == 1 else BE - 1)
            xvalue = moved(window(0, cx), shift - BE * cx)
            if cy != 0:
                xvalue = jnp.where(ycross, moved(window(cy, cx), shift - BE * cx), xvalue)
            value = jnp.where(xcross, xvalue, value)
        return value

    blocked_of = {}
    for cx in (-1, 0, 1):
        for cy in (-1, 0, 1):
            blocked_of[(cx, cy)] = gathered(solid_channel, 0, cx, cy) > 0.5
    for heading in range(27):
        cx, cy, cz = (int(v) for v in speeds[heading])
        blocked = blocked_of[(cx, cy)]
        for level in range(2):
            bounced = pad_ref[26 - heading, level, base:base + blocks, :]
            if cz == 1 and level == 0:
                out_ref[heading, level] = bounced
                continue
            if cz == 0:
                source = gathered(heading, level, cx, cy)
            elif cz == 1:
                source = gathered(heading, 0, cx, cy)
            elif level == 0:
                source = gathered(heading, 1, cx, cy)
            else:
                source = gathered(heading + 2, 1, cx, cy)
            out_ref[heading, level] = jnp.where(blocked, bounced, source)


def stream(padded, sides):
    channels = padded.shape[0] - 1
    levels = padded.shape[1]
    cells = padded.shape[3]
    return pl.pallas_call(
        stream_kernel,
        out_shape=jax.ShapeDtypeStruct((channels, levels, TX * TY, cells), jnp.float32),
        in_specs=[
            pl.BlockSpec(memory_space=pltpu.VMEM),
            pl.BlockSpec(memory_space=pltpu.VMEM),
        ],
        out_specs=pl.BlockSpec(memory_space=pltpu.VMEM),
    )(padded, sides)


def on_device(
    scaled_distributions,
    remaining_brick_places,
    retained_wavenumbers,
    regional_amplitudes,
    relaxation_frequencies,
):
    forward, backward, speeds = lattice_tables()
    slot_state = scaled_distributions[0, 0]
    living_brick_keys = remaining_brick_places[0, 0]
    seats = living_brick_keys.shape[0]
    channels = slot_state.shape[1]
    cells = BE * BE
    levels = slot_state.shape[2] // cells
    blocks = TX * TY
    rows_tile = TY * BE
    cols_tile = TX * BE
    positions = jnp.arange(blocks, dtype=jnp.int32)
    matches = living_brick_keys[None, :] == positions[:, None]
    slot_of = jnp.sum(jnp.where(matches, jnp.arange(seats, dtype=jnp.int32)[None, :], 0), axis=1)
    present = jnp.any(matches, axis=1)
    fluid = present.astype(jnp.float32)
    picked = jnp.take(slot_state.reshape(seats, channels, levels, cells), slot_of, axis=0)
    pops = picked.transpose(1, 2, 0, 3) * fluid[None, None, :, None]
    solid = jnp.broadcast_to((1.0 - fluid)[None, None, :, None], (1, levels, blocks, cells))
    extended = jnp.concatenate([pops, solid], axis=0)
    width = channels + 1
    modes = regional_amplitudes.shape[3]

    ahead, behind = ring_pairs("curve")
    top_row = extended[:, :, blocks - TX:, cells - BE:]
    bottom_row = extended[:, :, :TX, :BE]
    row_size = top_row.size

    def packed(row, amplitude_row):
        return jnp.concatenate([row.reshape(-1), amplitude_row.reshape(-1)])

    below_message = lax.ppermute(packed(top_row, regional_amplitudes[:, :, rows_tile - 1:]), "curve", ahead)
    above_message = lax.ppermute(packed(bottom_row, regional_amplitudes[:, :, :1]), "curve", behind)
    below_pre = below_message[:row_size].reshape(top_row.shape)
    above_pre = above_message[:row_size].reshape(top_row.shape)
    amplitude_below = below_message[row_size:].reshape(3, levels, 1, modes)
    amplitude_above = above_message[row_size:].reshape(3, levels, 1, modes)

    ahead, behind = ring_pairs("line")
    by_rows = extended.reshape(width, levels, TY, TX, BE, BE)
    to_right = jnp.concatenate(
        [
            jnp.broadcast_to(below_pre[:, :, TX - 1:, BE - 1:], (width, levels, 1, BE)),
            by_rows[:, :, :, TX - 1, :, BE - 1],
            jnp.broadcast_to(above_pre[:, :, TX - 1:, BE - 1:], (width, levels, 1, BE)),
        ],
        axis=2,
    )
    to_left = jnp.concatenate(
        [
            jnp.broadcast_to(below_pre[:, :, :1, :1], (width, levels, 1, BE)),
            by_rows[:, :, :, 0, :, 0],
            jnp.broadcast_to(above_pre[:, :, :1, :1], (width, levels, 1, BE)),
        ],
        axis=2,
    )
    left_pre = lax.ppermute(to_right, "line", ahead)
    right_pre = lax.ppermute(to_left, "line", behind)

    line_length = lax.axis_size("line") * cols_tile
    first_column = lax.axis_index("line") * cols_tile
    own_columns = first_column + jnp.arange(cols_tile, dtype=jnp.int32)
    mode_basis = mode_basis_at(retained_wavenumbers, own_columns, line_length).reshape(TX, BE, -1)
    edge_columns = jnp.stack([first_column - 1, first_column + cols_tile]) % line_length
    edge_basis = mode_basis_at(retained_wavenumbers, edge_columns, line_length)

    moments = jnp.einsum("ij,jzpl->izpl", forward, pops, precision=HIGHEST)
    wind = velocity_of(moments, solid[0])
    partial = jnp.einsum(
        "kzyxrq,xqm->kzyrm", wind.reshape(3, levels, TY, TX, BE, BE), mode_basis,
        precision=HIGHEST,
    ).reshape(3, levels, rows_tile, -1)
    halo_rows = jnp.stack([below_pre, above_pre], axis=2)
    halo_row_moments = jnp.einsum("ij,jzhxq->izhxq", forward, halo_rows[:channels], precision=HIGHEST)
    halo_row_wind = velocity_of(halo_row_moments, halo_rows[channels])
    halo_partial = jnp.einsum("kzhxq,xqm->kzhm", halo_row_wind, mode_basis, precision=HIGHEST)
    partial_rows = jnp.concatenate([halo_partial[:, :, :1], partial, halo_partial[:, :, 1:]], axis=2)
    coefficients = butterfly_sum(partial_rows, "line")
    amplitudes = jnp.concatenate([amplitude_below, regional_amplitudes, amplitude_above], axis=2)
    misfit = amplitudes - 2.0 / line_length * coefficients

    nudge = NUDGE_GAIN * jnp.einsum(
        "kzyrm,xqm->kzyxrq", misfit[:, :, 1:rows_tile + 1].reshape(3, levels, TY, BE, -1), mode_basis,
        precision=HIGHEST,
    ).reshape(3, levels, blocks, cells)
    post = collide_cells(moments, wind, nudge, backward, relaxation_frequencies)
    extended = jnp.concatenate([post, solid], axis=0)

    halo_row_misfit = jnp.stack([misfit[:, :, 0], misfit[:, :, rows_tile + 1]], axis=2)
    halo_row_nudge = NUDGE_GAIN * jnp.einsum(
        "kzhm,xqm->kzhxq", halo_row_misfit, mode_basis, precision=HIGHEST
    )
    halo_row_post = collide_cells(
        halo_row_moments, halo_row_wind, halo_row_nudge, backward, relaxation_frequencies
    )
    below = jnp.concatenate([halo_row_post[:, :, 0], below_pre[channels:]], axis=0)
    above = jnp.concatenate([halo_row_post[:, :, 1], above_pre[channels:]], axis=0)

    column_misfit = jnp.concatenate(
        [
            jnp.broadcast_to(misfit[:, :, :1, None], (3, levels, 1, BE, modes)),
            misfit[:, :, 1:rows_tile + 1].reshape(3, levels, TY, BE, modes),
            jnp.broadcast_to(misfit[:, :, rows_tile + 1:, None], (3, levels, 1, BE, modes)),
        ],
        axis=2,
    )
    columns_pre = jnp.stack([left_pre, right_pre], axis=2)
    column_moments = jnp.einsum("ij,jzsyr->izsyr", forward, columns_pre[:channels], precision=HIGHEST)
    column_wind = velocity_of(column_moments, columns_pre[channels])
    column_nudge = NUDGE_GAIN * jnp.einsum(
        "kzyrm,sm->kzsyr", column_misfit, edge_basis, precision=HIGHEST
    )
    column_post = collide_cells(
        column_moments, column_wind, column_nudge, backward, relaxation_frequencies
    )
    from_left = jnp.concatenate([column_post[:, :, 0], left_pre[channels:]], axis=0)
    from_right = jnp.concatenate([column_post[:, :, 1], right_pre[channels:]], axis=0)
    spread_below = jnp.pad(below, ((0, 0), (0, 0), (0, 0), (cells - BE, 0)))
    spread_above = jnp.pad(above, ((0, 0), (0, 0), (0, 0), (0, cells - BE)))
    filler = jnp.zeros((width, levels, TX, cells), jnp.float32)
    padded = jnp.concatenate([filler, spread_below, extended, spread_above, filler], axis=2)
    sides = jnp.concatenate(
        [
            jnp.pad(from_left[..., None], ((0, 0), (0, 0), (0, 0), (0, 0), (BE - 1, 0))),
            jnp.pad(from_right[..., None], ((0, 0), (0, 0), (0, 0), (0, 0), (0, BE - 1))),
        ],
        axis=2,
    ).reshape(width, levels, 2 * (TY + 2), cells)
    result = stream(padded, sides)
    by_block = result.transpose(2, 0, 1, 3).reshape(blocks, channels, levels * cells)
    occupied = living_brick_keys >= 0
    new_state = jnp.take(by_block, jnp.maximum(living_brick_keys, 0), axis=0)
    new_state = new_state * occupied[:, None, None].astype(jnp.float32)
    return new_state[None, None]


def solution(mesh):
    return jax.shard_map(
        on_device,
        mesh=mesh,
        in_specs=(
            P("curve", "line", None, None, None),
            P("curve", "line", None),
            P(),
            P(None, None, "curve", None),
            P(),
        ),
        out_specs=P("curve", "line", None, None, None),
        check_vma=False,
    )
```

```python
import jax
import jax.numpy as jnp
import numpy as np
from jax import lax
from jax.experimental import pallas as pl
from jax.experimental.pallas import tpu as pltpu
from jax.sharding import PartitionSpec as P

BE = 16
TX = 4
TY = 2


NUDGE_GAIN = 0.5
TWO_PI = 6.283185307179586
HIGHEST = lax.Precision.HIGHEST


def butterfly_sum(value, axis):
    count = lax.axis_size(axis)
    stride = 1
    while stride < count:
        value = value + lax.ppermute(value, axis, [(i, i ^ stride) for i in range(count)])
        stride *= 2
    return value


def ring_pairs(axis):
    count = lax.axis_size(axis)
    forward = [(i, (i + 1) % count) for i in range(count)]
    backward = [(target, source) for source, target in forward]
    return forward, backward


def lattice_tables():
    one_weights = np.array([1.0 / 6.0, 2.0 / 3.0, 1.0 / 6.0])
    speeds = np.array(
        [
            [along_x - 1, along_y - 1, along_z - 1]
            for along_x in range(3)
            for along_y in range(3)
            for along_z in range(3)
        ]
    )
    weights = np.array(
        [
            one_weights[along_x] * one_weights[along_y] * one_weights[along_z]
            for along_x in range(3)
            for along_y in range(3)
            for along_z in range(3)
        ]
    )
    vander = np.array([[1.0, 1.0, 1.0], [-1.0, 0.0, 1.0], [1.0, 0.0, 1.0]])
    undo_vander = np.array([[0.0, -0.5, 0.5], [1.0, 0.0, -1.0], [0.0, 0.5, 0.5]])
    moment_matrix = np.kron(vander, np.kron(vander, vander))
    inverse = np.kron(undo_vander, np.kron(undo_vander, undo_vander))
    forward = jnp.asarray(moment_matrix * weights[None, :], dtype=jnp.float32)
    backward = jnp.asarray(inverse / weights[:, None], dtype=jnp.float32)
    return (forward, backward, speeds)


def mode_basis_at(mode_ids, positions, length):
    phase_ids = positions[:, None] * mode_ids[None, :] % length
    angles = phase_ids.astype(jnp.float32) * (TWO_PI / length)
    return jnp.concatenate([jnp.cos(angles), jnp.sin(angles)], axis=1)


def collide_blocks(moments, velocity, nudge, backward, relaxation_frequencies):
    density = moments[0]
    shifted = velocity + nudge
    powers = jnp.stack([jnp.ones_like(shifted), shifted, shifted * shifted + 1.0 / 3.0], axis=0)
    equilibrium = (
        density[None, None, None]
        * powers[:, None, None, 0]
        * powers[None, :, None, 1]
        * powers[None, None, :, 2]
    )
    equilibrium = equilibrium.reshape(moments.shape)
    relaxed = moments - relaxation_frequencies[:, None, None, None] * (moments - equilibrium)
    return jnp.einsum("ij,jzpl->izpl", backward, relaxed, precision=HIGHEST)


def stream_kernel(post_ref, solid_ref, below_ref, above_ref, left_ref, right_ref, out_ref, spread_ref):
    channels = out_ref.shape[0]
    blocks = out_ref.shape[2]
    cells = out_ref.shape[3]
    levels = out_ref.shape[1]
    _, _, speeds = lattice_tables()
    front = 8
    grid_row = lax.broadcasted_iota(jnp.int32, (BE, cells), 0)
    grid_lane = lax.broadcasted_iota(jnp.int32, (BE, cells), 1)
    tile_copy = (grid_lane % BE == grid_row).astype(jnp.float32)
    group_copy = (grid_lane // BE == grid_row).astype(jnp.float32)
    halo_rows = below_ref.shape[0]
    for slot, (source, copier) in enumerate(
        ((below_ref, tile_copy), (above_ref, tile_copy), (left_ref, group_copy), (right_ref, group_copy))
    ):
        spread_ref[slot, front:front + halo_rows, :] = jnp.dot(
            source[...], copier, precision=HIGHEST, preferred_element_type=jnp.float32
        )
    lane = lax.broadcasted_iota(jnp.int32, (blocks, cells), 1)
    seat = lax.broadcasted_iota(jnp.int32, (blocks, cells), 0)
    q = lane % BE
    r = lane // BE
    py = seat // TX

    def own(channel, level):
        if channel == channels:
            return solid_ref[...]
        return post_ref[channel, level]

    def moved(plane, shift):
        shift = shift % cells
        if shift == 0:
            return plane
        return pltpu.roll(plane, shift, 1)

    def gathered(channel, level, cx, cy):
        shift = cy * BE + cx
        first = front + (channel * levels + level) * (TY + 2)
        base = own(channel, level)
        if cy != 0:
            stepped = pltpu.roll(base, TX, 0)
            if cy == 1:
                halo = spread_ref[0, first:first + blocks, :]
                yplane = jnp.where(py == 0, halo, stepped)
            else:
                halo = spread_ref[1, first - TX:first - TX + blocks, :]
                yplane = jnp.where(py == TY - 1, halo, stepped)

        def sideways(plane, dy, dx):
            plane = pltpu.roll(plane, dx % blocks, 0)
            edge = 0 if dx == 1 else TX - 1
            side = 2 if dx == 1 else 3
            at = first + 1 - dy
            return jnp.where(
                seat == edge,
                spread_ref[side, at:at + 1, :],
                jnp.where(seat == edge + TX, spread_ref[side, at + 1:at + 2, :], plane),
            )

        value = moved(base, shift)
        if cy != 0:
            ycross = r == (0 if cy == 1 else BE - 1)
            value = jnp.where(ycross, moved(yplane, shift), value)
        if cx != 0:
            xcross = q == (0 if cx == 1 else BE - 1)
            xvalue = moved(sideways(base, 0, cx), shift - BE * cx)
            if cy != 0:
                xvalue = jnp.where(ycross, moved(sideways(yplane, cy, cx), shift - BE * cx), xvalue)
            value = jnp.where(xcross, xvalue, value)
        return value

    blocked_of = {}
    for cx in (-1, 0, 1):
        for cy in (-1, 0, 1):
            blocked_of[(cx, cy)] = gathered(channels, 0, cx, cy) > 0.5
    for heading in range(27):
        cx, cy, cz = (int(v) for v in speeds[heading])
        blocked = blocked_of[(cx, cy)]
        for level in range(levels):
            bounced = post_ref[26 - heading, level]
            if cz == 1 and level == 0:
                out_ref[heading, level] = bounced
                continue
            if cz == 0:
                source = gathered(heading, level, cx, cy)
            elif cz == 1:
                source = gathered(heading, 0, cx, cy)
            elif level == 0:
                source = gathered(heading, 1, cx, cy)
            else:
                source = gathered(heading + 2, 1, cx, cy)
            out_ref[heading, level] = jnp.where(blocked, bounced, source)


def stream(post, solid_plane, below, above, from_left, from_right):
    channels, levels, blocks, cells = post.shape
    halo_rows = below.shape[0]
    vmem = pl.BlockSpec(memory_space=pltpu.VMEM)
    return pl.pallas_call(
        stream_kernel,
        out_shape=jax.ShapeDtypeStruct((channels, levels, blocks, cells), jnp.float32),
        in_specs=[vmem] * 6,
        out_specs=vmem,
        scratch_shapes=[pltpu.VMEM((4, halo_rows + 16, cells), jnp.float32)],
    )(post, solid_plane, below, above, from_left, from_right)


def on_device(
    scaled_distributions,
    remaining_brick_places,
    retained_wavenumbers,
    regional_amplitudes,
    relaxation_frequencies,
):
    forward, backward, speeds = lattice_tables()
    slot_state = scaled_distributions[0, 0]
    living_brick_keys = remaining_brick_places[0, 0]
    seats = living_brick_keys.shape[0]
    channels = slot_state.shape[1]
    cells = BE * BE
    levels = slot_state.shape[2] // cells
    blocks = TX * TY
    rows_tile = TY * BE
    cols_tile = TX * BE
    positions = jnp.arange(blocks, dtype=jnp.int32)
    matches = living_brick_keys[None, :] == positions[:, None]
    slot_of = jnp.sum(jnp.where(matches, jnp.arange(seats, dtype=jnp.int32)[None, :], 0), axis=1)
    present = jnp.any(matches, axis=1)
    fluid = present.astype(jnp.float32)
    picked = jnp.take(slot_state.reshape(seats, channels, levels, cells), slot_of, axis=0)
    pops = picked.transpose(1, 2, 0, 3) * fluid[None, None, :, None]
    moments = jnp.einsum("ij,jzpl->izpl", forward, pops, precision=HIGHEST)
    safe_density = jnp.where(present[None, :, None], moments[0], 1.0)
    wind = jnp.stack([moments[9], moments[3], moments[1]], axis=0) / safe_density[None]
    line_length = lax.axis_size("line") * cols_tile
    own_columns = lax.axis_index("line") * cols_tile + jnp.arange(cols_tile, dtype=jnp.int32)
    mode_basis = mode_basis_at(retained_wavenumbers, own_columns, line_length).reshape(TX, BE, -1)
    partial = jnp.einsum(
        "kzyxrq,xqm->kzyrm", wind.reshape(3, levels, TY, TX, BE, BE), mode_basis,
        precision=HIGHEST,
    ).reshape(3, levels, rows_tile, -1)
    coefficients = butterfly_sum(partial, "line")
    misfit = regional_amplitudes - 2.0 / line_length * coefficients
    nudge = NUDGE_GAIN * jnp.einsum(
        "kzyrm,xqm->kzyxrq", misfit.reshape(3, levels, TY, BE, -1), mode_basis,
        precision=HIGHEST,
    ).reshape(3, levels, blocks, cells)
    post = collide_blocks(moments, wind, nudge, backward, relaxation_frequencies)
    solid = jnp.broadcast_to((1.0 - fluid)[None, None, :, None], (1, levels, blocks, cells))
    extended = jnp.concatenate([post, solid], axis=0)
    width = channels + 1
    ahead, behind = ring_pairs("curve")
    top_row = extended[:, :, blocks - TX:, cells - BE:]
    bottom_row = extended[:, :, :TX, :BE]
    below = lax.ppermute(top_row, "curve", ahead)
    above = lax.ppermute(bottom_row, "curve", behind)
    ahead, behind = ring_pairs("line")
    by_rows = extended.reshape(width, levels, TY, TX, BE, BE)
    right_cols = by_rows[:, :, :, TX - 1, :, BE - 1]
    left_cols = by_rows[:, :, :, 0, :, 0]
    to_right = jnp.concatenate(
        [
            jnp.broadcast_to(below[:, :, TX - 1:, BE - 1:], (width, levels, 1, BE)),
            right_cols,
            jnp.broadcast_to(above[:, :, TX - 1:, BE - 1:], (width, levels, 1, BE)),
        ],
        axis=2,
    )
    to_left = jnp.concatenate(
        [
            jnp.broadcast_to(below[:, :, :1, :1], (width, levels, 1, BE)),
            left_cols,
            jnp.broadcast_to(above[:, :, :1, :1], (width, levels, 1, BE)),
        ],
        axis=2,
    )
    from_left = lax.ppermute(to_right, "line", ahead)
    from_right = lax.ppermute(to_left, "line", behind)
    flat = lambda halo: halo.reshape(-1, BE)
    solid_plane = jnp.broadcast_to((1.0 - fluid)[:, None], (blocks, cells))
    result = stream(post, solid_plane, flat(below), flat(above), flat(from_left), flat(from_right))
    by_block = result.transpose(2, 0, 1, 3).reshape(blocks, channels, levels * cells)
    occupied = living_brick_keys >= 0
    new_state = jnp.take(by_block, jnp.maximum(living_brick_keys, 0), axis=0)
    new_state = new_state * occupied[:, None, None].astype(jnp.float32)
    return new_state[None, None]


def solution(mesh):
    return jax.shard_map(
        on_device,
        mesh=mesh,
        in_specs=(
            P("curve", "line", None, None, None),
            P("curve", "line", None),
            P(),
            P(None, None, "curve", None),
            P(),
        ),
        out_specs=P("curve", "line", None, None, None),
        check_vma=False,
    )
```

```python
import jax
import jax.numpy as jnp
import numpy as np
from jax import lax
from jax.experimental import pallas as pl
from jax.experimental.pallas import tpu as pltpu
from jax.sharding import PartitionSpec as P

BE = 16
TX = 4
TY = 2


NUDGE_GAIN = 0.5
TWO_PI = 6.283185307179586
HIGHEST = lax.Precision.HIGHEST


def butterfly_sum(value, axis):
    count = lax.axis_size(axis)
    stride = 1
    while stride < count:
        value = value + lax.ppermute(value, axis, [(i, i ^ stride) for i in range(count)])
        stride *= 2
    return value


def ring_pairs(axis):
    count = lax.axis_size(axis)
    forward = [(i, (i + 1) % count) for i in range(count)]
    backward = [(target, source) for source, target in forward]
    return forward, backward


def lattice_tables():
    one_weights = np.array([1.0 / 6.0, 2.0 / 3.0, 1.0 / 6.0])
    speeds = np.array(
        [
            [along_x - 1, along_y - 1, along_z - 1]
            for along_x in range(3)
            for along_y in range(3)
            for along_z in range(3)
        ]
    )
    weights = np.array(
        [
            one_weights[along_x] * one_weights[along_y] * one_weights[along_z]
            for along_x in range(3)
            for along_y in range(3)
            for along_z in range(3)
        ]
    )
    vander = np.array([[1.0, 1.0, 1.0], [-1.0, 0.0, 1.0], [1.0, 0.0, 1.0]])
    undo_vander = np.array([[0.0, -0.5, 0.5], [1.0, 0.0, -1.0], [0.0, 0.5, 0.5]])
    moment_matrix = np.kron(vander, np.kron(vander, vander))
    inverse = np.kron(undo_vander, np.kron(undo_vander, undo_vander))
    forward = jnp.asarray(moment_matrix * weights[None, :], dtype=jnp.float32)
    backward = jnp.asarray(inverse / weights[:, None], dtype=jnp.float32)
    return (forward, backward, speeds)


def mode_basis_at(mode_ids, positions, length):
    phase_ids = positions[:, None] * mode_ids[None, :] % length
    angles = phase_ids.astype(jnp.float32) * (TWO_PI / length)
    return jnp.concatenate([jnp.cos(angles), jnp.sin(angles)], axis=1)


def collide_blocks(moments, velocity, nudge, backward, relaxation_frequencies):
    density = moments[0]
    shifted = velocity + nudge
    powers = jnp.stack([jnp.ones_like(shifted), shifted, shifted * shifted + 1.0 / 3.0], axis=0)
    equilibrium = (
        density[None, None, None]
        * powers[:, None, None, 0]
        * powers[None, :, None, 1]
        * powers[None, None, :, 2]
    )
    equilibrium = equilibrium.reshape(moments.shape)
    relaxed = moments - relaxation_frequencies[:, None, None, None] * (moments - equilibrium)
    return jnp.einsum("ij,jzpl->izpl", backward, relaxed, precision=HIGHEST)


def stream_kernel(fluid_ref, post_ref, below_ref, above_ref, left_ref, right_ref, out_ref, spread_ref):
    channels = out_ref.shape[0]
    blocks = out_ref.shape[2]
    cells = out_ref.shape[3]
    levels = out_ref.shape[1]
    _, _, speeds = lattice_tables()
    front = 8
    grid_row = lax.broadcasted_iota(jnp.int32, (BE, cells), 0)
    grid_lane = lax.broadcasted_iota(jnp.int32, (BE, cells), 1)
    tile_copy = (grid_lane % BE == grid_row).astype(jnp.float32)
    group_copy = (grid_lane // BE == grid_row).astype(jnp.float32)
    halo_rows = below_ref.shape[0]
    for slot, (source, copier) in enumerate(
        ((below_ref, tile_copy), (above_ref, tile_copy), (left_ref, group_copy), (right_ref, group_copy))
    ):
        spread_ref[slot, front:front + halo_rows, :] = jnp.dot(
            source[...], copier, precision=HIGHEST, preferred_element_type=jnp.float32
        )
    lane = lax.broadcasted_iota(jnp.int32, (blocks, cells), 1)
    seat = lax.broadcasted_iota(jnp.int32, (blocks, cells), 0)
    q = lane % BE
    r = lane // BE
    py = seat // TX

    solid_plane = jnp.zeros((blocks, cells), jnp.float32)
    for block in range(blocks):
        solid_plane = jnp.where(seat == block, 1.0 - fluid_ref[block], solid_plane)

    def own(channel, level):
        if channel == channels:
            return solid_plane
        return post_ref[channel, level]

    def moved(plane, shift):
        shift = shift % cells
        if shift == 0:
            return plane
        return pltpu.roll(plane, shift, 1)

    def gathered(channel, level, cx, cy):
        shift = cy * BE + cx
        first = front + (channel * levels + level) * (TY + 2)
        base = own(channel, level)
        if cy != 0:
            stepped = pltpu.roll(base, TX, 0)
            if cy == 1:
                halo = spread_ref[0, first:first + blocks, :]
                yplane = jnp.where(py == 0, halo, stepped)
            else:
                halo = spread_ref[1, first - TX:first - TX + blocks, :]
                yplane = jnp.where(py == TY - 1, halo, stepped)

        def sideways(plane, dy, dx):
            plane = pltpu.roll(plane, dx % blocks, 0)
            edge = 0 if dx == 1 else TX - 1
            side = 2 if dx == 1 else 3
            at = first + 1 - dy
            return jnp.where(
                seat == edge,
                spread_ref[side, at:at + 1, :],
                jnp.where(seat == edge + TX, spread_ref[side, at + 1:at + 2, :], plane),
            )

        value = moved(base, shift)
        if cy != 0:
            ycross = r == (0 if cy == 1 else BE - 1)
            value = jnp.where(ycross, moved(yplane, shift), value)
        if cx != 0:
            xcross = q == (0 if cx == 1 else BE - 1)
            xvalue = moved(sideways(base, 0, cx), shift - BE * cx)
            if cy != 0:
                xvalue = jnp.where(ycross, moved(sideways(yplane, cy, cx), shift - BE * cx), xvalue)
            value = jnp.where(xcross, xvalue, value)
        return value

    blocked_of = {}
    for cx in (-1, 0, 1):
        for cy in (-1, 0, 1):
            blocked_of[(cx, cy)] = gathered(channels, 0, cx, cy) > 0.5
    for heading in range(27):
        cx, cy, cz = (int(v) for v in speeds[heading])
        blocked = blocked_of[(cx, cy)]
        for level in range(levels):
            bounced = post_ref[26 - heading, level]
            if cz == 1 and level == 0:
                out_ref[heading, level] = bounced
                continue
            if cz == 0:
                source = gathered(heading, level, cx, cy)
            elif cz == 1:
                source = gathered(heading, 0, cx, cy)
            elif level == 0:
                source = gathered(heading, 1, cx, cy)
            else:
                source = gathered(heading + 2, 1, cx, cy)
            out_ref[heading, level] = jnp.where(blocked, bounced, source)


def stream(fluid, post, below, above, from_left, from_right):
    channels, levels, blocks, cells = post.shape
    halo_rows = below.shape[0]
    vmem = pl.BlockSpec(memory_space=pltpu.VMEM)
    smem = pl.BlockSpec(memory_space=pltpu.SMEM)
    return pl.pallas_call(
        stream_kernel,
        out_shape=jax.ShapeDtypeStruct((channels, levels, blocks, cells), jnp.float32),
        in_specs=[smem] + [vmem] * 5,
        out_specs=vmem,
        scratch_shapes=[pltpu.VMEM((4, halo_rows + 16, cells), jnp.float32)],
    )(fluid, post, below, above, from_left, from_right)


def on_device(
    scaled_distributions,
    remaining_brick_places,
    retained_wavenumbers,
    regional_amplitudes,
    relaxation_frequencies,
):
    forward, backward, speeds = lattice_tables()
    slot_state = scaled_distributions[0, 0]
    living_brick_keys = remaining_brick_places[0, 0]
    seats = living_brick_keys.shape[0]
    channels = slot_state.shape[1]
    cells = BE * BE
    levels = slot_state.shape[2] // cells
    blocks = TX * TY
    rows_tile = TY * BE
    cols_tile = TX * BE
    positions = jnp.arange(blocks, dtype=jnp.int32)
    matches = living_brick_keys[None, :] == positions[:, None]
    slot_of = jnp.sum(jnp.where(matches, jnp.arange(seats, dtype=jnp.int32)[None, :], 0), axis=1)
    present = jnp.any(matches, axis=1)
    fluid = present.astype(jnp.float32)
    picked = jnp.take(slot_state.reshape(seats, channels, levels, cells), slot_of, axis=0)
    pops = picked.transpose(1, 2, 0, 3) * fluid[None, None, :, None]
    moments = jnp.einsum("ij,jzpl->izpl", forward, pops, precision=HIGHEST)
    safe_density = jnp.where(present[None, :, None], moments[0], 1.0)
    wind = jnp.stack([moments[9], moments[3], moments[1]], axis=0) / safe_density[None]
    line_length = lax.axis_size("line") * cols_tile
    own_columns = lax.axis_index("line") * cols_tile + jnp.arange(cols_tile, dtype=jnp.int32)
    mode_basis = mode_basis_at(retained_wavenumbers, own_columns, line_length).reshape(TX, BE, -1)
    partial = jnp.einsum(
        "kzyxrq,xqm->kzyrm", wind.reshape(3, levels, TY, TX, BE, BE), mode_basis,
        precision=HIGHEST,
    ).reshape(3, levels, rows_tile, -1)
    coefficients = butterfly_sum(partial, "line")
    misfit = regional_amplitudes - 2.0 / line_length * coefficients
    nudge = NUDGE_GAIN * jnp.einsum(
        "kzyrm,xqm->kzyxrq", misfit.reshape(3, levels, TY, BE, -1), mode_basis,
        precision=HIGHEST,
    ).reshape(3, levels, blocks, cells)
    post = collide_blocks(moments, wind, nudge, backward, relaxation_frequencies)
    solid = jnp.broadcast_to((1.0 - fluid)[None, None, :, None], (1, levels, blocks, cells))
    extended = jnp.concatenate([post, solid], axis=0)
    width = channels + 1
    ahead, behind = ring_pairs("curve")
    flat = lambda halo: halo.reshape(-1, BE)
    halo_shape = (width, levels, TX, BE)
    top_row = extended[:, :, blocks - TX:, cells - BE:]
    bottom_row = extended[:, :, :TX, :BE]
    below_flat = lax.ppermute(flat(top_row), "curve", ahead)
    above_flat = lax.ppermute(flat(bottom_row), "curve", behind)
    below = below_flat.reshape(halo_shape)
    above = above_flat.reshape(halo_shape)
    ahead, behind = ring_pairs("line")
    by_rows = extended.reshape(width, levels, TY, TX, BE, BE)
    right_cols = by_rows[:, :, :, TX - 1, :, BE - 1]
    left_cols = by_rows[:, :, :, 0, :, 0]
    to_right = jnp.concatenate(
        [
            jnp.broadcast_to(below[:, :, TX - 1:, BE - 1:], (width, levels, 1, BE)),
            right_cols,
            jnp.broadcast_to(above[:, :, TX - 1:, BE - 1:], (width, levels, 1, BE)),
        ],
        axis=2,
    )
    to_left = jnp.concatenate(
        [
            jnp.broadcast_to(below[:, :, :1, :1], (width, levels, 1, BE)),
            left_cols,
            jnp.broadcast_to(above[:, :, :1, :1], (width, levels, 1, BE)),
        ],
        axis=2,
    )
    from_left = lax.ppermute(flat(to_right), "line", ahead)
    from_right = lax.ppermute(flat(to_left), "line", behind)
    result = stream(fluid, post, below_flat, above_flat, from_left, from_right)
    by_block = result.transpose(2, 0, 1, 3).reshape(blocks, channels, levels * cells)
    occupied = living_brick_keys >= 0
    new_state = jnp.take(by_block, jnp.maximum(living_brick_keys, 0), axis=0)
    new_state = new_state * occupied[:, None, None].astype(jnp.float32)
    return new_state[None, None]


def solution(mesh):
    return jax.shard_map(
        on_device,
        mesh=mesh,
        in_specs=(
            P("curve", "line", None, None, None),
            P("curve", "line", None),
            P(),
            P(None, None, "curve", None),
            P(),
        ),
        out_specs=P("curve", "line", None, None, None),
        check_vma=False,
    )
```

```python
import jax
import jax.numpy as jnp
import numpy as np
from jax import lax
from jax.experimental import pallas as pl
from jax.experimental.pallas import tpu as pltpu
from jax.sharding import PartitionSpec as P

BE = 16
TX = 4
TY = 2


NUDGE_GAIN = 0.5
TWO_PI = 6.283185307179586
HIGHEST = lax.Precision.HIGHEST


def butterfly_sum(value, axis):
    count = lax.axis_size(axis)
    stride = 1
    while stride < count:
        value = value + lax.ppermute(value, axis, [(i, i ^ stride) for i in range(count)])
        stride *= 2
    return value


def ring_pairs(axis):
    count = lax.axis_size(axis)
    forward = [(i, (i + 1) % count) for i in range(count)]
    backward = [(target, source) for source, target in forward]
    return forward, backward


def lattice_tables():
    one_weights = np.array([1.0 / 6.0, 2.0 / 3.0, 1.0 / 6.0])
    speeds = np.array(
        [
            [along_x - 1, along_y - 1, along_z - 1]
            for along_x in range(3)
            for along_y in range(3)
            for along_z in range(3)
        ]
    )
    weights = np.array(
        [
            one_weights[along_x] * one_weights[along_y] * one_weights[along_z]
            for along_x in range(3)
            for along_y in range(3)
            for along_z in range(3)
        ]
    )
    vander = np.array([[1.0, 1.0, 1.0], [-1.0, 0.0, 1.0], [1.0, 0.0, 1.0]])
    undo_vander = np.array([[0.0, -0.5, 0.5], [1.0, 0.0, -1.0], [0.0, 0.5, 0.5]])
    moment_matrix = np.kron(vander, np.kron(vander, vander))
    inverse = np.kron(undo_vander, np.kron(undo_vander, undo_vander))
    forward = jnp.asarray(moment_matrix * weights[None, :], dtype=jnp.float32)
    backward = jnp.asarray(inverse / weights[:, None], dtype=jnp.float32)
    return (forward, backward, speeds)


def mode_basis_at(mode_ids, positions, length):
    phase_ids = positions[:, None] * mode_ids[None, :] % length
    angles = phase_ids.astype(jnp.float32) * (TWO_PI / length)
    return jnp.concatenate([jnp.cos(angles), jnp.sin(angles)], axis=1)


def collide_blocks(moments, velocity, nudge, backward, relaxation_frequencies):
    density = moments[0]
    shifted = velocity + nudge
    powers = jnp.stack([jnp.ones_like(shifted), shifted, shifted * shifted + 1.0 / 3.0], axis=0)
    equilibrium = (
        density[None, None, None]
        * powers[:, None, None, 0]
        * powers[None, :, None, 1]
        * powers[None, None, :, 2]
    )
    equilibrium = equilibrium.reshape(moments.shape)
    relaxed = moments - relaxation_frequencies[:, None, None, None] * (moments - equilibrium)
    return jnp.einsum("ij,jzpl->izpl", backward, relaxed, precision=HIGHEST)


def stream_kernel(fluid_ref, post_ref, below_ref, above_ref, left_ref, right_ref, out_ref, spread_ref):
    channels, levels, blocks, cells = post_ref.shape
    _, _, speeds = lattice_tables()
    front = 8
    grid_row = lax.broadcasted_iota(jnp.int32, (BE, cells), 0)
    grid_lane = lax.broadcasted_iota(jnp.int32, (BE, cells), 1)
    tile_copy = (grid_lane % BE == grid_row).astype(jnp.float32)
    group_copy = (grid_lane // BE == grid_row).astype(jnp.float32)
    halo_rows = below_ref.shape[0]
    for slot, (source, copier) in enumerate(
        ((below_ref, tile_copy), (above_ref, tile_copy), (left_ref, group_copy), (right_ref, group_copy))
    ):
        spread_ref[slot, front:front + halo_rows, :] = jnp.dot(
            source[...], copier, precision=HIGHEST, preferred_element_type=jnp.float32
        )
    lane = lax.broadcasted_iota(jnp.int32, (blocks, cells), 1)
    seat = lax.broadcasted_iota(jnp.int32, (blocks, cells), 0)
    q = lane % BE
    r = lane // BE
    py = seat // TX

    solid_plane = jnp.zeros((blocks, cells), jnp.float32)
    for block in range(blocks):
        solid_plane = jnp.where(seat == block, 1.0 - fluid_ref[block], solid_plane)

    def own(channel, level):
        if channel == channels:
            return solid_plane
        return post_ref[channel, level]

    def moved(plane, shift):
        shift = shift % cells
        if shift == 0:
            return plane
        return pltpu.roll(plane, shift, 1)

    def gathered(channel, level, cx, cy):
        shift = cy * BE + cx
        first = front + (channel * levels + level) * (TY + 2)
        base = own(channel, level)
        if cy != 0:
            stepped = pltpu.roll(base, TX, 0)
            if cy == 1:
                halo = spread_ref[0, first:first + blocks, :]
                yplane = jnp.where(py == 0, halo, stepped)
            else:
                halo = spread_ref[1, first - TX:first - TX + blocks, :]
                yplane = jnp.where(py == TY - 1, halo, stepped)

        def sideways(plane, dy, dx):
            plane = pltpu.roll(plane, dx % blocks, 0)
            edge = 0 if dx == 1 else TX - 1
            side = 2 if dx == 1 else 3
            at = first + 1 - dy
            return jnp.where(
                seat == edge,
                spread_ref[side, at:at + 1, :],
                jnp.where(seat == edge + TX, spread_ref[side, at + 1:at + 2, :], plane),
            )

        value = moved(base, shift)
        if cy != 0:
            ycross = r == (0 if cy == 1 else BE - 1)
            value = jnp.where(ycross, moved(yplane, shift), value)
        if cx != 0:
            xcross = q == (0 if cx == 1 else BE - 1)
            xvalue = moved(sideways(base, 0, cx), shift - BE * cx)
            if cy != 0:
                xvalue = jnp.where(ycross, moved(sideways(yplane, cy, cx), shift - BE * cx), xvalue)
            value = jnp.where(xcross, xvalue, value)
        return value

    blocked_of = {}
    for cx in (-1, 0, 1):
        for cy in (-1, 0, 1):
            blocked_of[(cx, cy)] = gathered(channels, 0, cx, cy) > 0.5
    for heading in range(27):
        cx, cy, cz = (int(v) for v in speeds[heading])
        blocked = blocked_of[(cx, cy)]
        for level in range(levels):
            bounced = post_ref[26 - heading, level]
            window = pl.ds(level * cells, cells)
            if cz == 1 and level == 0:
                out_ref[:, heading, window] = bounced
                continue
            if cz == 0:
                source = gathered(heading, level, cx, cy)
            elif cz == 1:
                source = gathered(heading, 0, cx, cy)
            elif level == 0:
                source = gathered(heading, 1, cx, cy)
            else:
                source = gathered(heading + 2, 1, cx, cy)
            out_ref[:, heading, window] = jnp.where(blocked, bounced, source)


def stream(fluid, post, below, above, from_left, from_right):
    channels, levels, blocks, cells = post.shape
    halo_rows = below.shape[0]
    vmem = pl.BlockSpec(memory_space=pltpu.VMEM)
    smem = pl.BlockSpec(memory_space=pltpu.SMEM)
    return pl.pallas_call(
        stream_kernel,
        out_shape=jax.ShapeDtypeStruct((blocks, channels, levels * cells), jnp.float32),
        in_specs=[smem] + [vmem] * 5,
        out_specs=vmem,
        scratch_shapes=[pltpu.VMEM((4, halo_rows + 16, cells), jnp.float32)],
    )(fluid, post, below, above, from_left, from_right)


def on_device(
    scaled_distributions,
    remaining_brick_places,
    retained_wavenumbers,
    regional_amplitudes,
    relaxation_frequencies,
):
    forward, backward, speeds = lattice_tables()
    slot_state = scaled_distributions[0, 0]
    living_brick_keys = remaining_brick_places[0, 0]
    seats = living_brick_keys.shape[0]
    channels = slot_state.shape[1]
    cells = BE * BE
    levels = slot_state.shape[2] // cells
    blocks = TX * TY
    rows_tile = TY * BE
    cols_tile = TX * BE
    positions = jnp.arange(blocks, dtype=jnp.int32)
    matches = living_brick_keys[None, :] == positions[:, None]
    code = jnp.max(jnp.where(matches, jnp.arange(1, seats + 1, dtype=jnp.int32)[None, :], 0), axis=1)
    present = code > 0
    slot_of = jnp.maximum(code - 1, 0)
    fluid = present.astype(jnp.float32)
    picked = jnp.take(slot_state.reshape(seats, channels, levels, cells), slot_of, axis=0)
    pops = picked.transpose(1, 2, 0, 3) * fluid[None, None, :, None]
    moments = jnp.einsum("ij,jzpl->izpl", forward, pops, precision=HIGHEST)
    safe_density = jnp.where(present[None, :, None], moments[0], 1.0)
    wind = jnp.stack([moments[9], moments[3], moments[1]], axis=0) / safe_density[None]
    line_length = lax.axis_size("line") * cols_tile
    own_columns = lax.axis_index("line") * cols_tile + jnp.arange(cols_tile, dtype=jnp.int32)
    mode_basis = mode_basis_at(retained_wavenumbers, own_columns, line_length).reshape(TX, BE, -1)
    partial = jnp.einsum(
        "kzyxrq,xqm->kzyrm", wind.reshape(3, levels, TY, TX, BE, BE), mode_basis,
        precision=HIGHEST,
    ).reshape(3, levels, rows_tile, -1)
    coefficients = butterfly_sum(partial, "line")
    misfit = regional_amplitudes - 2.0 / line_length * coefficients
    nudge = NUDGE_GAIN * jnp.einsum(
        "kzyrm,xqm->kzyxrq", misfit.reshape(3, levels, TY, BE, -1), mode_basis,
        precision=HIGHEST,
    ).reshape(3, levels, blocks, cells)
    post = collide_blocks(moments, wind, nudge, backward, relaxation_frequencies)
    solid = jnp.broadcast_to((1.0 - fluid)[None, None, :, None], (1, levels, blocks, cells))
    extended = jnp.concatenate([post, solid], axis=0)
    width = channels + 1
    ahead, behind = ring_pairs("curve")
    flat = lambda halo: halo.reshape(-1, BE)
    halo_shape = (width, levels, TX, BE)
    top_row = extended[:, :, blocks - TX:, cells - BE:]
    bottom_row = extended[:, :, :TX, :BE]
    below_flat = lax.ppermute(flat(top_row), "curve", ahead)
    above_flat = lax.ppermute(flat(bottom_row), "curve", behind)
    below = below_flat.reshape(halo_shape)
    above = above_flat.reshape(halo_shape)
    ahead, behind = ring_pairs("line")
    by_rows = extended.reshape(width, levels, TY, TX, BE, BE)
    right_cols = by_rows[:, :, :, TX - 1, :, BE - 1]
    left_cols = by_rows[:, :, :, 0, :, 0]
    to_right = jnp.concatenate(
        [
            jnp.broadcast_to(below[:, :, TX - 1:, BE - 1:], (width, levels, 1, BE)),
            right_cols,
            jnp.broadcast_to(above[:, :, TX - 1:, BE - 1:], (width, levels, 1, BE)),
        ],
        axis=2,
    )
    to_left = jnp.concatenate(
        [
            jnp.broadcast_to(below[:, :, :1, :1], (width, levels, 1, BE)),
            left_cols,
            jnp.broadcast_to(above[:, :, :1, :1], (width, levels, 1, BE)),
        ],
        axis=2,
    )
    from_left = lax.ppermute(flat(to_right), "line", ahead)
    from_right = lax.ppermute(flat(to_left), "line", behind)
    result = stream(fluid, post, below_flat, above_flat, from_left, from_right)
    by_block = result
    occupied = living_brick_keys >= 0
    new_state = jnp.take(by_block, jnp.maximum(living_brick_keys, 0), axis=0)
    new_state = new_state * occupied[:, None, None].astype(jnp.float32)
    return new_state[None, None]


def solution(mesh):
    return jax.shard_map(
        on_device,
        mesh=mesh,
        in_specs=(
            P("curve", "line", None, None, None),
            P("curve", "line", None),
            P(),
            P(None, None, "curve", None),
            P(),
        ),
        out_specs=P("curve", "line", None, None, None),
        check_vma=False,
    )
```

```python
import jax
import jax.numpy as jnp
import numpy as np
from jax import lax
from jax.experimental import pallas as pl
from jax.experimental.pallas import tpu as pltpu
from jax.sharding import PartitionSpec as P

BE = 16
TX = 4
TY = 2


NUDGE_GAIN = 0.5
TWO_PI = 6.283185307179586
HIGHEST = lax.Precision.HIGHEST


def butterfly_sum(value, axis):
    count = lax.axis_size(axis)
    stride = 1
    while stride < count:
        value = value + lax.ppermute(value, axis, [(i, i ^ stride) for i in range(count)])
        stride *= 2
    return value


def ring_pairs(axis):
    count = lax.axis_size(axis)
    forward = [(i, (i + 1) % count) for i in range(count)]
    backward = [(target, source) for source, target in forward]
    return forward, backward


def lattice_tables():
    one_weights = np.array([1.0 / 6.0, 2.0 / 3.0, 1.0 / 6.0])
    speeds = np.array(
        [
            [along_x - 1, along_y - 1, along_z - 1]
            for along_x in range(3)
            for along_y in range(3)
            for along_z in range(3)
        ]
    )
    weights = np.array(
        [
            one_weights[along_x] * one_weights[along_y] * one_weights[along_z]
            for along_x in range(3)
            for along_y in range(3)
            for along_z in range(3)
        ]
    )
    vander = np.array([[1.0, 1.0, 1.0], [-1.0, 0.0, 1.0], [1.0, 0.0, 1.0]])
    undo_vander = np.array([[0.0, -0.5, 0.5], [1.0, 0.0, -1.0], [0.0, 0.5, 0.5]])
    moment_matrix = np.kron(vander, np.kron(vander, vander))
    inverse = np.kron(undo_vander, np.kron(undo_vander, undo_vander))
    forward = jnp.asarray(moment_matrix * weights[None, :], dtype=jnp.float32)
    backward = jnp.asarray(inverse / weights[:, None], dtype=jnp.float32)
    return (forward, backward, speeds)


def mode_basis_at(mode_ids, positions, length):
    phase_ids = positions[:, None] * mode_ids[None, :] % length
    angles = phase_ids.astype(jnp.float32) * (TWO_PI / length)
    return jnp.concatenate([jnp.cos(angles), jnp.sin(angles)], axis=1)


def collide_blocks(moments, velocity, nudge, backward, relaxation_frequencies):
    density = moments[0]
    shifted = velocity + nudge
    powers = jnp.stack([jnp.ones_like(shifted), shifted, shifted * shifted + 1.0 / 3.0], axis=0)
    equilibrium = (
        density[None, None, None]
        * powers[:, None, None, 0]
        * powers[None, :, None, 1]
        * powers[None, None, :, 2]
    )
    equilibrium = equilibrium.reshape(moments.shape)
    relaxed = moments - relaxation_frequencies[:, None, None, None] * (moments - equilibrium)
    return jnp.einsum("ij,jzpl->izpl", backward, relaxed, precision=HIGHEST)


def stream_kernel(
    fluid_ref, keys_ref, post_ref, below_ref, above_ref, left_ref, right_ref, out_ref, spread_ref, result_ref
):
    levels, blocks, channels, cells = post_ref.shape
    _, _, speeds = lattice_tables()
    front = 8
    grid_row = lax.broadcasted_iota(jnp.int32, (BE, cells), 0)
    grid_lane = lax.broadcasted_iota(jnp.int32, (BE, cells), 1)
    tile_copy = (grid_lane % BE == grid_row).astype(jnp.float32)
    group_copy = (grid_lane // BE == grid_row).astype(jnp.float32)
    halo_rows = below_ref.shape[0]
    for slot, (source, copier) in enumerate(
        ((below_ref, tile_copy), (above_ref, tile_copy), (left_ref, group_copy), (right_ref, group_copy))
    ):
        spread_ref[slot, front:front + halo_rows, :] = jnp.dot(
            source[...], copier, precision=HIGHEST, preferred_element_type=jnp.float32
        )
    lane = lax.broadcasted_iota(jnp.int32, (blocks, cells), 1)
    seat = lax.broadcasted_iota(jnp.int32, (blocks, cells), 0)
    q = lane % BE
    r = lane // BE
    py = seat // TX

    solid_plane = jnp.zeros((blocks, cells), jnp.float32)
    for block in range(blocks):
        solid_plane = jnp.where(seat == block, 1.0 - fluid_ref[block], solid_plane)

    def own(channel, level):
        if channel == channels:
            return solid_plane
        return post_ref[level, :, channel, :]

    def moved(plane, shift):
        shift = shift % cells
        if shift == 0:
            return plane
        return pltpu.roll(plane, shift, 1)

    def gathered(channel, level, cx, cy):
        shift = cy * BE + cx
        first = front + (channel * levels + level) * (TY + 2)
        base = own(channel, level)
        if cy != 0:
            stepped = pltpu.roll(base, TX, 0)
            if cy == 1:
                halo = spread_ref[0, first:first + blocks, :]
                yplane = jnp.where(py == 0, halo, stepped)
            else:
                halo = spread_ref[1, first - TX:first - TX + blocks, :]
                yplane = jnp.where(py == TY - 1, halo, stepped)

        def sideways(plane, dy, dx):
            plane = pltpu.roll(plane, dx % blocks, 0)
            edge = 0 if dx == 1 else TX - 1
            side = 2 if dx == 1 else 3
            at = first + 1 - dy
            return jnp.where(
                seat == edge,
                spread_ref[side, at:at + 1, :],
                jnp.where(seat == edge + TX, spread_ref[side, at + 1:at + 2, :], plane),
            )

        value = moved(base, shift)
        if cy != 0:
            ycross = r == (0 if cy == 1 else BE - 1)
            value = jnp.where(ycross, moved(yplane, shift), value)
        if cx != 0:
            xcross = q == (0 if cx == 1 else BE - 1)
            xvalue = moved(sideways(base, 0, cx), shift - BE * cx)
            if cy != 0:
                xvalue = jnp.where(ycross, moved(sideways(yplane, cy, cx), shift - BE * cx), xvalue)
            value = jnp.where(xcross, xvalue, value)
        return value

    blocked_of = {}
    for cx in (-1, 0, 1):
        for cy in (-1, 0, 1):
            blocked_of[(cx, cy)] = gathered(channels, 0, cx, cy) > 0.5
    for heading in range(27):
        cx, cy, cz = (int(v) for v in speeds[heading])
        blocked = blocked_of[(cx, cy)]
        for level in range(levels):
            bounced = post_ref[level, :, 26 - heading, :]
            window = pl.ds(level * cells, cells)
            if cz == 1 and level == 0:
                result_ref[:, heading, window] = bounced
                continue
            if cz == 0:
                source = gathered(heading, level, cx, cy)
            elif cz == 1:
                source = gathered(heading, 0, cx, cy)
            elif level == 0:
                source = gathered(heading, 1, cx, cy)
            else:
                source = gathered(heading + 2, 1, cx, cy)
            result_ref[:, heading, window] = jnp.where(blocked, bounced, source)
    for seat_number in range(out_ref.shape[0]):
        key = keys_ref[seat_number]
        picked = result_ref[jnp.maximum(key, 0)]
        out_ref[seat_number] = jnp.where(key >= 0, picked, 0.0)


def stream(fluid, keys, post, below, above, from_left, from_right):
    channels, levels, blocks, cells = post.shape
    seats = keys.shape[0]
    halo_rows = below.shape[0]
    vmem = pl.BlockSpec(memory_space=pltpu.VMEM)
    smem = pl.BlockSpec(memory_space=pltpu.SMEM)
    return pl.pallas_call(
        stream_kernel,
        out_shape=jax.ShapeDtypeStruct((seats, channels, levels * cells), jnp.float32),
        in_specs=[smem, smem] + [vmem] * 5,
        out_specs=vmem,
        scratch_shapes=[
            pltpu.VMEM((4, halo_rows + 16, cells), jnp.float32),
            pltpu.VMEM((blocks, channels, levels * cells), jnp.float32),
        ],
    )(fluid, keys, post.transpose(1, 2, 0, 3), below, above, from_left, from_right)


def on_device(
    scaled_distributions,
    remaining_brick_places,
    retained_wavenumbers,
    regional_amplitudes,
    relaxation_frequencies,
):
    forward, backward, speeds = lattice_tables()
    slot_state = scaled_distributions[0, 0]
    living_brick_keys = remaining_brick_places[0, 0]
    seats = living_brick_keys.shape[0]
    channels = slot_state.shape[1]
    cells = BE * BE
    levels = slot_state.shape[2] // cells
    blocks = TX * TY
    rows_tile = TY * BE
    cols_tile = TX * BE
    positions = jnp.arange(blocks, dtype=jnp.int32)
    matches = living_brick_keys[None, :] == positions[:, None]
    code = jnp.max(jnp.where(matches, jnp.arange(1, seats + 1, dtype=jnp.int32)[None, :], 0), axis=1)
    present = code > 0
    slot_of = jnp.maximum(code - 1, 0)
    fluid = present.astype(jnp.float32)
    picked = jnp.take(slot_state.reshape(seats, channels, levels, cells), slot_of, axis=0)
    pops = picked.transpose(1, 2, 0, 3) * fluid[None, None, :, None]
    moments = jnp.einsum("ij,jzpl->izpl", forward, pops, precision=HIGHEST)
    safe_density = jnp.where(present[None, :, None], moments[0], 1.0)
    wind = jnp.stack([moments[9], moments[3], moments[1]], axis=0) / safe_density[None]
    line_length = lax.axis_size("line") * cols_tile
    own_columns = lax.axis_index("line") * cols_tile + jnp.arange(cols_tile, dtype=jnp.int32)
    mode_basis = mode_basis_at(retained_wavenumbers, own_columns, line_length).reshape(TX, BE, -1)
    partial = jnp.einsum(
        "kzyxrq,xqm->kzyrm", wind.reshape(3, levels, TY, TX, BE, BE), mode_basis,
        precision=HIGHEST,
    ).reshape(3, levels, rows_tile, -1)
    coefficients = butterfly_sum(partial, "line")
    misfit = regional_amplitudes - 2.0 / line_length * coefficients
    nudge = NUDGE_GAIN * jnp.einsum(
        "kzyrm,xqm->kzyxrq", misfit.reshape(3, levels, TY, BE, -1), mode_basis,
        precision=HIGHEST,
    ).reshape(3, levels, blocks, cells)
    post = collide_blocks(moments, wind, nudge, backward, relaxation_frequencies)
    solid = jnp.broadcast_to((1.0 - fluid)[None, None, :, None], (1, levels, blocks, cells))
    extended = jnp.concatenate([post, solid], axis=0)
    width = channels + 1
    ahead, behind = ring_pairs("curve")
    flat = lambda halo: halo.reshape(-1, BE)
    halo_shape = (width, levels, TX, BE)
    top_row = extended[:, :, blocks - TX:, cells - BE:]
    bottom_row = extended[:, :, :TX, :BE]
    below_flat = lax.ppermute(flat(top_row), "curve", ahead)
    above_flat = lax.ppermute(flat(bottom_row), "curve", behind)
    below = below_flat.reshape(halo_shape)
    above = above_flat.reshape(halo_shape)
    ahead, behind = ring_pairs("line")
    by_rows = extended.reshape(width, levels, TY, TX, BE, BE)
    right_cols = by_rows[:, :, :, TX - 1, :, BE - 1]
    left_cols = by_rows[:, :, :, 0, :, 0]
    to_right = jnp.concatenate(
        [
            jnp.broadcast_to(below[:, :, TX - 1:, BE - 1:], (width, levels, 1, BE)),
            right_cols,
            jnp.broadcast_to(above[:, :, TX - 1:, BE - 1:], (width, levels, 1, BE)),
        ],
        axis=2,
    )
    to_left = jnp.concatenate(
        [
            jnp.broadcast_to(below[:, :, :1, :1], (width, levels, 1, BE)),
            left_cols,
            jnp.broadcast_to(above[:, :, :1, :1], (width, levels, 1, BE)),
        ],
        axis=2,
    )
    from_left = lax.ppermute(flat(to_right), "line", ahead)
    from_right = lax.ppermute(flat(to_left), "line", behind)
    new_state = stream(fluid, living_brick_keys, post, below_flat, above_flat, from_left, from_right)
    return new_state[None, None]


def solution(mesh):
    return jax.shard_map(
        on_device,
        mesh=mesh,
        in_specs=(
            P("curve", "line", None, None, None),
            P("curve", "line", None),
            P(),
            P(None, None, "curve", None),
            P(),
        ),
        out_specs=P("curve", "line", None, None, None),
        check_vma=False,
    )
```

```python
import jax
import jax.numpy as jnp
import numpy as np
from jax import lax
from jax.experimental import pallas as pl
from jax.experimental.pallas import tpu as pltpu
from jax.sharding import PartitionSpec as P

BE = 16
TX = 4
TY = 2


NUDGE_GAIN = 0.5
TWO_PI = 6.283185307179586
HIGHEST = lax.Precision.HIGHEST


def butterfly_sum(value, axis):
    count = lax.axis_size(axis)
    stride = 1
    while stride < count:
        value = value + lax.ppermute(value, axis, [(i, i ^ stride) for i in range(count)])
        stride *= 2
    return value


def ring_pairs(axis):
    count = lax.axis_size(axis)
    forward = [(i, (i + 1) % count) for i in range(count)]
    backward = [(target, source) for source, target in forward]
    return forward, backward


def lattice_tables():
    one_weights = np.array([1.0 / 6.0, 2.0 / 3.0, 1.0 / 6.0])
    speeds = np.array(
        [
            [along_x - 1, along_y - 1, along_z - 1]
            for along_x in range(3)
            for along_y in range(3)
            for along_z in range(3)
        ]
    )
    weights = np.array(
        [
            one_weights[along_x] * one_weights[along_y] * one_weights[along_z]
            for along_x in range(3)
            for along_y in range(3)
            for along_z in range(3)
        ]
    )
    vander = np.array([[1.0, 1.0, 1.0], [-1.0, 0.0, 1.0], [1.0, 0.0, 1.0]])
    undo_vander = np.array([[0.0, -0.5, 0.5], [1.0, 0.0, -1.0], [0.0, 0.5, 0.5]])
    moment_matrix = np.kron(vander, np.kron(vander, vander))
    inverse = np.kron(undo_vander, np.kron(undo_vander, undo_vander))
    forward = jnp.asarray(moment_matrix * weights[None, :], dtype=jnp.float32)
    backward = jnp.asarray(inverse / weights[:, None], dtype=jnp.float32)
    return (forward, backward, speeds)


def mode_basis_at(mode_ids, positions, length):
    phase_ids = positions[:, None] * mode_ids[None, :] % length
    angles = phase_ids.astype(jnp.float32) * (TWO_PI / length)
    return jnp.concatenate([jnp.cos(angles), jnp.sin(angles)], axis=1)


def collide_blocks(moments, velocity, nudge, backward, relaxation_frequencies):
    density = moments[0]
    shifted = velocity + nudge
    powers = jnp.stack([jnp.ones_like(shifted), shifted, shifted * shifted + 1.0 / 3.0], axis=0)
    equilibrium = (
        density[None, None, None]
        * powers[:, None, None, 0]
        * powers[None, :, None, 1]
        * powers[None, None, :, 2]
    )
    equilibrium = equilibrium.reshape(moments.shape)
    relaxed = moments - relaxation_frequencies[:, None, None, None] * (moments - equilibrium)
    return jnp.einsum("ij,jzpl->izpl", backward, relaxed, precision=HIGHEST)


def stream_kernel(
    fluid_ref, keys_ref, post_ref, below_ref, above_ref, left_ref, right_ref, out_ref, spread_ref, result_ref
):
    levels, blocks, channels, cells = post_ref.shape
    _, _, speeds = lattice_tables()
    front = 8
    grid_row = lax.broadcasted_iota(jnp.int32, (BE, cells), 0)
    grid_lane = lax.broadcasted_iota(jnp.int32, (BE, cells), 1)
    tile_copy = (grid_lane % BE == grid_row).astype(jnp.float32)
    group_copy = (grid_lane // BE == grid_row).astype(jnp.float32)
    halo_rows = below_ref.shape[0]
    for slot, (source, copier) in enumerate(
        ((below_ref, tile_copy), (above_ref, tile_copy), (left_ref, group_copy), (right_ref, group_copy))
    ):
        spread_ref[slot, front:front + halo_rows, :] = jnp.dot(
            source[...], copier, precision=HIGHEST, preferred_element_type=jnp.float32
        )
    lane = lax.broadcasted_iota(jnp.int32, (blocks, cells), 1)
    seat = lax.broadcasted_iota(jnp.int32, (blocks, cells), 0)
    q = lane % BE
    r = lane // BE
    py = seat // TX

    solid_plane = jnp.zeros((blocks, cells), jnp.float32)
    for block in range(blocks):
        solid_plane = jnp.where(seat == block, 1.0 - fluid_ref[block], solid_plane)

    def own(channel, level):
        if channel == channels:
            return solid_plane
        return post_ref[level, :, channel, :]

    def moved(plane, shift):
        shift = shift % cells
        if shift == 0:
            return plane
        return pltpu.roll(plane, shift, 1)

    def gathered(channel, level, cx, cy):
        shift = cy * BE + cx
        first = front + (channel * levels + level) * (TY + 2)
        base = own(channel, level)
        if cy != 0:
            stepped = pltpu.roll(base, TX, 0)
            if cy == 1:
                halo = spread_ref[0, first:first + blocks, :]
                yplane = jnp.where(py == 0, halo, stepped)
            else:
                halo = spread_ref[1, first - TX:first - TX + blocks, :]
                yplane = jnp.where(py == TY - 1, halo, stepped)

        def sideways(plane, dy, dx):
            plane = pltpu.roll(plane, dx % blocks, 0)
            edge = 0 if dx == 1 else TX - 1
            side = 2 if dx == 1 else 3
            at = first + 1 - dy
            return jnp.where(
                seat == edge,
                spread_ref[side, at:at + 1, :],
                jnp.where(seat == edge + TX, spread_ref[side, at + 1:at + 2, :], plane),
            )

        value = moved(base, shift)
        if cy != 0:
            ycross = r == (0 if cy == 1 else BE - 1)
            value = jnp.where(ycross, moved(yplane, shift), value)
        if cx != 0:
            xcross = q == (0 if cx == 1 else BE - 1)
            xvalue = moved(sideways(base, 0, cx), shift - BE * cx)
            if cy != 0:
                xvalue = jnp.where(ycross, moved(sideways(yplane, cy, cx), shift - BE * cx), xvalue)
            value = jnp.where(xcross, xvalue, value)
        return value

    blocked_of = {}
    for cx in (-1, 0, 1):
        for cy in (-1, 0, 1):
            blocked_of[(cx, cy)] = gathered(channels, 0, cx, cy) > 0.5
    for heading in range(27):
        cx, cy, cz = (int(v) for v in speeds[heading])
        blocked = blocked_of[(cx, cy)]
        for level in range(levels):
            bounced = post_ref[level, :, 26 - heading, :]
            window = pl.ds(level * cells, cells)
            if cz == 1 and level == 0:
                result_ref[:, heading, window] = bounced
                continue
            if cz == 0:
                source = gathered(heading, level, cx, cy)
            elif cz == 1:
                source = gathered(heading, 0, cx, cy)
            elif level == 0:
                source = gathered(heading, 1, cx, cy)
            else:
                source = gathered(heading + 2, 1, cx, cy)
            result_ref[:, heading, window] = jnp.where(blocked, bounced, source)
    chunks = levels * cells // 128
    for seat_number in range(keys_ref.shape[0]):
        key = keys_ref[seat_number]
        for chunk in range(chunks):
            picked = result_ref[jnp.maximum(key, 0), :, chunk * 128:(chunk + 1) * 128]
            rows = pl.ds(seat_number * channels * chunks + chunk, channels, stride=chunks)
            out_ref[rows, :] = jnp.where(key >= 0, picked, 0.0)


def stream(fluid, keys, post, below, above, from_left, from_right):
    channels, levels, blocks, cells = post.shape
    seats = keys.shape[0]
    halo_rows = below.shape[0]
    vmem = pl.BlockSpec(memory_space=pltpu.VMEM)
    smem = pl.BlockSpec(memory_space=pltpu.SMEM)
    return pl.pallas_call(
        stream_kernel,
        out_shape=jax.ShapeDtypeStruct((seats * channels * levels * cells // 128, 128), jnp.float32),
        in_specs=[smem, smem] + [vmem] * 5,
        out_specs=vmem,
        scratch_shapes=[
            pltpu.VMEM((4, halo_rows + 16, cells), jnp.float32),
            pltpu.VMEM((blocks, channels, levels * cells), jnp.float32),
        ],
    )(fluid, keys, post.transpose(1, 2, 0, 3), below, above, from_left, from_right)


def on_device(
    scaled_distributions,
    remaining_brick_places,
    retained_wavenumbers,
    regional_amplitudes,
    relaxation_frequencies,
):
    forward, backward, speeds = lattice_tables()
    slot_state = scaled_distributions[0, 0]
    living_brick_keys = remaining_brick_places[0, 0]
    seats = living_brick_keys.shape[0]
    channels = slot_state.shape[1]
    cells = BE * BE
    levels = slot_state.shape[2] // cells
    blocks = TX * TY
    rows_tile = TY * BE
    cols_tile = TX * BE
    positions = jnp.arange(blocks, dtype=jnp.int32)
    matches = living_brick_keys[None, :] == positions[:, None]
    code = jnp.max(jnp.where(matches, jnp.arange(1, seats + 1, dtype=jnp.int32)[None, :], 0), axis=1)
    present = code > 0
    slot_of = jnp.maximum(code - 1, 0)
    fluid = present.astype(jnp.float32)
    picked = jnp.take(slot_state.reshape(seats, channels, levels, cells), slot_of, axis=0)
    pops = picked.transpose(1, 2, 0, 3) * fluid[None, None, :, None]
    moments = jnp.einsum("ij,jzpl->izpl", forward, pops, precision=HIGHEST)
    safe_density = jnp.where(present[None, :, None], moments[0], 1.0)
    wind = jnp.stack([moments[9], moments[3], moments[1]], axis=0) / safe_density[None]
    line_length = lax.axis_size("line") * cols_tile
    own_columns = lax.axis_index("line") * cols_tile + jnp.arange(cols_tile, dtype=jnp.int32)
    mode_basis = mode_basis_at(retained_wavenumbers, own_columns, line_length).reshape(TX, BE, -1)
    partial = jnp.einsum(
        "kzyxrq,xqm->kzyrm", wind.reshape(3, levels, TY, TX, BE, BE), mode_basis,
        precision=HIGHEST,
    ).reshape(3, levels, rows_tile, -1)
    coefficients = butterfly_sum(partial, "line")
    misfit = regional_amplitudes - 2.0 / line_length * coefficients
    nudge = NUDGE_GAIN * jnp.einsum(
        "kzyrm,xqm->kzyxrq", misfit.reshape(3, levels, TY, BE, -1), mode_basis,
        precision=HIGHEST,
    ).reshape(3, levels, blocks, cells)
    post = collide_blocks(moments, wind, nudge, backward, relaxation_frequencies)
    solid = jnp.broadcast_to((1.0 - fluid)[None, None, :, None], (1, levels, blocks, cells))
    extended = jnp.concatenate([post, solid], axis=0)
    width = channels + 1
    ahead, behind = ring_pairs("curve")
    flat = lambda halo: halo.reshape(-1, BE)
    halo_shape = (width, levels, TX, BE)
    top_row = extended[:, :, blocks - TX:, cells - BE:]
    bottom_row = extended[:, :, :TX, :BE]
    below_flat = lax.ppermute(flat(top_row), "curve", ahead)
    above_flat = lax.ppermute(flat(bottom_row), "curve", behind)
    below = below_flat.reshape(halo_shape)
    above = above_flat.reshape(halo_shape)
    ahead, behind = ring_pairs("line")
    by_rows = extended.reshape(width, levels, TY, TX, BE, BE)
    right_cols = by_rows[:, :, :, TX - 1, :, BE - 1]
    left_cols = by_rows[:, :, :, 0, :, 0]
    to_right = jnp.concatenate(
        [
            jnp.broadcast_to(below[:, :, TX - 1:, BE - 1:], (width, levels, 1, BE)),
            right_cols,
            jnp.broadcast_to(above[:, :, TX - 1:, BE - 1:], (width, levels, 1, BE)),
        ],
        axis=2,
    )
    to_left = jnp.concatenate(
        [
            jnp.broadcast_to(below[:, :, :1, :1], (width, levels, 1, BE)),
            left_cols,
            jnp.broadcast_to(above[:, :, :1, :1], (width, levels, 1, BE)),
        ],
        axis=2,
    )
    from_left = lax.ppermute(flat(to_right), "line", ahead)
    from_right = lax.ppermute(flat(to_left), "line", behind)
    new_state = stream(fluid, living_brick_keys, post, below_flat, above_flat, from_left, from_right)
    return new_state.reshape((1, 1, seats, channels, levels * cells))


def solution(mesh):
    return jax.shard_map(
        on_device,
        mesh=mesh,
        in_specs=(
            P("curve", "line", None, None, None),
            P("curve", "line", None),
            P(),
            P(None, None, "curve", None),
            P(),
        ),
        out_specs=P("curve", "line", None, None, None),
        check_vma=False,
    )
```

```python
import jax
import jax.numpy as jnp
import numpy as np
from jax import lax
from jax.experimental import pallas as pl
from jax.experimental.pallas import tpu as pltpu
from jax.sharding import PartitionSpec as P

BE = 16
TX = 4
TY = 2


NUDGE_GAIN = 0.5
TWO_PI = 6.283185307179586
HIGHEST = lax.Precision.HIGHEST


def butterfly_sum(value, axis):
    count = lax.axis_size(axis)
    stride = 1
    while stride < count:
        value = value + lax.ppermute(value, axis, [(i, i ^ stride) for i in range(count)])
        stride *= 2
    return value


def ring_pairs(axis):
    count = lax.axis_size(axis)
    forward = [(i, (i + 1) % count) for i in range(count)]
    backward = [(target, source) for source, target in forward]
    return forward, backward


def lattice_tables():
    one_weights = np.array([1.0 / 6.0, 2.0 / 3.0, 1.0 / 6.0])
    speeds = np.array(
        [
            [along_x - 1, along_y - 1, along_z - 1]
            for along_x in range(3)
            for along_y in range(3)
            for along_z in range(3)
        ]
    )
    weights = np.array(
        [
            one_weights[along_x] * one_weights[along_y] * one_weights[along_z]
            for along_x in range(3)
            for along_y in range(3)
            for along_z in range(3)
        ]
    )
    vander = np.array([[1.0, 1.0, 1.0], [-1.0, 0.0, 1.0], [1.0, 0.0, 1.0]])
    undo_vander = np.array([[0.0, -0.5, 0.5], [1.0, 0.0, -1.0], [0.0, 0.5, 0.5]])
    moment_matrix = np.kron(vander, np.kron(vander, vander))
    inverse = np.kron(undo_vander, np.kron(undo_vander, undo_vander))
    forward = jnp.asarray(moment_matrix * weights[None, :], dtype=jnp.float32)
    backward = jnp.asarray(inverse / weights[:, None], dtype=jnp.float32)
    return (forward, backward, speeds)


def mode_basis_at(mode_ids, positions, length):
    phase_ids = positions[:, None] * mode_ids[None, :] % length
    angles = phase_ids.astype(jnp.float32) * (TWO_PI / length)
    return jnp.concatenate([jnp.cos(angles), jnp.sin(angles)], axis=1)


def collide_blocks(moments, velocity, nudge, backward, relaxation_frequencies):
    density = moments[0]
    shifted = velocity + nudge
    powers = jnp.stack([jnp.ones_like(shifted), shifted, shifted * shifted + 1.0 / 3.0], axis=0)
    equilibrium = (
        density[None, None, None]
        * powers[:, None, None, 0]
        * powers[None, :, None, 1]
        * powers[None, None, :, 2]
    )
    equilibrium = equilibrium.reshape(moments.shape)
    relaxed = moments - relaxation_frequencies[:, None, None, None] * (moments - equilibrium)
    return jnp.einsum("ij,jzpl->izpl", backward, relaxed, precision=HIGHEST)


def moments_kernel(slot_ref, fluid_ref, forward_ref, state_ref, out_ref, scratch_ref):
    levels, blocks, channels, cells = out_ref.shape
    seats = scratch_ref.shape[0]
    chunks = levels * cells // 128
    forward = forward_ref[...]
    for seat_number in range(seats):
        pieces = [
            state_ref[pl.ds(seat_number * channels * chunks + chunk, channels, stride=chunks), :]
            for chunk in range(chunks)
        ]
        scratch_ref[seat_number] = jnp.dot(
            forward, jnp.concatenate(pieces, axis=1), precision=HIGHEST,
            preferred_element_type=jnp.float32,
        )
    for block in range(blocks):
        slot = slot_ref[block]
        keep = fluid_ref[block]
        for level in range(levels):
            out_ref[level, block] = scratch_ref[slot, :, level * cells:(level + 1) * cells] * keep


def cell_moments(slot_of, fluid, forward, rows, seats, levels):
    channels = forward.shape[0]
    cells = rows.size // (seats * channels * levels)
    vmem = pl.BlockSpec(memory_space=pltpu.VMEM)
    smem = pl.BlockSpec(memory_space=pltpu.SMEM)
    return pl.pallas_call(
        moments_kernel,
        out_shape=jax.ShapeDtypeStruct((levels, TX * TY, channels, cells), jnp.float32),
        in_specs=[smem, smem, vmem, vmem],
        out_specs=vmem,
        scratch_shapes=[pltpu.VMEM((seats, channels, levels * cells), jnp.float32)],
    )(slot_of, fluid, forward, rows)


def stream_kernel(
    fluid_ref, keys_ref, post_ref, below_ref, above_ref, left_ref, right_ref, out_ref, spread_ref, result_ref
):
    levels, blocks, channels, cells = post_ref.shape
    _, _, speeds = lattice_tables()
    front = 8
    grid_row = lax.broadcasted_iota(jnp.int32, (BE, cells), 0)
    grid_lane = lax.broadcasted_iota(jnp.int32, (BE, cells), 1)
    tile_copy = (grid_lane % BE == grid_row).astype(jnp.float32)
    group_copy = (grid_lane // BE == grid_row).astype(jnp.float32)
    halo_rows = below_ref.shape[0]
    for slot, (source, copier) in enumerate(
        ((below_ref, tile_copy), (above_ref, tile_copy), (left_ref, group_copy), (right_ref, group_copy))
    ):
        spread_ref[slot, front:front + halo_rows, :] = jnp.dot(
            source[...], copier, precision=HIGHEST, preferred_element_type=jnp.float32
        )
    lane = lax.broadcasted_iota(jnp.int32, (blocks, cells), 1)
    seat = lax.broadcasted_iota(jnp.int32, (blocks, cells), 0)
    q = lane % BE
    r = lane // BE
    py = seat // TX

    solid_plane = jnp.zeros((blocks, cells), jnp.float32)
    for block in range(blocks):
        solid_plane = jnp.where(seat == block, 1.0 - fluid_ref[block], solid_plane)

    def own(channel, level):
        if channel == channels:
            return solid_plane
        return post_ref[level, :, channel, :]

    def moved(plane, shift):
        shift = shift % cells
        if shift == 0:
            return plane
        return pltpu.roll(plane, shift, 1)

    def gathered(channel, level, cx, cy):
        shift = cy * BE + cx
        first = front + (channel * levels + level) * (TY + 2)
        base = own(channel, level)
        if cy != 0:
            stepped = pltpu.roll(base, TX, 0)
            if cy == 1:
                halo = spread_ref[0, first:first + blocks, :]
                yplane = jnp.where(py == 0, halo, stepped)
            else:
                halo = spread_ref[1, first - TX:first - TX + blocks, :]
                yplane = jnp.where(py == TY - 1, halo, stepped)

        def sideways(plane, dy, dx):
            plane = pltpu.roll(plane, dx % blocks, 0)
            edge = 0 if dx == 1 else TX - 1
            side = 2 if dx == 1 else 3
            at = first + 1 - dy
            return jnp.where(
                seat == edge,
                spread_ref[side, at:at + 1, :],
                jnp.where(seat == edge + TX, spread_ref[side, at + 1:at + 2, :], plane),
            )

        value = moved(base, shift)
        if cy != 0:
            ycross = r == (0 if cy == 1 else BE - 1)
            value = jnp.where(ycross, moved(yplane, shift), value)
        if cx != 0:
            xcross = q == (0 if cx == 1 else BE - 1)
            xvalue = moved(sideways(base, 0, cx), shift - BE * cx)
            if cy != 0:
                xvalue = jnp.where(ycross, moved(sideways(yplane, cy, cx), shift - BE * cx), xvalue)
            value = jnp.where(xcross, xvalue, value)
        return value

    blocked_of = {}
    for cx in (-1, 0, 1):
        for cy in (-1, 0, 1):
            blocked_of[(cx, cy)] = gathered(channels, 0, cx, cy) > 0.5
    for heading in range(27):
        cx, cy, cz = (int(v) for v in speeds[heading])
        blocked = blocked_of[(cx, cy)]
        for level in range(levels):
            bounced = post_ref[level, :, 26 - heading, :]
            window = pl.ds(level * cells, cells)
            if cz == 1 and level == 0:
                result_ref[:, heading, window] = bounced
                continue
            if cz == 0:
                source = gathered(heading, level, cx, cy)
            elif cz == 1:
                source = gathered(heading, 0, cx, cy)
            elif level == 0:
                source = gathered(heading, 1, cx, cy)
            else:
                source = gathered(heading + 2, 1, cx, cy)
            result_ref[:, heading, window] = jnp.where(blocked, bounced, source)
    chunks = levels * cells // 128
    for seat_number in range(keys_ref.shape[0]):
        key = keys_ref[seat_number]
        for chunk in range(chunks):
            picked = result_ref[jnp.maximum(key, 0), :, chunk * 128:(chunk + 1) * 128]
            rows = pl.ds(seat_number * channels * chunks + chunk, channels, stride=chunks)
            out_ref[rows, :] = jnp.where(key >= 0, picked, 0.0)


def stream(fluid, keys, post, below, above, from_left, from_right):
    channels, levels, blocks, cells = post.shape
    seats = keys.shape[0]
    halo_rows = below.shape[0]
    vmem = pl.BlockSpec(memory_space=pltpu.VMEM)
    smem = pl.BlockSpec(memory_space=pltpu.SMEM)
    return pl.pallas_call(
        stream_kernel,
        out_shape=jax.ShapeDtypeStruct((seats * channels * levels * cells // 128, 128), jnp.float32),
        in_specs=[smem, smem] + [vmem] * 5,
        out_specs=vmem,
        scratch_shapes=[
            pltpu.VMEM((4, halo_rows + 16, cells), jnp.float32),
            pltpu.VMEM((blocks, channels, levels * cells), jnp.float32),
        ],
    )(fluid, keys, post.transpose(1, 2, 0, 3), below, above, from_left, from_right)


def on_device(
    scaled_distributions,
    remaining_brick_places,
    retained_wavenumbers,
    regional_amplitudes,
    relaxation_frequencies,
):
    forward, backward, speeds = lattice_tables()
    slot_state = scaled_distributions[0, 0]
    living_brick_keys = remaining_brick_places[0, 0]
    seats = living_brick_keys.shape[0]
    channels = slot_state.shape[1]
    cells = BE * BE
    levels = slot_state.shape[2] // cells
    blocks = TX * TY
    rows_tile = TY * BE
    cols_tile = TX * BE
    positions = jnp.arange(blocks, dtype=jnp.int32)
    matches = living_brick_keys[None, :] == positions[:, None]
    code = jnp.max(jnp.where(matches, jnp.arange(1, seats + 1, dtype=jnp.int32)[None, :], 0), axis=1)
    present = code > 0
    slot_of = jnp.maximum(code - 1, 0)
    fluid = present.astype(jnp.float32)
    rows = slot_state.reshape(-1, 128)
    moments = cell_moments(slot_of, fluid, forward, rows, seats, levels).transpose(2, 0, 1, 3)
    safe_density = jnp.where(present[None, :, None], moments[0], 1.0)
    wind = jnp.stack([moments[9], moments[3], moments[1]], axis=0) / safe_density[None]
    line_length = lax.axis_size("line") * cols_tile
    own_columns = lax.axis_index("line") * cols_tile + jnp.arange(cols_tile, dtype=jnp.int32)
    mode_basis = mode_basis_at(retained_wavenumbers, own_columns, line_length).reshape(TX, BE, -1)
    partial = jnp.einsum(
        "kzyxrq,xqm->kzyrm", wind.reshape(3, levels, TY, TX, BE, BE), mode_basis,
        precision=HIGHEST,
    ).reshape(3, levels, rows_tile, -1)
    coefficients = butterfly_sum(partial, "line")
    misfit = regional_amplitudes - 2.0 / line_length * coefficients
    nudge = NUDGE_GAIN * jnp.einsum(
        "kzyrm,xqm->kzyxrq", misfit.reshape(3, levels, TY, BE, -1), mode_basis,
        precision=HIGHEST,
    ).reshape(3, levels, blocks, cells)
    post = collide_blocks(moments, wind, nudge, backward, relaxation_frequencies)
    solid = jnp.broadcast_to((1.0 - fluid)[None, None, :, None], (1, levels, blocks, cells))
    extended = jnp.concatenate([post, solid], axis=0)
    width = channels + 1
    ahead, behind = ring_pairs("curve")
    flat = lambda halo: halo.reshape(-1, BE)
    halo_shape = (width, levels, TX, BE)
    top_row = extended[:, :, blocks - TX:, cells - BE:]
    bottom_row = extended[:, :, :TX, :BE]
    below_flat = lax.ppermute(flat(top_row), "curve", ahead)
    above_flat = lax.ppermute(flat(bottom_row), "curve", behind)
    below = below_flat.reshape(halo_shape)
    above = above_flat.reshape(halo_shape)
    ahead, behind = ring_pairs("line")
    by_rows = extended.reshape(width, levels, TY, TX, BE, BE)
    right_cols = by_rows[:, :, :, TX - 1, :, BE - 1]
    left_cols = by_rows[:, :, :, 0, :, 0]
    to_right = jnp.concatenate(
        [
            jnp.broadcast_to(below[:, :, TX - 1:, BE - 1:], (width, levels, 1, BE)),
            right_cols,
            jnp.broadcast_to(above[:, :, TX - 1:, BE - 1:], (width, levels, 1, BE)),
        ],
        axis=2,
    )
    to_left = jnp.concatenate(
        [
            jnp.broadcast_to(below[:, :, :1, :1], (width, levels, 1, BE)),
            left_cols,
            jnp.broadcast_to(above[:, :, :1, :1], (width, levels, 1, BE)),
        ],
        axis=2,
    )
    from_left = lax.ppermute(flat(to_right), "line", ahead)
    from_right = lax.ppermute(flat(to_left), "line", behind)
    new_state = stream(fluid, living_brick_keys, post, below_flat, above_flat, from_left, from_right)
    return new_state.reshape((1, 1, seats, channels, levels * cells))


def solution(mesh):
    return jax.shard_map(
        on_device,
        mesh=mesh,
        in_specs=(
            P("curve", "line", None, None, None),
            P("curve", "line", None),
            P(),
            P(None, None, "curve", None),
            P(),
        ),
        out_specs=P("curve", "line", None, None, None),
        check_vma=False,
    )
```

```python
import jax
import jax.numpy as jnp
import numpy as np
from jax import lax
from jax.experimental import pallas as pl
from jax.experimental.pallas import tpu as pltpu
from jax.sharding import PartitionSpec as P

BE = 16
TX = 4
TY = 2


NUDGE_GAIN = 0.5
TWO_PI = 6.283185307179586
HIGHEST = lax.Precision.HIGHEST


def butterfly_sum(value, axis):
    count = lax.axis_size(axis)
    stride = 1
    while stride < count:
        value = value + lax.ppermute(value, axis, [(i, i ^ stride) for i in range(count)])
        stride *= 2
    return value


def ring_pairs(axis):
    count = lax.axis_size(axis)
    forward = [(i, (i + 1) % count) for i in range(count)]
    backward = [(target, source) for source, target in forward]
    return forward, backward


def lattice_tables():
    one_weights = np.array([1.0 / 6.0, 2.0 / 3.0, 1.0 / 6.0])
    speeds = np.array(
        [
            [along_x - 1, along_y - 1, along_z - 1]
            for along_x in range(3)
            for along_y in range(3)
            for along_z in range(3)
        ]
    )
    weights = np.array(
        [
            one_weights[along_x] * one_weights[along_y] * one_weights[along_z]
            for along_x in range(3)
            for along_y in range(3)
            for along_z in range(3)
        ]
    )
    vander = np.array([[1.0, 1.0, 1.0], [-1.0, 0.0, 1.0], [1.0, 0.0, 1.0]])
    undo_vander = np.array([[0.0, -0.5, 0.5], [1.0, 0.0, -1.0], [0.0, 0.5, 0.5]])
    moment_matrix = np.kron(vander, np.kron(vander, vander))
    inverse = np.kron(undo_vander, np.kron(undo_vander, undo_vander))
    forward = jnp.asarray(moment_matrix * weights[None, :], dtype=jnp.float32)
    backward = jnp.asarray(inverse / weights[:, None], dtype=jnp.float32)
    return (forward, backward, speeds)


def mode_basis_at(mode_ids, positions, length):
    phase_ids = positions[:, None] * mode_ids[None, :] % length
    angles = phase_ids.astype(jnp.float32) * (TWO_PI / length)
    return jnp.concatenate([jnp.cos(angles), jnp.sin(angles)], axis=1)


def collide_blocks(moments, velocity, nudge, backward, relaxation_frequencies):
    density = moments[0]
    shifted = velocity + nudge
    powers = jnp.stack([jnp.ones_like(shifted), shifted, shifted * shifted + 1.0 / 3.0], axis=0)
    equilibrium = (
        density[None, None, None]
        * powers[:, None, None, 0]
        * powers[None, :, None, 1]
        * powers[None, None, :, 2]
    )
    equilibrium = equilibrium.reshape(moments.shape)
    relaxed = moments - relaxation_frequencies[:, None, None, None] * (moments - equilibrium)
    return jnp.einsum("ij,jzpl->izpl", backward, relaxed, precision=HIGHEST)


def moments_kernel(keys_ref, forward_ref, state_ref, out_ref, wind_ref, solid_ref, scratch_ref):
    levels, blocks, channels, cells = out_ref.shape
    seats = scratch_ref.shape[0]
    chunks = levels * cells // 128
    forward = forward_ref[...]
    for seat_number in range(seats):
        pieces = [
            state_ref[pl.ds(seat_number * channels * chunks + chunk, channels, stride=chunks), :]
            for chunk in range(chunks)
        ]
        scratch_ref[seat_number] = jnp.dot(
            forward, jnp.concatenate(pieces, axis=1), precision=HIGHEST,
            preferred_element_type=jnp.float32,
        )
    for block in range(blocks):
        slot = 0
        found = False
        for seat_number in range(seats):
            hit = keys_ref[seat_number] == block
            slot = jnp.where(hit, seat_number, slot)
            found = jnp.logical_or(found, hit)
        keep = jnp.where(found, 1.0, 0.0)
        for level in range(levels):
            values = scratch_ref[slot, :, level * cells:(level + 1) * cells] * keep
            out_ref[level, block] = values
            density = jnp.where(found, values[0:1], 1.0)
            for component, row in enumerate((9, 3, 1)):
                wind_ref[component, level, block:block + 1, :] = values[row:row + 1] / density
            solid_ref[level, block:block + 1, :] = jnp.broadcast_to(1.0 - keep, (1, cells))


def cell_moments(keys, forward, rows, seats, levels):
    channels = forward.shape[0]
    blocks = TX * TY
    cells = rows.size // (seats * channels * levels)
    vmem = pl.BlockSpec(memory_space=pltpu.VMEM)
    smem = pl.BlockSpec(memory_space=pltpu.SMEM)
    return pl.pallas_call(
        moments_kernel,
        out_shape=(
            jax.ShapeDtypeStruct((levels, blocks, channels, cells), jnp.float32),
            jax.ShapeDtypeStruct((3, levels, blocks, cells), jnp.float32),
            jax.ShapeDtypeStruct((levels, blocks, cells), jnp.float32),
        ),
        in_specs=[smem, vmem, vmem],
        out_specs=(vmem, vmem, vmem),
        scratch_shapes=[pltpu.VMEM((seats, channels, levels * cells), jnp.float32)],
    )(keys, forward, rows)


def stream_kernel(
    keys_ref, solid_ref, post_ref, below_ref, above_ref, left_ref, right_ref, out_ref, spread_ref, result_ref
):
    levels, blocks, channels, cells = post_ref.shape
    _, _, speeds = lattice_tables()
    front = 8
    grid_row = lax.broadcasted_iota(jnp.int32, (BE, cells), 0)
    grid_lane = lax.broadcasted_iota(jnp.int32, (BE, cells), 1)
    tile_copy = (grid_lane % BE == grid_row).astype(jnp.float32)
    group_copy = (grid_lane // BE == grid_row).astype(jnp.float32)
    halo_rows = below_ref.shape[0]
    for slot, (source, copier) in enumerate(
        ((below_ref, tile_copy), (above_ref, tile_copy), (left_ref, group_copy), (right_ref, group_copy))
    ):
        spread_ref[slot, front:front + halo_rows, :] = jnp.dot(
            source[...], copier, precision=HIGHEST, preferred_element_type=jnp.float32
        )
    lane = lax.broadcasted_iota(jnp.int32, (blocks, cells), 1)
    seat = lax.broadcasted_iota(jnp.int32, (blocks, cells), 0)
    q = lane % BE
    r = lane // BE
    py = seat // TX

    solid_plane = solid_ref[...]

    def own(channel, level):
        if channel == channels:
            return solid_plane
        return post_ref[level, :, channel, :]

    def moved(plane, shift):
        shift = shift % cells
        if shift == 0:
            return plane
        return pltpu.roll(plane, shift, 1)

    def gathered(channel, level, cx, cy):
        shift = cy * BE + cx
        first = front + (channel * levels + level) * (TY + 2)
        base = own(channel, level)
        if cy != 0:
            stepped = pltpu.roll(base, TX, 0)
            if cy == 1:
                halo = spread_ref[0, first:first + blocks, :]
                yplane = jnp.where(py == 0, halo, stepped)
            else:
                halo = spread_ref[1, first - TX:first - TX + blocks, :]
                yplane = jnp.where(py == TY - 1, halo, stepped)

        def sideways(plane, dy, dx):
            plane = pltpu.roll(plane, dx % blocks, 0)
            edge = 0 if dx == 1 else TX - 1
            side = 2 if dx == 1 else 3
            at = first + 1 - dy
            return jnp.where(
                seat == edge,
                spread_ref[side, at:at + 1, :],
                jnp.where(seat == edge + TX, spread_ref[side, at + 1:at + 2, :], plane),
            )

        value = moved(base, shift)
        if cy != 0:
            ycross = r == (0 if cy == 1 else BE - 1)
            value = jnp.where(ycross, moved(yplane, shift), value)
        if cx != 0:
            xcross = q == (0 if cx == 1 else BE - 1)
            xvalue = moved(sideways(base, 0, cx), shift - BE * cx)
            if cy != 0:
                xvalue = jnp.where(ycross, moved(sideways(yplane, cy, cx), shift - BE * cx), xvalue)
            value = jnp.where(xcross, xvalue, value)
        return value

    blocked_of = {}
    for cx in (-1, 0, 1):
        for cy in (-1, 0, 1):
            blocked_of[(cx, cy)] = gathered(channels, 0, cx, cy) > 0.5
    for heading in range(27):
        cx, cy, cz = (int(v) for v in speeds[heading])
        blocked = blocked_of[(cx, cy)]
        for level in range(levels):
            bounced = post_ref[level, :, 26 - heading, :]
            window = pl.ds(level * cells, cells)
            if cz == 1 and level == 0:
                result_ref[:, heading, window] = bounced
                continue
            if cz == 0:
                source = gathered(heading, level, cx, cy)
            elif cz == 1:
                source = gathered(heading, 0, cx, cy)
            elif level == 0:
                source = gathered(heading, 1, cx, cy)
            else:
                source = gathered(heading + 2, 1, cx, cy)
            result_ref[:, heading, window] = jnp.where(blocked, bounced, source)
    chunks = levels * cells // 128
    for seat_number in range(keys_ref.shape[0]):
        key = keys_ref[seat_number]
        for chunk in range(chunks):
            picked = result_ref[jnp.maximum(key, 0), :, chunk * 128:(chunk + 1) * 128]
            rows = pl.ds(seat_number * channels * chunks + chunk, channels, stride=chunks)
            out_ref[rows, :] = jnp.where(key >= 0, picked, 0.0)


def stream(keys, solid_plane, post, below, above, from_left, from_right):
    channels, levels, blocks, cells = post.shape
    seats = keys.shape[0]
    halo_rows = below.shape[0]
    vmem = pl.BlockSpec(memory_space=pltpu.VMEM)
    smem = pl.BlockSpec(memory_space=pltpu.SMEM)
    return pl.pallas_call(
        stream_kernel,
        out_shape=jax.ShapeDtypeStruct((seats * channels * levels * cells // 128, 128), jnp.float32),
        in_specs=[smem] + [vmem] * 6,
        out_specs=vmem,
        scratch_shapes=[
            pltpu.VMEM((4, halo_rows + 16, cells), jnp.float32),
            pltpu.VMEM((blocks, channels, levels * cells), jnp.float32),
        ],
    )(keys, solid_plane, post.transpose(1, 2, 0, 3), below, above, from_left, from_right)


def on_device(
    scaled_distributions,
    remaining_brick_places,
    retained_wavenumbers,
    regional_amplitudes,
    relaxation_frequencies,
):
    forward, backward, speeds = lattice_tables()
    slot_state = scaled_distributions[0, 0]
    living_brick_keys = remaining_brick_places[0, 0]
    seats = living_brick_keys.shape[0]
    channels = slot_state.shape[1]
    cells = BE * BE
    levels = slot_state.shape[2] // cells
    blocks = TX * TY
    rows_tile = TY * BE
    cols_tile = TX * BE
    rows = slot_state.reshape(-1, 128)
    moments, wind, solid_plane = cell_moments(living_brick_keys, forward, rows, seats, levels)
    moments = moments.transpose(2, 0, 1, 3)
    line_length = lax.axis_size("line") * cols_tile
    own_columns = lax.axis_index("line") * cols_tile + jnp.arange(cols_tile, dtype=jnp.int32)
    mode_basis = mode_basis_at(retained_wavenumbers, own_columns, line_length).reshape(TX, BE, -1)
    partial = jnp.einsum(
        "kzyxrq,xqm->kzyrm", wind.reshape(3, levels, TY, TX, BE, BE), mode_basis,
        precision=HIGHEST,
    ).reshape(3, levels, rows_tile, -1)
    coefficients = butterfly_sum(partial, "line")
    misfit = regional_amplitudes - 2.0 / line_length * coefficients
    nudge = NUDGE_GAIN * jnp.einsum(
        "kzyrm,xqm->kzyxrq", misfit.reshape(3, levels, TY, BE, -1), mode_basis,
        precision=HIGHEST,
    ).reshape(3, levels, blocks, cells)
    post = collide_blocks(moments, wind, nudge, backward, relaxation_frequencies)
    solid = solid_plane[None]
    extended = jnp.concatenate([post, solid], axis=0)
    width = channels + 1
    ahead, behind = ring_pairs("curve")
    flat = lambda halo: halo.reshape(-1, BE)
    halo_shape = (width, levels, TX, BE)
    top_row = extended[:, :, blocks - TX:, cells - BE:]
    bottom_row = extended[:, :, :TX, :BE]
    below_flat = lax.ppermute(flat(top_row), "curve", ahead)
    above_flat = lax.ppermute(flat(bottom_row), "curve", behind)
    below = below_flat.reshape(halo_shape)
    above = above_flat.reshape(halo_shape)
    ahead, behind = ring_pairs("line")
    by_rows = extended.reshape(width, levels, TY, TX, BE, BE)
    right_cols = by_rows[:, :, :, TX - 1, :, BE - 1]
    left_cols = by_rows[:, :, :, 0, :, 0]
    to_right = jnp.concatenate(
        [
            jnp.broadcast_to(below[:, :, TX - 1:, BE - 1:], (width, levels, 1, BE)),
            right_cols,
            jnp.broadcast_to(above[:, :, TX - 1:, BE - 1:], (width, levels, 1, BE)),
        ],
        axis=2,
    )
    to_left = jnp.concatenate(
        [
            jnp.broadcast_to(below[:, :, :1, :1], (width, levels, 1, BE)),
            left_cols,
            jnp.broadcast_to(above[:, :, :1, :1], (width, levels, 1, BE)),
        ],
        axis=2,
    )
    from_left = lax.ppermute(flat(to_right), "line", ahead)
    from_right = lax.ppermute(flat(to_left), "line", behind)
    new_state = stream(living_brick_keys, solid_plane[0], post, below_flat, above_flat, from_left, from_right)
    return new_state.reshape((1, 1, seats, channels, levels * cells))


def solution(mesh):
    return jax.shard_map(
        on_device,
        mesh=mesh,
        in_specs=(
            P("curve", "line", None, None, None),
            P("curve", "line", None),
            P(),
            P(None, None, "curve", None),
            P(),
        ),
        out_specs=P("curve", "line", None, None, None),
        check_vma=False,
    )
```

```python
import jax
import jax.numpy as jnp
import numpy as np
from jax import lax
from jax.experimental import pallas as pl
from jax.experimental.pallas import tpu as pltpu
from jax.sharding import PartitionSpec as P

BE = 16
TX = 4
TY = 2


NUDGE_GAIN = 0.5
TWO_PI = 6.283185307179586
HIGHEST = lax.Precision.HIGHEST


def butterfly_sum(value, axis):
    count = lax.axis_size(axis)
    stride = 1
    while stride < count:
        value = value + lax.ppermute(value, axis, [(i, i ^ stride) for i in range(count)])
        stride *= 2
    return value


def ring_pairs(axis):
    count = lax.axis_size(axis)
    forward = [(i, (i + 1) % count) for i in range(count)]
    backward = [(target, source) for source, target in forward]
    return forward, backward


def lattice_tables():
    one_weights = np.array([1.0 / 6.0, 2.0 / 3.0, 1.0 / 6.0])
    speeds = np.array(
        [
            [along_x - 1, along_y - 1, along_z - 1]
            for along_x in range(3)
            for along_y in range(3)
            for along_z in range(3)
        ]
    )
    weights = np.array(
        [
            one_weights[along_x] * one_weights[along_y] * one_weights[along_z]
            for along_x in range(3)
            for along_y in range(3)
            for along_z in range(3)
        ]
    )
    vander = np.array([[1.0, 1.0, 1.0], [-1.0, 0.0, 1.0], [1.0, 0.0, 1.0]])
    undo_vander = np.array([[0.0, -0.5, 0.5], [1.0, 0.0, -1.0], [0.0, 0.5, 0.5]])
    moment_matrix = np.kron(vander, np.kron(vander, vander))
    inverse = np.kron(undo_vander, np.kron(undo_vander, undo_vander))
    forward = jnp.asarray(moment_matrix * weights[None, :], dtype=jnp.float32)
    backward = jnp.asarray(inverse / weights[:, None], dtype=jnp.float32)
    return (forward, backward, speeds)


def mode_basis_at(mode_ids, positions, length):
    phase_ids = positions[:, None] * mode_ids[None, :] % length
    angles = phase_ids.astype(jnp.float32) * (TWO_PI / length)
    return jnp.concatenate([jnp.cos(angles), jnp.sin(angles)], axis=1)


def collide_blocks(moments, velocity, nudge, backward, relaxation_frequencies):
    density = moments[0]
    shifted = velocity + nudge
    powers = jnp.stack([jnp.ones_like(shifted), shifted, shifted * shifted + 1.0 / 3.0], axis=0)
    equilibrium = (
        density[None, None, None]
        * powers[:, None, None, 0]
        * powers[None, :, None, 1]
        * powers[None, None, :, 2]
    )
    equilibrium = equilibrium.reshape(moments.shape)
    relaxed = moments - relaxation_frequencies[:, None, None, None] * (moments - equilibrium)
    return jnp.einsum("ij,jzpl->izpl", backward, relaxed, precision=HIGHEST)


def moments_kernel(keys_ref, forward_ref, state_ref, out_ref, wind_ref, scratch_ref):
    levels, blocks, channels, cells = out_ref.shape
    seats = scratch_ref.shape[0]
    chunks = levels * cells // 128
    forward = forward_ref[...]
    for seat_number in range(seats):
        pieces = [
            state_ref[pl.ds(seat_number * channels * chunks + chunk, channels, stride=chunks), :]
            for chunk in range(chunks)
        ]
        scratch_ref[seat_number] = jnp.dot(
            forward, jnp.concatenate(pieces, axis=1), precision=HIGHEST,
            preferred_element_type=jnp.float32,
        )
    for block in range(blocks):
        slot = 0
        found = False
        for seat_number in range(seats):
            hit = keys_ref[seat_number] == block
            slot = jnp.where(hit, seat_number, slot)
            found = jnp.logical_or(found, hit)
        keep = jnp.where(found, 1.0, 0.0)
        for level in range(levels):
            values = scratch_ref[slot, :, level * cells:(level + 1) * cells] * keep
            out_ref[level, block] = values
            density = jnp.where(found, values[0:1], 1.0)
            for component, row in enumerate((9, 3, 1)):
                wind_ref[component, level, block:block + 1, :] = values[row:row + 1] / density


def cell_moments(keys, forward, rows, seats, levels):
    channels = forward.shape[0]
    blocks = TX * TY
    cells = rows.size // (seats * channels * levels)
    vmem = pl.BlockSpec(memory_space=pltpu.VMEM)
    smem = pl.BlockSpec(memory_space=pltpu.SMEM)
    return pl.pallas_call(
        moments_kernel,
        out_shape=(
            jax.ShapeDtypeStruct((levels, blocks, channels, cells), jnp.float32),
            jax.ShapeDtypeStruct((3, levels, blocks, cells), jnp.float32),
        ),
        in_specs=[smem, vmem, vmem],
        out_specs=(vmem, vmem),
        scratch_shapes=[pltpu.VMEM((seats, channels, levels * cells), jnp.float32)],
    )(keys, forward, rows)


def stream_kernel(
    keys_ref, post_ref, below_ref, above_ref, left_ref, right_ref, out_ref, spread_ref, result_ref
):
    levels, blocks, channels, cells = post_ref.shape
    _, _, speeds = lattice_tables()
    front = 8
    grid_row = lax.broadcasted_iota(jnp.int32, (BE, cells), 0)
    grid_lane = lax.broadcasted_iota(jnp.int32, (BE, cells), 1)
    tile_copy = (grid_lane % BE == grid_row).astype(jnp.float32)
    group_copy = (grid_lane // BE == grid_row).astype(jnp.float32)
    halo_rows = below_ref.shape[0]
    for slot, (source, copier) in enumerate(
        ((below_ref, tile_copy), (above_ref, tile_copy), (left_ref, group_copy), (right_ref, group_copy))
    ):
        spread_ref[slot, front:front + halo_rows, :] = jnp.dot(
            source[...], copier, precision=HIGHEST, preferred_element_type=jnp.float32
        )
    lane = lax.broadcasted_iota(jnp.int32, (blocks, cells), 1)
    seat = lax.broadcasted_iota(jnp.int32, (blocks, cells), 0)
    q = lane % BE
    r = lane // BE
    py = seat // TX

    solid_plane = jnp.zeros((blocks, cells), jnp.float32)
    for block in range(blocks):
        found = False
        for seat_number in range(keys_ref.shape[0]):
            found = jnp.logical_or(found, keys_ref[seat_number] == block)
        solid_plane = jnp.where(seat == block, jnp.where(found, 0.0, 1.0), solid_plane)

    def own(channel, level):
        if channel == channels:
            return solid_plane
        return post_ref[level, :, channel, :]

    def moved(plane, shift):
        shift = shift % cells
        if shift == 0:
            return plane
        return pltpu.roll(plane, shift, 1)

    def gathered(channel, level, cx, cy):
        shift = cy * BE + cx
        first = front + (channel * levels + level) * (TY + 2)
        base = own(channel, level)
        if cy != 0:
            stepped = pltpu.roll(base, TX, 0)
            if cy == 1:
                halo = spread_ref[0, first:first + blocks, :]
                yplane = jnp.where(py == 0, halo, stepped)
            else:
                halo = spread_ref[1, first - TX:first - TX + blocks, :]
                yplane = jnp.where(py == TY - 1, halo, stepped)

        def sideways(plane, dy, dx):
            plane = pltpu.roll(plane, dx % blocks, 0)
            edge = 0 if dx == 1 else TX - 1
            side = 2 if dx == 1 else 3
            at = first + 1 - dy
            return jnp.where(
                seat == edge,
                spread_ref[side, at:at + 1, :],
                jnp.where(seat == edge + TX, spread_ref[side, at + 1:at + 2, :], plane),
            )

        value = moved(base, shift)
        if cy != 0:
            ycross = r == (0 if cy == 1 else BE - 1)
            value = jnp.where(ycross, moved(yplane, shift), value)
        if cx != 0:
            xcross = q == (0 if cx == 1 else BE - 1)
            xvalue = moved(sideways(base, 0, cx), shift - BE * cx)
            if cy != 0:
                xvalue = jnp.where(ycross, moved(sideways(yplane, cy, cx), shift - BE * cx), xvalue)
            value = jnp.where(xcross, xvalue, value)
        return value

    blocked_of = {}
    for cx in (-1, 0, 1):
        for cy in (-1, 0, 1):
            blocked_of[(cx, cy)] = gathered(channels, 0, cx, cy) > 0.5
    for heading in range(27):
        cx, cy, cz = (int(v) for v in speeds[heading])
        blocked = blocked_of[(cx, cy)]
        for level in range(levels):
            bounced = post_ref[level, :, 26 - heading, :]
            window = pl.ds(level * cells, cells)
            if cz == 1 and level == 0:
                result_ref[:, heading, window] = bounced
                continue
            if cz == 0:
                source = gathered(heading, level, cx, cy)
            elif cz == 1:
                source = gathered(heading, 0, cx, cy)
            elif level == 0:
                source = gathered(heading, 1, cx, cy)
            else:
                source = gathered(heading + 2, 1, cx, cy)
            result_ref[:, heading, window] = jnp.where(blocked, bounced, source)
    chunks = levels * cells // 128
    for seat_number in range(keys_ref.shape[0]):
        key = keys_ref[seat_number]
        for chunk in range(chunks):
            picked = result_ref[jnp.maximum(key, 0), :, chunk * 128:(chunk + 1) * 128]
            rows = pl.ds(seat_number * channels * chunks + chunk, channels, stride=chunks)
            out_ref[rows, :] = jnp.where(key >= 0, picked, 0.0)


def stream(keys, post, below, above, from_left, from_right):
    channels, levels, blocks, cells = post.shape
    seats = keys.shape[0]
    halo_rows = below.shape[0]
    vmem = pl.BlockSpec(memory_space=pltpu.VMEM)
    smem = pl.BlockSpec(memory_space=pltpu.SMEM)
    return pl.pallas_call(
        stream_kernel,
        out_shape=jax.ShapeDtypeStruct((seats * channels * levels * cells // 128, 128), jnp.float32),
        in_specs=[smem] + [vmem] * 5,
        out_specs=vmem,
        scratch_shapes=[
            pltpu.VMEM((4, halo_rows + 16, cells), jnp.float32),
            pltpu.VMEM((blocks, channels, levels * cells), jnp.float32),
        ],
    )(keys, post.transpose(1, 2, 0, 3), below, above, from_left, from_right)


def on_device(
    scaled_distributions,
    remaining_brick_places,
    retained_wavenumbers,
    regional_amplitudes,
    relaxation_frequencies,
):
    forward, backward, speeds = lattice_tables()
    slot_state = scaled_distributions[0, 0]
    living_brick_keys = remaining_brick_places[0, 0]
    seats = living_brick_keys.shape[0]
    channels = slot_state.shape[1]
    cells = BE * BE
    levels = slot_state.shape[2] // cells
    blocks = TX * TY
    rows_tile = TY * BE
    cols_tile = TX * BE
    rows = slot_state.reshape(-1, 128)
    moments, wind = cell_moments(living_brick_keys, forward, rows, seats, levels)
    moments = moments.transpose(2, 0, 1, 3)
    line_length = lax.axis_size("line") * cols_tile
    own_columns = lax.axis_index("line") * cols_tile + jnp.arange(cols_tile, dtype=jnp.int32)
    mode_basis = mode_basis_at(retained_wavenumbers, own_columns, line_length).reshape(TX, BE, -1)
    partial = jnp.einsum(
        "kzyxrq,xqm->kzyrm", wind.reshape(3, levels, TY, TX, BE, BE), mode_basis,
        precision=HIGHEST,
    ).reshape(3, levels, rows_tile, -1)
    coefficients = butterfly_sum(partial, "line")
    misfit = regional_amplitudes - 2.0 / line_length * coefficients
    nudge = NUDGE_GAIN * jnp.einsum(
        "kzyrm,xqm->kzyxrq", misfit.reshape(3, levels, TY, BE, -1), mode_basis,
        precision=HIGHEST,
    ).reshape(3, levels, blocks, cells)
    post = collide_blocks(moments, wind, nudge, backward, relaxation_frequencies)
    present = jnp.any(living_brick_keys[None, :] == jnp.arange(blocks, dtype=jnp.int32)[:, None], axis=1)
    fluid = present.astype(jnp.float32)
    solid = jnp.broadcast_to((1.0 - fluid)[None, None, :, None], (1, levels, blocks, cells))
    extended = jnp.concatenate([post, solid], axis=0)
    width = channels + 1
    ahead, behind = ring_pairs("curve")
    flat = lambda halo: halo.reshape(-1, BE)
    halo_shape = (width, levels, TX, BE)
    top_row = extended[:, :, blocks - TX:, cells - BE:]
    bottom_row = extended[:, :, :TX, :BE]
    below_flat = lax.ppermute(flat(top_row), "curve", ahead)
    above_flat = lax.ppermute(flat(bottom_row), "curve", behind)
    below = below_flat.reshape(halo_shape)
    above = above_flat.reshape(halo_shape)
    ahead, behind = ring_pairs("line")
    by_rows = extended.reshape(width, levels, TY, TX, BE, BE)
    right_cols = by_rows[:, :, :, TX - 1, :, BE - 1]
    left_cols = by_rows[:, :, :, 0, :, 0]
    to_right = jnp.concatenate(
        [
            jnp.broadcast_to(below[:, :, TX - 1:, BE - 1:], (width, levels, 1, BE)),
            right_cols,
            jnp.broadcast_to(above[:, :, TX - 1:, BE - 1:], (width, levels, 1, BE)),
        ],
        axis=2,
    )
    to_left = jnp.concatenate(
        [
            jnp.broadcast_to(below[:, :, :1, :1], (width, levels, 1, BE)),
            left_cols,
            jnp.broadcast_to(above[:, :, :1, :1], (width, levels, 1, BE)),
        ],
        axis=2,
    )
    from_left = lax.ppermute(flat(to_right), "line", ahead)
    from_right = lax.ppermute(flat(to_left), "line", behind)
    new_state = stream(living_brick_keys, post, below_flat, above_flat, from_left, from_right)
    return new_state.reshape((1, 1, seats, channels, levels * cells))


def solution(mesh):
    return jax.shard_map(
        on_device,
        mesh=mesh,
        in_specs=(
            P("curve", "line", None, None, None),
            P("curve", "line", None),
            P(),
            P(None, None, "curve", None),
            P(),
        ),
        out_specs=P("curve", "line", None, None, None),
        check_vma=False,
    )
```

```python
import jax
import jax.numpy as jnp
import numpy as np
from jax import lax
from jax.experimental import pallas as pl
from jax.experimental.pallas import tpu as pltpu
from jax.sharding import PartitionSpec as P

BE = 16
TX = 4
TY = 2


NUDGE_GAIN = 0.5
TWO_PI = 6.283185307179586
HIGHEST = lax.Precision.HIGHEST


def butterfly_sum(value, axis):
    count = lax.axis_size(axis)
    stride = count // 2
    while stride >= 1:
        value = value + lax.ppermute(value, axis, [(i, i ^ stride) for i in range(count)])
        stride //= 2
    return value


def ring_pairs(axis):
    count = lax.axis_size(axis)
    forward = [(i, (i + 1) % count) for i in range(count)]
    backward = [(target, source) for source, target in forward]
    return forward, backward


def lattice_tables():
    one_weights = np.array([1.0 / 6.0, 2.0 / 3.0, 1.0 / 6.0])
    speeds = np.array(
        [
            [along_x - 1, along_y - 1, along_z - 1]
            for along_x in range(3)
            for along_y in range(3)
            for along_z in range(3)
        ]
    )
    weights = np.array(
        [
            one_weights[along_x] * one_weights[along_y] * one_weights[along_z]
            for along_x in range(3)
            for along_y in range(3)
            for along_z in range(3)
        ]
    )
    vander = np.array([[1.0, 1.0, 1.0], [-1.0, 0.0, 1.0], [1.0, 0.0, 1.0]])
    undo_vander = np.array([[0.0, -0.5, 0.5], [1.0, 0.0, -1.0], [0.0, 0.5, 0.5]])
    moment_matrix = np.kron(vander, np.kron(vander, vander))
    inverse = np.kron(undo_vander, np.kron(undo_vander, undo_vander))
    forward = jnp.asarray(moment_matrix * weights[None, :], dtype=jnp.float32)
    backward = jnp.asarray(inverse / weights[:, None], dtype=jnp.float32)
    return (forward, backward, speeds)


def mode_basis_at(mode_ids, positions, length):
    phase_ids = positions[:, None] * mode_ids[None, :] % length
    angles = phase_ids.astype(jnp.float32) * (TWO_PI / length)
    return jnp.concatenate([jnp.cos(angles), jnp.sin(angles)], axis=1)


def collide_blocks(moments, velocity, nudge, backward, relaxation_frequencies):
    density = moments[0]
    shifted = velocity + nudge
    powers = jnp.stack([jnp.ones_like(shifted), shifted, shifted * shifted + 1.0 / 3.0], axis=0)
    equilibrium = (
        density[None, None, None]
        * powers[:, None, None, 0]
        * powers[None, :, None, 1]
        * powers[None, None, :, 2]
    )
    equilibrium = equilibrium.reshape(moments.shape)
    relaxed = moments - relaxation_frequencies[:, None, None, None] * (moments - equilibrium)
    return jnp.einsum("ij,jzpl->izpl", backward, relaxed, precision=HIGHEST)


def moments_kernel(keys_ref, forward_ref, state_ref, out_ref, wind_ref, scratch_ref):
    levels, blocks, channels, cells = out_ref.shape
    seats = scratch_ref.shape[0]
    chunks = levels * cells // 128
    forward = forward_ref[...]
    for seat_number in range(seats):
        pieces = [
            state_ref[pl.ds(seat_number * channels * chunks + chunk, channels, stride=chunks), :]
            for chunk in range(chunks)
        ]
        scratch_ref[seat_number] = jnp.dot(
            forward, jnp.concatenate(pieces, axis=1), precision=HIGHEST,
            preferred_element_type=jnp.float32,
        )
    for block in range(blocks):
        slot = 0
        found = False
        for seat_number in range(seats):
            hit = keys_ref[seat_number] == block
            slot = jnp.where(hit, seat_number, slot)
            found = jnp.logical_or(found, hit)
        keep = jnp.where(found, 1.0, 0.0)
        for level in range(levels):
            values = scratch_ref[slot, :, level * cells:(level + 1) * cells] * keep
            out_ref[level, block] = values
            density = jnp.where(found, values[0:1], 1.0)
            for component, row in enumerate((9, 3, 1)):
                wind_ref[component, level, block:block + 1, :] = values[row:row + 1] / density


def cell_moments(keys, forward, rows, seats, levels):
    channels = forward.shape[0]
    blocks = TX * TY
    cells = rows.size // (seats * channels * levels)
    vmem = pl.BlockSpec(memory_space=pltpu.VMEM)
    smem = pl.BlockSpec(memory_space=pltpu.SMEM)
    return pl.pallas_call(
        moments_kernel,
        out_shape=(
            jax.ShapeDtypeStruct((levels, blocks, channels, cells), jnp.float32),
            jax.ShapeDtypeStruct((3, levels, blocks, cells), jnp.float32),
        ),
        in_specs=[smem, vmem, vmem],
        out_specs=(vmem, vmem),
        scratch_shapes=[pltpu.VMEM((seats, channels, levels * cells), jnp.float32)],
    )(keys, forward, rows)


def stream_kernel(
    keys_ref, post_ref, below_ref, above_ref, left_ref, right_ref, out_ref, spread_ref, result_ref
):
    levels, blocks, channels, cells = post_ref.shape
    _, _, speeds = lattice_tables()
    front = 8
    grid_row = lax.broadcasted_iota(jnp.int32, (BE, cells), 0)
    grid_lane = lax.broadcasted_iota(jnp.int32, (BE, cells), 1)
    tile_copy = (grid_lane % BE == grid_row).astype(jnp.float32)
    group_copy = (grid_lane // BE == grid_row).astype(jnp.float32)
    halo_rows = below_ref.shape[0]
    for slot, (source, copier) in enumerate(
        ((below_ref, tile_copy), (above_ref, tile_copy), (left_ref, group_copy), (right_ref, group_copy))
    ):
        spread_ref[slot, front:front + halo_rows, :] = jnp.dot(
            source[...], copier, precision=HIGHEST, preferred_element_type=jnp.float32
        )
    lane = lax.broadcasted_iota(jnp.int32, (blocks, cells), 1)
    seat = lax.broadcasted_iota(jnp.int32, (blocks, cells), 0)
    q = lane % BE
    r = lane // BE
    py = seat // TX

    solid_plane = jnp.zeros((blocks, cells), jnp.float32)
    for block in range(blocks):
        found = False
        for seat_number in range(keys_ref.shape[0]):
            found = jnp.logical_or(found, keys_ref[seat_number] == block)
        solid_plane = jnp.where(seat == block, jnp.where(found, 0.0, 1.0), solid_plane)

    def own(channel, level):
        if channel == channels:
            return solid_plane
        return post_ref[level, :, channel, :]

    def moved(plane, shift):
        shift = shift % cells
        if shift == 0:
            return plane
        return pltpu.roll(plane, shift, 1)

    def gathered(channel, level, cx, cy):
        shift = cy * BE + cx
        first = front + (channel * levels + level) * (TY + 2)
        base = own(channel, level)
        if cy != 0:
            stepped = pltpu.roll(base, TX, 0)
            if cy == 1:
                halo = spread_ref[0, first:first + blocks, :]
                yplane = jnp.where(py == 0, halo, stepped)
            else:
                halo = spread_ref[1, first - TX:first - TX + blocks, :]
                yplane = jnp.where(py == TY - 1, halo, stepped)

        def sideways(plane, dy, dx):
            plane = pltpu.roll(plane, dx % blocks, 0)
            edge = 0 if dx == 1 else TX - 1
            side = 2 if dx == 1 else 3
            at = first + 1 - dy
            return jnp.where(
                seat == edge,
                spread_ref[side, at:at + 1, :],
                jnp.where(seat == edge + TX, spread_ref[side, at + 1:at + 2, :], plane),
            )

        value = moved(base, shift)
        if cy != 0:
            ycross = r == (0 if cy == 1 else BE - 1)
            value = jnp.where(ycross, moved(yplane, shift), value)
        if cx != 0:
            xcross = q == (0 if cx == 1 else BE - 1)
            xvalue = moved(sideways(base, 0, cx), shift - BE * cx)
            if cy != 0:
                xvalue = jnp.where(ycross, moved(sideways(yplane, cy, cx), shift - BE * cx), xvalue)
            value = jnp.where(xcross, xvalue, value)
        return value

    blocked_of = {}
    for cx in (-1, 0, 1):
        for cy in (-1, 0, 1):
            blocked_of[(cx, cy)] = gathered(channels, 0, cx, cy) > 0.5
    for heading in range(27):
        cx, cy, cz = (int(v) for v in speeds[heading])
        blocked = blocked_of[(cx, cy)]
        for level in range(levels):
            bounced = post_ref[level, :, 26 - heading, :]
            window = pl.ds(level * cells, cells)
            if cz == 1 and level == 0:
                result_ref[:, heading, window] = bounced
                continue
            if cz == 0:
                source = gathered(heading, level, cx, cy)
            elif cz == 1:
                source = gathered(heading, 0, cx, cy)
            elif level == 0:
                source = gathered(heading, 1, cx, cy)
            else:
                source = gathered(heading + 2, 1, cx, cy)
            result_ref[:, heading, window] = jnp.where(blocked, bounced, source)
    chunks = levels * cells // 128
    for seat_number in range(keys_ref.shape[0]):
        key = keys_ref[seat_number]
        for chunk in range(chunks):
            picked = result_ref[jnp.maximum(key, 0), :, chunk * 128:(chunk + 1) * 128]
            rows = pl.ds(seat_number * channels * chunks + chunk, channels, stride=chunks)
            out_ref[rows, :] = jnp.where(key >= 0, picked, 0.0)


def stream(keys, post, below, above, from_left, from_right):
    channels, levels, blocks, cells = post.shape
    seats = keys.shape[0]
    halo_rows = below.shape[0]
    vmem = pl.BlockSpec(memory_space=pltpu.VMEM)
    smem = pl.BlockSpec(memory_space=pltpu.SMEM)
    return pl.pallas_call(
        stream_kernel,
        out_shape=jax.ShapeDtypeStruct((seats * channels * levels * cells // 128, 128), jnp.float32),
        in_specs=[smem] + [vmem] * 5,
        out_specs=vmem,
        scratch_shapes=[
            pltpu.VMEM((4, halo_rows + 16, cells), jnp.float32),
            pltpu.VMEM((blocks, channels, levels * cells), jnp.float32),
        ],
    )(keys, post.transpose(1, 2, 0, 3), below, above, from_left, from_right)


def on_device(
    scaled_distributions,
    remaining_brick_places,
    retained_wavenumbers,
    regional_amplitudes,
    relaxation_frequencies,
):
    forward, backward, speeds = lattice_tables()
    slot_state = scaled_distributions[0, 0]
    living_brick_keys = remaining_brick_places[0, 0]
    seats = living_brick_keys.shape[0]
    channels = slot_state.shape[1]
    cells = BE * BE
    levels = slot_state.shape[2] // cells
    blocks = TX * TY
    rows_tile = TY * BE
    cols_tile = TX * BE
    rows = slot_state.reshape(-1, 128)
    moments, wind = cell_moments(living_brick_keys, forward, rows, seats, levels)
    moments = moments.transpose(2, 0, 1, 3)
    line_length = lax.axis_size("line") * cols_tile
    own_columns = lax.axis_index("line") * cols_tile + jnp.arange(cols_tile, dtype=jnp.int32)
    mode_basis = mode_basis_at(retained_wavenumbers, own_columns, line_length).reshape(TX, BE, -1)
    partial = jnp.einsum(
        "kzyxrq,xqm->kzyrm", wind.reshape(3, levels, TY, TX, BE, BE), mode_basis,
        precision=HIGHEST,
    ).reshape(3, levels, rows_tile, -1)
    coefficients = butterfly_sum(partial, "line")
    misfit = regional_amplitudes - 2.0 / line_length * coefficients
    nudge = NUDGE_GAIN * jnp.einsum(
        "kzyrm,xqm->kzyxrq", misfit.reshape(3, levels, TY, BE, -1), mode_basis,
        precision=HIGHEST,
    ).reshape(3, levels, blocks, cells)
    post = collide_blocks(moments, wind, nudge, backward, relaxation_frequencies)
    present = jnp.any(living_brick_keys[None, :] == jnp.arange(blocks, dtype=jnp.int32)[:, None], axis=1)
    fluid = present.astype(jnp.float32)
    solid = jnp.broadcast_to((1.0 - fluid)[None, None, :, None], (1, levels, blocks, cells))
    extended = jnp.concatenate([post, solid], axis=0)
    width = channels + 1
    ahead, behind = ring_pairs("curve")
    flat = lambda halo: halo.reshape(-1, BE)
    halo_shape = (width, levels, TX, BE)
    top_row = extended[:, :, blocks - TX:, cells - BE:]
    bottom_row = extended[:, :, :TX, :BE]
    below_flat = lax.ppermute(flat(top_row), "curve", ahead)
    above_flat = lax.ppermute(flat(bottom_row), "curve", behind)
    below = below_flat.reshape(halo_shape)
    above = above_flat.reshape(halo_shape)
    ahead, behind = ring_pairs("line")
    by_rows = extended.reshape(width, levels, TY, TX, BE, BE)
    right_cols = by_rows[:, :, :, TX - 1, :, BE - 1]
    left_cols = by_rows[:, :, :, 0, :, 0]
    to_right = jnp.concatenate(
        [
            jnp.broadcast_to(below[:, :, TX - 1:, BE - 1:], (width, levels, 1, BE)),
            right_cols,
            jnp.broadcast_to(above[:, :, TX - 1:, BE - 1:], (width, levels, 1, BE)),
        ],
        axis=2,
    )
    to_left = jnp.concatenate(
        [
            jnp.broadcast_to(below[:, :, :1, :1], (width, levels, 1, BE)),
            left_cols,
            jnp.broadcast_to(above[:, :, :1, :1], (width, levels, 1, BE)),
        ],
        axis=2,
    )
    from_left = lax.ppermute(flat(to_right), "line", ahead)
    from_right = lax.ppermute(flat(to_left), "line", behind)
    new_state = stream(living_brick_keys, post, below_flat, above_flat, from_left, from_right)
    return new_state.reshape((1, 1, seats, channels, levels * cells))


def solution(mesh):
    return jax.shard_map(
        on_device,
        mesh=mesh,
        in_specs=(
            P("curve", "line", None, None, None),
            P("curve", "line", None),
            P(),
            P(None, None, "curve", None),
            P(),
        ),
        out_specs=P("curve", "line", None, None, None),
        check_vma=False,
    )
```

```python
import jax
import jax.numpy as jnp
import numpy as np
from jax import lax
from jax.experimental import pallas as pl
from jax.experimental.pallas import tpu as pltpu
from jax.sharding import PartitionSpec as P

BE = 16
TX = 4
TY = 2


NUDGE_GAIN = 0.5
TWO_PI = 6.283185307179586
HIGHEST = lax.Precision.HIGHEST


def butterfly_sum(value, axis):
    count = lax.axis_size(axis)
    stride = 1
    while stride < count:
        value = value + lax.ppermute(value, axis, [(i, i ^ stride) for i in range(count)])
        stride *= 2
    return value


def ring_pairs(axis):
    count = lax.axis_size(axis)
    forward = [(i, (i + 1) % count) for i in range(count)]
    backward = [(target, source) for source, target in forward]
    return forward, backward


def lattice_tables():
    one_weights = np.array([1.0 / 6.0, 2.0 / 3.0, 1.0 / 6.0])
    speeds = np.array(
        [
            [along_x - 1, along_y - 1, along_z - 1]
            for along_x in range(3)
            for along_y in range(3)
            for along_z in range(3)
        ]
    )
    weights = np.array(
        [
            one_weights[along_x] * one_weights[along_y] * one_weights[along_z]
            for along_x in range(3)
            for along_y in range(3)
            for along_z in range(3)
        ]
    )
    vander = np.array([[1.0, 1.0, 1.0], [-1.0, 0.0, 1.0], [1.0, 0.0, 1.0]])
    undo_vander = np.array([[0.0, -0.5, 0.5], [1.0, 0.0, -1.0], [0.0, 0.5, 0.5]])
    moment_matrix = np.kron(vander, np.kron(vander, vander))
    inverse = np.kron(undo_vander, np.kron(undo_vander, undo_vander))
    forward = jnp.asarray(moment_matrix * weights[None, :], dtype=jnp.float32)
    backward = jnp.asarray(inverse / weights[:, None], dtype=jnp.float32)
    return (forward, backward, speeds)


def mode_basis_at(mode_ids, positions, length):
    phase_ids = positions[:, None] * mode_ids[None, :] % length
    angles = phase_ids.astype(jnp.float32) * (TWO_PI / length)
    return jnp.concatenate([jnp.cos(angles), jnp.sin(angles)], axis=1)


def collide_blocks(moments, velocity, nudge, backward, relaxation_frequencies):
    density = moments[0]
    shifted = velocity + nudge
    powers = jnp.stack([jnp.ones_like(shifted), shifted, shifted * shifted + 1.0 / 3.0], axis=0)
    equilibrium = (
        density[None, None, None]
        * powers[:, None, None, 0]
        * powers[None, :, None, 1]
        * powers[None, None, :, 2]
    )
    equilibrium = equilibrium.reshape(moments.shape)
    relaxed = moments - relaxation_frequencies[:, None, None, None] * (moments - equilibrium)
    return jnp.einsum("ij,jzpl->izpl", backward, relaxed, precision=HIGHEST)


def moments_kernel(keys_ref, forward_ref, state_ref, out_ref, wind_ref, scratch_ref):
    levels, blocks, channels, cells = out_ref.shape
    seats = scratch_ref.shape[0]
    chunks = levels * cells // 128
    forward = forward_ref[...]
    for seat_number in range(seats):
        pieces = [
            state_ref[pl.ds(seat_number * channels * chunks + chunk, channels, stride=chunks), :]
            for chunk in range(chunks)
        ]
        scratch_ref[seat_number] = jnp.dot(
            forward, jnp.concatenate(pieces, axis=1), precision=HIGHEST,
            preferred_element_type=jnp.float32,
        )
    for block in range(blocks):
        slot = 0
        found = False
        for seat_number in range(seats):
            hit = keys_ref[seat_number] == block
            slot = jnp.where(hit, seat_number, slot)
            found = jnp.logical_or(found, hit)
        keep = jnp.where(found, 1.0, 0.0)
        for level in range(levels):
            values = scratch_ref[slot, :, level * cells:(level + 1) * cells] * keep
            out_ref[level, block] = values
            density = jnp.where(found, values[0:1], 1.0)
            for component, row in enumerate((9, 3, 1)):
                wind_ref[component, level, block:block + 1, :] = values[row:row + 1] / density


def cell_moments(keys, forward, rows, seats, levels):
    channels = forward.shape[0]
    blocks = TX * TY
    cells = rows.size // (seats * channels * levels)
    vmem = pl.BlockSpec(memory_space=pltpu.VMEM)
    smem = pl.BlockSpec(memory_space=pltpu.SMEM)
    return pl.pallas_call(
        moments_kernel,
        out_shape=(
            jax.ShapeDtypeStruct((levels, blocks, channels, cells), jnp.float32),
            jax.ShapeDtypeStruct((3, levels, blocks, cells), jnp.float32),
        ),
        in_specs=[smem, vmem, vmem],
        out_specs=(vmem, vmem),
        scratch_shapes=[pltpu.VMEM((seats, channels, levels * cells), jnp.float32)],
    )(keys, forward, rows)


def stream_kernel(
    keys_ref, post_ref, below_ref, above_ref, left_ref, right_ref, out_ref, spread_ref, result_ref
):
    levels, blocks, channels, cells = post_ref.shape
    _, _, speeds = lattice_tables()
    front = 8
    grid_row = lax.broadcasted_iota(jnp.int32, (BE, cells), 0)
    grid_lane = lax.broadcasted_iota(jnp.int32, (BE, cells), 1)
    tile_copy = (grid_lane % BE == grid_row).astype(jnp.float32)
    group_copy = (grid_lane // BE == grid_row).astype(jnp.float32)
    halo_rows = below_ref.shape[0]
    for slot, (source, copier) in enumerate(
        ((below_ref, tile_copy), (above_ref, tile_copy), (left_ref, group_copy), (right_ref, group_copy))
    ):
        spread_ref[slot, front:front + halo_rows, :] = jnp.dot(
            source[...], copier, precision=HIGHEST, preferred_element_type=jnp.float32
        )
    lane = lax.broadcasted_iota(jnp.int32, (blocks, cells), 1)
    seat = lax.broadcasted_iota(jnp.int32, (blocks, cells), 0)
    q = lane % BE
    r = lane // BE
    py = seat // TX

    solid_plane = jnp.zeros((blocks, cells), jnp.float32)
    for block in range(blocks):
        found = False
        for seat_number in range(keys_ref.shape[0]):
            found = jnp.logical_or(found, keys_ref[seat_number] == block)
        solid_plane = jnp.where(seat == block, jnp.where(found, 0.0, 1.0), solid_plane)

    def own(channel, level):
        if channel == channels:
            return solid_plane
        return post_ref[level, :, channel, :]

    def moved(plane, shift):
        shift = shift % cells
        if shift == 0:
            return plane
        return pltpu.roll(plane, shift, 1)

    def gathered(channel, level, cx, cy):
        shift = cy * BE + cx
        first = front + (channel * levels + level) * (TY + 2)
        base = own(channel, level)
        if cy != 0:
            stepped = pltpu.roll(base, TX, 0)
            if cy == 1:
                halo = spread_ref[0, first:first + blocks, :]
                yplane = jnp.where(py == 0, halo, stepped)
            else:
                halo = spread_ref[1, first - TX:first - TX + blocks, :]
                yplane = jnp.where(py == TY - 1, halo, stepped)

        def sideways(plane, dy, dx):
            plane = pltpu.roll(plane, dx % blocks, 0)
            edge = 0 if dx == 1 else TX - 1
            side = 2 if dx == 1 else 3
            at = first + 1 - dy
            return jnp.where(
                seat == edge,
                spread_ref[side, at:at + 1, :],
                jnp.where(seat == edge + TX, spread_ref[side, at + 1:at + 2, :], plane),
            )

        value = moved(base, shift)
        if cy != 0:
            ycross = r == (0 if cy == 1 else BE - 1)
            value = jnp.where(ycross, moved(yplane, shift), value)
        if cx != 0:
            xcross = q == (0 if cx == 1 else BE - 1)
            xvalue = moved(sideways(base, 0, cx), shift - BE * cx)
            if cy != 0:
                xvalue = jnp.where(ycross, moved(sideways(yplane, cy, cx), shift - BE * cx), xvalue)
            value = jnp.where(xcross, xvalue, value)
        return value

    blocked_of = {}
    for cx in (-1, 0, 1):
        for cy in (-1, 0, 1):
            blocked_of[(cx, cy)] = gathered(channels, 0, cx, cy) > 0.5
    for heading in range(27):
        cx, cy, cz = (int(v) for v in speeds[heading])
        blocked = blocked_of[(cx, cy)]
        for level in range(levels):
            bounced = post_ref[level, :, 26 - heading, :]
            window = pl.ds(level * cells, cells)
            if cz == 1 and level == 0:
                result_ref[:, heading, window] = bounced
                continue
            if cz == 0:
                source = gathered(heading, level, cx, cy)
            elif cz == 1:
                source = gathered(heading, 0, cx, cy)
            elif level == 0:
                source = gathered(heading, 1, cx, cy)
            else:
                source = gathered(heading + 2, 1, cx, cy)
            result_ref[:, heading, window] = jnp.where(blocked, bounced, source)
    chunks = levels * cells // 128
    for seat_number in range(keys_ref.shape[0]):
        key = keys_ref[seat_number]
        for chunk in range(chunks):
            picked = result_ref[jnp.maximum(key, 0), :, chunk * 128:(chunk + 1) * 128]
            rows = pl.ds(seat_number * channels * chunks + chunk, channels, stride=chunks)
            out_ref[rows, :] = jnp.where(key >= 0, picked, 0.0)


def stream(keys, post, below, above, from_left, from_right):
    channels, levels, blocks, cells = post.shape
    seats = keys.shape[0]
    halo_rows = below.shape[0]
    vmem = pl.BlockSpec(memory_space=pltpu.VMEM)
    smem = pl.BlockSpec(memory_space=pltpu.SMEM)
    return pl.pallas_call(
        stream_kernel,
        out_shape=jax.ShapeDtypeStruct((seats * channels * levels * cells // 128, 128), jnp.float32),
        in_specs=[smem] + [vmem] * 5,
        out_specs=vmem,
        scratch_shapes=[
            pltpu.VMEM((4, halo_rows + 16, cells), jnp.float32),
            pltpu.VMEM((blocks, channels, levels * cells), jnp.float32),
        ],
    )(keys, post.transpose(1, 2, 0, 3), below, above, from_left, from_right)


def on_device(
    scaled_distributions,
    remaining_brick_places,
    retained_wavenumbers,
    regional_amplitudes,
    relaxation_frequencies,
):
    forward, backward, speeds = lattice_tables()
    slot_state = scaled_distributions[0, 0]
    living_brick_keys = remaining_brick_places[0, 0]
    seats = living_brick_keys.shape[0]
    channels = slot_state.shape[1]
    cells = BE * BE
    levels = slot_state.shape[2] // cells
    blocks = TX * TY
    rows_tile = TY * BE
    cols_tile = TX * BE
    rows = slot_state.reshape(-1, 128)
    moments, wind = cell_moments(living_brick_keys, forward, rows, seats, levels)
    moments = moments.transpose(2, 0, 1, 3)
    line_length = lax.axis_size("line") * cols_tile
    own_columns = lax.axis_index("line") * cols_tile + jnp.arange(cols_tile, dtype=jnp.int32)
    mode_basis = mode_basis_at(retained_wavenumbers, own_columns, line_length).reshape(TX, BE, -1)
    partial = jnp.einsum(
        "kzyxrq,xqm->kzyrm", wind.reshape(3, levels, TY, TX, BE, BE), mode_basis,
        precision=HIGHEST,
    ).reshape(3, levels, rows_tile, -1)
    coefficients = butterfly_sum(partial, "line")
    misfit = regional_amplitudes - 2.0 / line_length * coefficients
    nudge = NUDGE_GAIN * jnp.einsum(
        "kzyrm,xqm->kzyxrq", misfit.reshape(3, levels, TY, BE, -1), mode_basis,
        precision=HIGHEST,
    ).reshape(3, levels, blocks, cells)
    post = collide_blocks(moments, wind, nudge, backward, relaxation_frequencies)
    present = jnp.any(living_brick_keys[None, :] == jnp.arange(blocks, dtype=jnp.int32)[:, None], axis=1)
    fluid = present.astype(jnp.float32)
    solid = jnp.broadcast_to((1.0 - fluid)[None, None, :, None], (1, levels, blocks, cells))
    extended = jnp.concatenate([post, solid], axis=0)
    width = channels + 1
    flat = lambda halo: halo.reshape(-1, BE)
    ahead, behind = ring_pairs("line")
    by_rows = extended.reshape(width, levels, TY, TX, BE, BE)
    column_shape = (width, levels, TY, BE)
    left_cols = lax.ppermute(flat(by_rows[:, :, :, TX - 1, :, BE - 1]), "line", ahead).reshape(column_shape)
    right_cols = lax.ppermute(flat(by_rows[:, :, :, 0, :, 0]), "line", behind).reshape(column_shape)
    corner = lambda cols, py, r: jnp.broadcast_to(cols[:, :, py:py + 1, r:r + 1], (width, levels, 1, BE))
    top_row = jnp.concatenate(
        [
            corner(left_cols, TY - 1, BE - 1),
            extended[:, :, blocks - TX:, cells - BE:],
            corner(right_cols, TY - 1, BE - 1),
        ],
        axis=2,
    )
    bottom_row = jnp.concatenate(
        [corner(left_cols, 0, 0), extended[:, :, :TX, :BE], corner(right_cols, 0, 0)], axis=2
    )
    ahead, behind = ring_pairs("curve")
    row_shape = (width, levels, TX + 2, BE)
    below = lax.ppermute(flat(top_row), "curve", ahead).reshape(row_shape)
    above = lax.ppermute(flat(bottom_row), "curve", behind).reshape(row_shape)
    below_flat = flat(below[:, :, 1:TX + 1])
    above_flat = flat(above[:, :, 1:TX + 1])
    from_left = flat(jnp.concatenate([below[:, :, :1], left_cols, above[:, :, :1]], axis=2))
    from_right = flat(
        jnp.concatenate([below[:, :, TX + 1:], right_cols, above[:, :, TX + 1:]], axis=2)
    )
    new_state = stream(living_brick_keys, post, below_flat, above_flat, from_left, from_right)
    return new_state.reshape((1, 1, seats, channels, levels * cells))


def solution(mesh):
    return jax.shard_map(
        on_device,
        mesh=mesh,
        in_specs=(
            P("curve", "line", None, None, None),
            P("curve", "line", None),
            P(),
            P(None, None, "curve", None),
            P(),
        ),
        out_specs=P("curve", "line", None, None, None),
        check_vma=False,
    )
```

```python
import jax
import jax.numpy as jnp
import numpy as np
from jax import lax
from jax.experimental import pallas as pl
from jax.experimental.pallas import tpu as pltpu
from jax.sharding import PartitionSpec as P

BE = 16
TX = 4
TY = 2


NUDGE_GAIN = 0.5
TWO_PI = 6.283185307179586
HIGHEST = lax.Precision.HIGHEST


def butterfly_sum(value, axis):
    count = lax.axis_size(axis)
    stride = 1
    while stride < count:
        value = value + lax.ppermute(value, axis, [(i, i ^ stride) for i in range(count)])
        stride *= 2
    return value


def ring_pairs(axis):
    count = lax.axis_size(axis)
    forward = [(i, (i + 1) % count) for i in range(count)]
    backward = [(target, source) for source, target in forward]
    return forward, backward


def lattice_tables():
    one_weights = np.array([1.0 / 6.0, 2.0 / 3.0, 1.0 / 6.0])
    speeds = np.array(
        [
            [along_x - 1, along_y - 1, along_z - 1]
            for along_x in range(3)
            for along_y in range(3)
            for along_z in range(3)
        ]
    )
    weights = np.array(
        [
            one_weights[along_x] * one_weights[along_y] * one_weights[along_z]
            for along_x in range(3)
            for along_y in range(3)
            for along_z in range(3)
        ]
    )
    vander = np.array([[1.0, 1.0, 1.0], [-1.0, 0.0, 1.0], [1.0, 0.0, 1.0]])
    undo_vander = np.array([[0.0, -0.5, 0.5], [1.0, 0.0, -1.0], [0.0, 0.5, 0.5]])
    moment_matrix = np.kron(vander, np.kron(vander, vander))
    inverse = np.kron(undo_vander, np.kron(undo_vander, undo_vander))
    forward = jnp.asarray(moment_matrix * weights[None, :], dtype=jnp.float32)
    backward = jnp.asarray(inverse / weights[:, None], dtype=jnp.float32)
    return (forward, backward, speeds)


def mode_basis_at(mode_ids, positions, length):
    phase_ids = positions[:, None] * mode_ids[None, :] % length
    angles = phase_ids.astype(jnp.float32) * (TWO_PI / length)
    return jnp.concatenate([jnp.cos(angles), jnp.sin(angles)], axis=1)


def collide_blocks(moments, velocity, nudge, backward, relaxation_frequencies):
    density = moments[0]
    shifted = velocity + nudge
    powers = jnp.stack([jnp.ones_like(shifted), shifted, shifted * shifted + 1.0 / 3.0], axis=0)
    equilibrium = (
        density[None, None, None]
        * powers[:, None, None, 0]
        * powers[None, :, None, 1]
        * powers[None, None, :, 2]
    )
    equilibrium = equilibrium.reshape(moments.shape)
    relaxed = moments - relaxation_frequencies[:, None, None, None] * (moments - equilibrium)
    return jnp.einsum("ij,jzpl->izpl", backward, relaxed, precision=HIGHEST)


def moments_kernel(keys_ref, forward_ref, state_ref, out_ref, wind_ref, scratch_ref):
    levels, blocks, channels, cells = out_ref.shape
    seats = scratch_ref.shape[0]
    chunks = levels * cells // 128
    forward = forward_ref[...]
    for seat_number in range(seats):
        pieces = [
            state_ref[pl.ds(seat_number * channels * chunks + chunk, channels, stride=chunks), :]
            for chunk in range(chunks)
        ]
        scratch_ref[seat_number] = jnp.dot(
            forward, jnp.concatenate(pieces, axis=1), precision=HIGHEST,
            preferred_element_type=jnp.float32,
        )
    for block in range(blocks):
        slot = 0
        found = False
        for seat_number in range(seats):
            hit = keys_ref[seat_number] == block
            slot = jnp.where(hit, seat_number, slot)
            found = jnp.logical_or(found, hit)
        keep = jnp.where(found, 1.0, 0.0)
        for level in range(levels):
            values = scratch_ref[slot, :, level * cells:(level + 1) * cells] * keep
            out_ref[level, block] = values
            density = jnp.where(found, values[0:1], 1.0)
            for component, row in enumerate((9, 3, 1)):
                wind_ref[component, level, block:block + 1, :] = values[row:row + 1] / density


def cell_moments(keys, forward, rows, seats, levels):
    channels = forward.shape[0]
    blocks = TX * TY
    cells = rows.size // (seats * channels * levels)
    vmem = pl.BlockSpec(memory_space=pltpu.VMEM)
    smem = pl.BlockSpec(memory_space=pltpu.SMEM)
    return pl.pallas_call(
        moments_kernel,
        out_shape=(
            jax.ShapeDtypeStruct((levels, blocks, channels, cells), jnp.float32),
            jax.ShapeDtypeStruct((3, levels, blocks, cells), jnp.float32),
        ),
        in_specs=[smem, vmem, vmem],
        out_specs=(vmem, vmem),
        scratch_shapes=[pltpu.VMEM((seats, channels, levels * cells), jnp.float32)],
    )(keys, forward, rows)


def stream_kernel(
    keys_ref, post_ref, below_ref, above_ref, left_ref, right_ref, out_ref, spread_ref, column_ref, result_ref
):
    levels, blocks, channels, cells = post_ref.shape
    _, _, speeds = lattice_tables()
    front = 8
    grid_row = lax.broadcasted_iota(jnp.int32, (BE, cells), 0)
    grid_lane = lax.broadcasted_iota(jnp.int32, (BE, cells), 1)
    tile_copy = (grid_lane % BE == grid_row).astype(jnp.float32)
    group_copy = (grid_lane // BE == grid_row).astype(jnp.float32)
    row_count = below_ref.shape[0]
    column_count = left_ref.shape[0]
    for slot, source in enumerate((below_ref, above_ref)):
        spread_ref[slot, front:front + row_count, :] = jnp.dot(
            source[...], tile_copy, precision=HIGHEST, preferred_element_type=jnp.float32
        )
    for slot, source in enumerate((left_ref, right_ref)):
        column_ref[slot, front:front + column_count, :] = jnp.dot(
            source[...], group_copy, precision=HIGHEST, preferred_element_type=jnp.float32
        )
    lane = lax.broadcasted_iota(jnp.int32, (blocks, cells), 1)
    seat = lax.broadcasted_iota(jnp.int32, (blocks, cells), 0)
    q = lane % BE
    r = lane // BE
    py = seat // TX

    solid_plane = jnp.zeros((blocks, cells), jnp.float32)
    for block in range(blocks):
        found = False
        for seat_number in range(keys_ref.shape[0]):
            found = jnp.logical_or(found, keys_ref[seat_number] == block)
        solid_plane = jnp.where(seat == block, jnp.where(found, 0.0, 1.0), solid_plane)

    def own(channel, level):
        if channel == channels:
            return solid_plane
        return post_ref[level, :, channel, :]

    def moved(plane, shift):
        shift = shift % cells
        if shift == 0:
            return plane
        return pltpu.roll(plane, shift, 1)

    def gathered(channel, level, cx, cy):
        shift = cy * BE + cx
        entry = channel * levels + level
        first = front + entry * (TX + 2)
        first_column = front + entry * TY
        base = own(channel, level)
        if cy != 0:
            stepped = pltpu.roll(base, TX, 0)
            if cy == 1:
                halo = spread_ref[0, first + 1:first + 1 + blocks, :]
                yplane = jnp.where(py == 0, halo, stepped)
            else:
                halo = spread_ref[1, first + 1 - TX:first + 1 - TX + blocks, :]
                yplane = jnp.where(py == TY - 1, halo, stepped)

        def side_row(k, dx):
            corner_at = first if dx == 1 else first + TX + 1
            if k == 0:
                return spread_ref[0, corner_at:corner_at + 1, :]
            if k == TY + 1:
                return spread_ref[1, corner_at:corner_at + 1, :]
            at = first_column + k - 1
            return column_ref[0 if dx == 1 else 1, at:at + 1, :]

        def sideways(plane, dy, dx):
            plane = pltpu.roll(plane, dx % blocks, 0)
            edge = 0 if dx == 1 else TX - 1
            return jnp.where(
                seat == edge,
                side_row(1 - dy, dx),
                jnp.where(seat == edge + TX, side_row(2 - dy, dx), plane),
            )
        value = moved(base, shift)
        if cy != 0:
            ycross = r == (0 if cy == 1 else BE - 1)
            value = jnp.where(ycross, moved(yplane, shift), value)
        if cx != 0:
            xcross = q == (0 if cx == 1 else BE - 1)
            xvalue = moved(sideways(base, 0, cx), shift - BE * cx)
            if cy != 0:
                xvalue = jnp.where(ycross, moved(sideways(yplane, cy, cx), shift - BE * cx), xvalue)
            value = jnp.where(xcross, xvalue, value)
        return value

    blocked_of = {}
    for cx in (-1, 0, 1):
        for cy in (-1, 0, 1):
            blocked_of[(cx, cy)] = gathered(channels, 0, cx, cy) > 0.5
    for heading in range(27):
        cx, cy, cz = (int(v) for v in speeds[heading])
        blocked = blocked_of[(cx, cy)]
        for level in range(levels):
            bounced = post_ref[level, :, 26 - heading, :]
            window = pl.ds(level * cells, cells)
            if cz == 1 and level == 0:
                result_ref[:, heading, window] = bounced
                continue
            if cz == 0:
                source = gathered(heading, level, cx, cy)
            elif cz == 1:
                source = gathered(heading, 0, cx, cy)
            elif level == 0:
                source = gathered(heading, 1, cx, cy)
            else:
                source = gathered(heading + 2, 1, cx, cy)
            result_ref[:, heading, window] = jnp.where(blocked, bounced, source)
    chunks = levels * cells // 128
    for seat_number in range(keys_ref.shape[0]):
        key = keys_ref[seat_number]
        for chunk in range(chunks):
            picked = result_ref[jnp.maximum(key, 0), :, chunk * 128:(chunk + 1) * 128]
            rows = pl.ds(seat_number * channels * chunks + chunk, channels, stride=chunks)
            out_ref[rows, :] = jnp.where(key >= 0, picked, 0.0)


def stream(keys, post, below, above, from_left, from_right):
    channels, levels, blocks, cells = post.shape
    seats = keys.shape[0]
    row_count = below.shape[0]
    column_count = from_left.shape[0]
    vmem = pl.BlockSpec(memory_space=pltpu.VMEM)
    smem = pl.BlockSpec(memory_space=pltpu.SMEM)
    return pl.pallas_call(
        stream_kernel,
        out_shape=jax.ShapeDtypeStruct((seats * channels * levels * cells // 128, 128), jnp.float32),
        in_specs=[smem] + [vmem] * 5,
        out_specs=vmem,
        scratch_shapes=[
            pltpu.VMEM((2, row_count + 16, cells), jnp.float32),
            pltpu.VMEM((2, column_count + 16, cells), jnp.float32),
            pltpu.VMEM((blocks, channels, levels * cells), jnp.float32),
        ],
    )(keys, post.transpose(1, 2, 0, 3), below, above, from_left, from_right)


def on_device(
    scaled_distributions,
    remaining_brick_places,
    retained_wavenumbers,
    regional_amplitudes,
    relaxation_frequencies,
):
    forward, backward, speeds = lattice_tables()
    slot_state = scaled_distributions[0, 0]
    living_brick_keys = remaining_brick_places[0, 0]
    seats = living_brick_keys.shape[0]
    channels = slot_state.shape[1]
    cells = BE * BE
    levels = slot_state.shape[2] // cells
    blocks = TX * TY
    rows_tile = TY * BE
    cols_tile = TX * BE
    rows = slot_state.reshape(-1, 128)
    moments, wind = cell_moments(living_brick_keys, forward, rows, seats, levels)
    moments = moments.transpose(2, 0, 1, 3)
    line_length = lax.axis_size("line") * cols_tile
    own_columns = lax.axis_index("line") * cols_tile + jnp.arange(cols_tile, dtype=jnp.int32)
    mode_basis = mode_basis_at(retained_wavenumbers, own_columns, line_length).reshape(TX, BE, -1)
    partial = jnp.einsum(
        "kzyxrq,xqm->kzyrm", wind.reshape(3, levels, TY, TX, BE, BE), mode_basis,
        precision=HIGHEST,
    ).reshape(3, levels, rows_tile, -1)
    coefficients = butterfly_sum(partial, "line")
    misfit = regional_amplitudes - 2.0 / line_length * coefficients
    nudge = NUDGE_GAIN * jnp.einsum(
        "kzyrm,xqm->kzyxrq", misfit.reshape(3, levels, TY, BE, -1), mode_basis,
        precision=HIGHEST,
    ).reshape(3, levels, blocks, cells)
    post = collide_blocks(moments, wind, nudge, backward, relaxation_frequencies)
    present = jnp.any(living_brick_keys[None, :] == jnp.arange(blocks, dtype=jnp.int32)[:, None], axis=1)
    fluid = present.astype(jnp.float32)
    solid = jnp.broadcast_to((1.0 - fluid)[None, None, :, None], (1, levels, blocks, cells))
    extended = jnp.concatenate([post, solid], axis=0)
    width = channels + 1
    flat = lambda halo: halo.reshape(-1, BE)
    ahead, behind = ring_pairs("line")
    by_rows = extended.reshape(width, levels, TY, TX, BE, BE)
    column_shape = (width, levels, TY, BE)
    left_cols = lax.ppermute(flat(by_rows[:, :, :, TX - 1, :, BE - 1]), "line", ahead).reshape(column_shape)
    right_cols = lax.ppermute(flat(by_rows[:, :, :, 0, :, 0]), "line", behind).reshape(column_shape)
    corner = lambda cols, py, r: jnp.broadcast_to(cols[:, :, py:py + 1, r:r + 1], (width, levels, 1, BE))
    top_row = jnp.concatenate(
        [
            corner(left_cols, TY - 1, BE - 1),
            extended[:, :, blocks - TX:, cells - BE:],
            corner(right_cols, TY - 1, BE - 1),
        ],
        axis=2,
    )
    bottom_row = jnp.concatenate(
        [corner(left_cols, 0, 0), extended[:, :, :TX, :BE], corner(right_cols, 0, 0)], axis=2
    )
    ahead, behind = ring_pairs("curve")
    row_shape = (width, levels, TX + 2, BE)
    below = lax.ppermute(flat(top_row), "curve", ahead).reshape(row_shape)
    above = lax.ppermute(flat(bottom_row), "curve", behind).reshape(row_shape)
    below_flat = flat(below)
    above_flat = flat(above)
    from_left = flat(left_cols)
    from_right = flat(right_cols)
    new_state = stream(living_brick_keys, post, below_flat, above_flat, from_left, from_right)
    return new_state.reshape((1, 1, seats, channels, levels * cells))


def solution(mesh):
    return jax.shard_map(
        on_device,
        mesh=mesh,
        in_specs=(
            P("curve", "line", None, None, None),
            P("curve", "line", None),
            P(),
            P(None, None, "curve", None),
            P(),
        ),
        out_specs=P("curve", "line", None, None, None),
        check_vma=False,
    )
```

```python
import jax
import jax.numpy as jnp
import numpy as np
from jax import lax
from jax.experimental import pallas as pl
from jax.experimental.pallas import tpu as pltpu
from jax.sharding import PartitionSpec as P

BE = 16
TX = 4
TY = 2


NUDGE_GAIN = 0.5
TWO_PI = 6.283185307179586
HIGHEST = lax.Precision.HIGHEST


def butterfly_sum(value, axis):
    count = lax.axis_size(axis)
    stride = 1
    while stride < count:
        value = value + lax.ppermute(value, axis, [(i, i ^ stride) for i in range(count)])
        stride *= 2
    return value


def ring_pairs(axis):
    count = lax.axis_size(axis)
    forward = [(i, (i + 1) % count) for i in range(count)]
    backward = [(target, source) for source, target in forward]
    return forward, backward


def lattice_tables():
    one_weights = np.array([1.0 / 6.0, 2.0 / 3.0, 1.0 / 6.0])
    speeds = np.array(
        [
            [along_x - 1, along_y - 1, along_z - 1]
            for along_x in range(3)
            for along_y in range(3)
            for along_z in range(3)
        ]
    )
    weights = np.array(
        [
            one_weights[along_x] * one_weights[along_y] * one_weights[along_z]
            for along_x in range(3)
            for along_y in range(3)
            for along_z in range(3)
        ]
    )
    vander = np.array([[1.0, 1.0, 1.0], [-1.0, 0.0, 1.0], [1.0, 0.0, 1.0]])
    undo_vander = np.array([[0.0, -0.5, 0.5], [1.0, 0.0, -1.0], [0.0, 0.5, 0.5]])
    moment_matrix = np.kron(vander, np.kron(vander, vander))
    inverse = np.kron(undo_vander, np.kron(undo_vander, undo_vander))
    forward = jnp.asarray(moment_matrix * weights[None, :], dtype=jnp.float32)
    backward = jnp.asarray(inverse / weights[:, None], dtype=jnp.float32)
    return (forward, backward, speeds)


def mode_basis_at(mode_ids, positions, length):
    phase_ids = positions[:, None] * mode_ids[None, :] % length
    angles = phase_ids.astype(jnp.float32) * (TWO_PI / length)
    return jnp.concatenate([jnp.cos(angles), jnp.sin(angles)], axis=1)


def collide_blocks(moments, velocity, nudge, backward, relaxation_frequencies):
    density = moments[0]
    shifted = velocity + nudge
    powers = jnp.stack([jnp.ones_like(shifted), shifted, shifted * shifted + 1.0 / 3.0], axis=0)
    equilibrium = (
        density[None, None, None]
        * powers[:, None, None, 0]
        * powers[None, :, None, 1]
        * powers[None, None, :, 2]
    )
    equilibrium = equilibrium.reshape(moments.shape)
    relaxed = moments - relaxation_frequencies[:, None, None, None] * (moments - equilibrium)
    return jnp.einsum("ij,jzpl->izpl", backward, relaxed, precision=HIGHEST)


def moments_kernel(keys_ref, forward_ref, state_ref, out_ref, wind_ref, scratch_ref):
    levels, blocks, channels, cells = out_ref.shape
    seats = scratch_ref.shape[0]
    chunks = levels * cells // 128
    forward = forward_ref[...]
    for seat_number in range(seats):
        pieces = [
            state_ref[pl.ds(seat_number * channels * chunks + chunk, channels, stride=chunks), :]
            for chunk in range(chunks)
        ]
        scratch_ref[seat_number] = jnp.dot(
            forward, jnp.concatenate(pieces, axis=1), precision=HIGHEST,
            preferred_element_type=jnp.float32,
        )
    for block in range(blocks):
        slot = 0
        found = False
        for seat_number in range(seats):
            hit = keys_ref[seat_number] == block
            slot = jnp.where(hit, seat_number, slot)
            found = jnp.logical_or(found, hit)
        keep = jnp.where(found, 1.0, 0.0)
        for level in range(levels):
            values = scratch_ref[slot, :, level * cells:(level + 1) * cells] * keep
            out_ref[level, block] = values
            density = jnp.where(found, values[0:1], 1.0)
            for component, row in enumerate((9, 3, 1)):
                wind_ref[component, level, block:block + 1, :] = values[row:row + 1] / density


def cell_moments(keys, forward, rows, seats, levels):
    channels = forward.shape[0]
    blocks = TX * TY
    cells = rows.size // (seats * channels * levels)
    vmem = pl.BlockSpec(memory_space=pltpu.VMEM)
    smem = pl.BlockSpec(memory_space=pltpu.SMEM)
    return pl.pallas_call(
        moments_kernel,
        out_shape=(
            jax.ShapeDtypeStruct((levels, blocks, channels, cells), jnp.float32),
            jax.ShapeDtypeStruct((3, levels, blocks, cells), jnp.float32),
        ),
        in_specs=[smem, vmem, vmem],
        out_specs=(vmem, vmem),
        scratch_shapes=[pltpu.VMEM((seats, channels, levels * cells), jnp.float32)],
    )(keys, forward, rows)


def stream_kernel(
    keys_ref, post_ref, below_ref, above_ref, left_ref, right_ref, out_ref, spread_ref, column_ref, result_ref
):
    levels, blocks, channels, cells = post_ref.shape
    _, _, speeds = lattice_tables()
    front = 8
    grid_row = lax.broadcasted_iota(jnp.int32, (BE, cells), 0)
    grid_lane = lax.broadcasted_iota(jnp.int32, (BE, cells), 1)
    tile_copy = (grid_lane % BE == grid_row).astype(jnp.float32)
    group_copy = (grid_lane // BE == grid_row).astype(jnp.float32)
    row_count = below_ref.shape[0]
    column_count = left_ref.shape[0]
    for slot, source in enumerate((below_ref, above_ref)):
        spread_ref[slot, front:front + row_count, :] = jnp.dot(
            source[...], tile_copy, precision=HIGHEST, preferred_element_type=jnp.float32
        )
    for slot, source in enumerate((left_ref, right_ref)):
        column_ref[slot, front:front + column_count, :] = jnp.dot(
            source[...], group_copy, precision=HIGHEST, preferred_element_type=jnp.float32
        )
    lane = lax.broadcasted_iota(jnp.int32, (blocks, cells), 1)
    seat = lax.broadcasted_iota(jnp.int32, (blocks, cells), 0)
    q = lane % BE
    r = lane // BE
    py = seat // TX

    solid_plane = jnp.zeros((blocks, cells), jnp.float32)
    for block in range(blocks):
        found = False
        for seat_number in range(keys_ref.shape[0]):
            found = jnp.logical_or(found, keys_ref[seat_number] == block)
        solid_plane = jnp.where(seat == block, jnp.where(found, 0.0, 1.0), solid_plane)

    def own(channel, level):
        if channel == channels:
            return solid_plane
        return post_ref[level, :, channel, :]

    def moved(plane, shift):
        shift = shift % cells
        if shift == 0:
            return plane
        return pltpu.roll(plane, shift, 1)

    def gathered(channel, level, cx, cy):
        shift = cy * BE + cx
        entry = channel * levels + level
        first = front + entry * (TX + 2)
        first_column = front + entry * TY
        base = own(channel, level)
        if cy != 0:
            stepped = pltpu.roll(base, TX, 0)
            if cy == 1:
                halo = spread_ref[0, first + 1:first + 1 + blocks, :]
                yplane = jnp.where(py == 0, halo, stepped)
            else:
                halo = spread_ref[1, first + 1 - TX:first + 1 - TX + blocks, :]
                yplane = jnp.where(py == TY - 1, halo, stepped)

        def side_row(k, dx):
            corner_at = first if dx == 1 else first + TX + 1
            if k == 0:
                return spread_ref[0, corner_at:corner_at + 1, :]
            if k == TY + 1:
                return spread_ref[1, corner_at:corner_at + 1, :]
            at = first_column + k - 1
            return column_ref[0 if dx == 1 else 1, at:at + 1, :]

        def sideways(plane, dy, dx):
            plane = pltpu.roll(plane, dx % blocks, 0)
            edge = 0 if dx == 1 else TX - 1
            return jnp.where(
                seat == edge,
                side_row(1 - dy, dx),
                jnp.where(seat == edge + TX, side_row(2 - dy, dx), plane),
            )
        value = moved(base, shift)
        if cy != 0:
            ycross = r == (0 if cy == 1 else BE - 1)
            value = jnp.where(ycross, moved(yplane, shift), value)
        if cx != 0:
            xcross = q == (0 if cx == 1 else BE - 1)
            xvalue = moved(sideways(base, 0, cx), shift - BE * cx)
            if cy != 0:
                xvalue = jnp.where(ycross, moved(sideways(yplane, cy, cx), shift - BE * cx), xvalue)
            value = jnp.where(xcross, xvalue, value)
        return value

    blocked_of = {}
    for cx in (-1, 0, 1):
        for cy in (-1, 0, 1):
            blocked_of[(cx, cy)] = gathered(channels, 0, cx, cy) > 0.5
    for heading in range(27):
        cx, cy, cz = (int(v) for v in speeds[heading])
        blocked = blocked_of[(cx, cy)]
        for level in range(levels):
            bounced = post_ref[level, :, 26 - heading, :]
            window = pl.ds(level * cells, cells)
            if cz == 1 and level == 0:
                result_ref[:, heading, window] = bounced
                continue
            if cz == 0:
                source = gathered(heading, level, cx, cy)
            elif cz == 1:
                source = gathered(heading, 0, cx, cy)
            elif level == 0:
                source = gathered(heading, 1, cx, cy)
            else:
                source = gathered(heading + 2, 1, cx, cy)
            result_ref[:, heading, window] = jnp.where(blocked, bounced, source)
    chunks = levels * cells // 128
    for seat_number in range(keys_ref.shape[0]):
        key = keys_ref[seat_number]
        for chunk in range(chunks):
            picked = result_ref[jnp.maximum(key, 0), :, chunk * 128:(chunk + 1) * 128]
            rows = pl.ds(seat_number * channels * chunks + chunk, channels, stride=chunks)
            out_ref[rows, :] = jnp.where(key >= 0, picked, 0.0)


def stream(keys, post, below, above, from_left, from_right):
    channels, levels, blocks, cells = post.shape
    seats = keys.shape[0]
    row_count = below.shape[0]
    column_count = from_left.shape[0]
    vmem = pl.BlockSpec(memory_space=pltpu.VMEM)
    smem = pl.BlockSpec(memory_space=pltpu.SMEM)
    return pl.pallas_call(
        stream_kernel,
        out_shape=jax.ShapeDtypeStruct((seats * channels * levels * cells // 128, 128), jnp.float32),
        in_specs=[smem] + [vmem] * 5,
        out_specs=vmem,
        scratch_shapes=[
            pltpu.VMEM((2, row_count + 16, cells), jnp.float32),
            pltpu.VMEM((2, column_count + 16, cells), jnp.float32),
            pltpu.VMEM((blocks, channels, levels * cells), jnp.float32),
        ],
    )(keys, post.transpose(1, 2, 0, 3), below, above, from_left, from_right)


def on_device(
    scaled_distributions,
    remaining_brick_places,
    retained_wavenumbers,
    regional_amplitudes,
    relaxation_frequencies,
):
    forward, backward, speeds = lattice_tables()
    slot_state = scaled_distributions[0, 0]
    living_brick_keys = remaining_brick_places[0, 0]
    seats = living_brick_keys.shape[0]
    channels = slot_state.shape[1]
    cells = BE * BE
    levels = slot_state.shape[2] // cells
    blocks = TX * TY
    rows_tile = TY * BE
    cols_tile = TX * BE
    rows = slot_state.reshape(-1, 128)
    moments, wind = cell_moments(living_brick_keys, forward, rows, seats, levels)
    moments = moments.transpose(2, 0, 1, 3)
    line_length = lax.axis_size("line") * cols_tile
    own_columns = lax.axis_index("line") * cols_tile + jnp.arange(cols_tile, dtype=jnp.int32)
    mode_basis = mode_basis_at(retained_wavenumbers, own_columns, line_length).reshape(TX, BE, -1)
    partial = jnp.einsum(
        "kzyxrq,xqm->kzyrm", wind.reshape(3, levels, TY, TX, BE, BE), mode_basis,
        precision=HIGHEST,
    ).reshape(3, levels, rows_tile, -1)
    coefficients = butterfly_sum(partial, "line")
    misfit = regional_amplitudes - 2.0 / line_length * coefficients
    nudge = NUDGE_GAIN * jnp.einsum(
        "kzyrm,xqm->kzyxrq", misfit.reshape(3, levels, TY, BE, -1), mode_basis,
        precision=HIGHEST,
    ).reshape(3, levels, blocks, cells)
    post = collide_blocks(moments, wind, nudge, backward, relaxation_frequencies)
    present = jnp.any(living_brick_keys[None, :] == jnp.arange(blocks, dtype=jnp.int32)[:, None], axis=1)
    fluid = present.astype(jnp.float32)
    solid = jnp.broadcast_to((1.0 - fluid)[None, None, :, None], (1, levels, blocks, cells))
    pick = lambda cut: jnp.concatenate([cut(post), cut(solid)], axis=0)
    width = channels + 1
    flat = lambda halo: halo.reshape(-1, BE)
    ahead, behind = ring_pairs("line")
    column_shape = (width, levels, TY, BE)
    by_rows = lambda part: part.reshape(part.shape[:2] + (TY, TX, BE, BE))
    right_edge = pick(lambda part: by_rows(part)[:, :, :, TX - 1, :, BE - 1])
    left_edge = pick(lambda part: by_rows(part)[:, :, :, 0, :, 0])
    left_cols = lax.ppermute(flat(right_edge), "line", ahead).reshape(column_shape)
    right_cols = lax.ppermute(flat(left_edge), "line", behind).reshape(column_shape)
    corner = lambda cols, py, r: jnp.broadcast_to(cols[:, :, py:py + 1, r:r + 1], (width, levels, 1, BE))
    top_row = jnp.concatenate(
        [
            corner(left_cols, TY - 1, BE - 1),
            pick(lambda part: part[:, :, blocks - TX:, cells - BE:]),
            corner(right_cols, TY - 1, BE - 1),
        ],
        axis=2,
    )
    bottom_row = jnp.concatenate(
        [corner(left_cols, 0, 0), pick(lambda part: part[:, :, :TX, :BE]), corner(right_cols, 0, 0)],
        axis=2,
    )
    ahead, behind = ring_pairs("curve")
    row_shape = (width, levels, TX + 2, BE)
    below = lax.ppermute(flat(top_row), "curve", ahead).reshape(row_shape)
    above = lax.ppermute(flat(bottom_row), "curve", behind).reshape(row_shape)
    below_flat = flat(below)
    above_flat = flat(above)
    from_left = flat(left_cols)
    from_right = flat(right_cols)
    new_state = stream(living_brick_keys, post, below_flat, above_flat, from_left, from_right)
    return new_state.reshape((1, 1, seats, channels, levels * cells))


def solution(mesh):
    return jax.shard_map(
        on_device,
        mesh=mesh,
        in_specs=(
            P("curve", "line", None, None, None),
            P("curve", "line", None),
            P(),
            P(None, None, "curve", None),
            P(),
        ),
        out_specs=P("curve", "line", None, None, None),
        check_vma=False,
    )
```

```python
import jax
import jax.numpy as jnp
import numpy as np
from jax import lax
from jax.experimental import pallas as pl
from jax.experimental.pallas import tpu as pltpu
from jax.sharding import PartitionSpec as P

BE = 16
TX = 4
TY = 2


NUDGE_GAIN = 0.5
TWO_PI = 6.283185307179586
HIGHEST = lax.Precision.HIGHEST


def butterfly_sum(value, axis):
    count = lax.axis_size(axis)
    stride = 1
    while stride < count:
        value = value + lax.ppermute(value, axis, [(i, i ^ stride) for i in range(count)])
        stride *= 2
    return value


def ring_pairs(axis):
    count = lax.axis_size(axis)
    forward = [(i, (i + 1) % count) for i in range(count)]
    backward = [(target, source) for source, target in forward]
    return forward, backward


def lattice_tables():
    one_weights = np.array([1.0 / 6.0, 2.0 / 3.0, 1.0 / 6.0])
    speeds = np.array(
        [
            [along_x - 1, along_y - 1, along_z - 1]
            for along_x in range(3)
            for along_y in range(3)
            for along_z in range(3)
        ]
    )
    weights = np.array(
        [
            one_weights[along_x] * one_weights[along_y] * one_weights[along_z]
            for along_x in range(3)
            for along_y in range(3)
            for along_z in range(3)
        ]
    )
    vander = np.array([[1.0, 1.0, 1.0], [-1.0, 0.0, 1.0], [1.0, 0.0, 1.0]])
    undo_vander = np.array([[0.0, -0.5, 0.5], [1.0, 0.0, -1.0], [0.0, 0.5, 0.5]])
    moment_matrix = np.kron(vander, np.kron(vander, vander))
    inverse = np.kron(undo_vander, np.kron(undo_vander, undo_vander))
    forward = jnp.asarray(moment_matrix * weights[None, :], dtype=jnp.float32)
    backward = jnp.asarray(inverse / weights[:, None], dtype=jnp.float32)
    return (forward, backward, speeds)


def mode_basis_at(mode_ids, positions, length):
    phase_ids = positions[:, None] * mode_ids[None, :] % length
    angles = phase_ids.astype(jnp.float32) * (TWO_PI / length)
    return jnp.concatenate([jnp.cos(angles), jnp.sin(angles)], axis=1)


def collide_blocks(moments, velocity, nudge, backward, relaxation_frequencies):
    density = moments[0]
    shifted = velocity + nudge
    powers = jnp.stack([jnp.ones_like(shifted), shifted, shifted * shifted + 1.0 / 3.0], axis=0)
    equilibrium = (
        density[None, None, None]
        * powers[:, None, None, 0]
        * powers[None, :, None, 1]
        * powers[None, None, :, 2]
    )
    equilibrium = equilibrium.reshape(moments.shape)
    relaxed = moments - relaxation_frequencies[:, None, None, None] * (moments - equilibrium)
    return jnp.einsum("ij,jzpl->izpl", backward, relaxed, precision=HIGHEST)


def moments_kernel(keys_ref, forward_ref, state_ref, out_ref, wind_ref, scratch_ref):
    levels, blocks, channels, cells = out_ref.shape
    seats = scratch_ref.shape[0]
    chunks = levels * cells // 128
    forward = forward_ref[...]
    for seat_number in range(seats):
        pieces = [
            state_ref[pl.ds(seat_number * channels * chunks + chunk, channels, stride=chunks), :]
            for chunk in range(chunks)
        ]
        scratch_ref[seat_number] = jnp.dot(
            forward, jnp.concatenate(pieces, axis=1), precision=HIGHEST,
            preferred_element_type=jnp.float32,
        )
    for block in range(blocks):
        slot = 0
        found = False
        for seat_number in range(seats):
            hit = keys_ref[seat_number] == block
            slot = jnp.where(hit, seat_number, slot)
            found = jnp.logical_or(found, hit)
        keep = jnp.where(found, 1.0, 0.0)
        for level in range(levels):
            values = scratch_ref[slot, :, level * cells:(level + 1) * cells] * keep
            out_ref[level, block] = values
            density = jnp.where(found, values[0:1], 1.0)
            for component, row in enumerate((9, 3, 1)):
                wind_ref[component, level, block:block + 1, :] = values[row:row + 1] / density


def cell_moments(keys, forward, rows, seats, levels):
    channels = forward.shape[0]
    blocks = TX * TY
    cells = rows.size // (seats * channels * levels)
    vmem = pl.BlockSpec(memory_space=pltpu.VMEM)
    smem = pl.BlockSpec(memory_space=pltpu.SMEM)
    return pl.pallas_call(
        moments_kernel,
        out_shape=(
            jax.ShapeDtypeStruct((levels, blocks, channels, cells), jnp.float32),
            jax.ShapeDtypeStruct((3, levels, blocks, cells), jnp.float32),
        ),
        in_specs=[smem, vmem, vmem],
        out_specs=(vmem, vmem),
        scratch_shapes=[pltpu.VMEM((seats, channels, levels * cells), jnp.float32)],
    )(keys, forward, rows)


def level_steps_kernel(keys_ref, post_ref, left_ref, right_ref, result_ref, column_ref):
    stream_body(0, keys_ref, post_ref, None, None, left_ref, right_ref, None, None, None, column_ref, result_ref)


def stream_kernel(
    keys_ref, post_ref, below_ref, above_ref, left_ref, right_ref, partial_ref, out_ref, spread_ref,
    column_ref, result_ref,
):
    stream_body(
        1, keys_ref, post_ref, below_ref, above_ref, left_ref, right_ref, partial_ref, out_ref, spread_ref,
        column_ref, result_ref,
    )


def stream_body(
    part, keys_ref, post_ref, below_ref, above_ref, left_ref, right_ref, partial_ref, out_ref, spread_ref,
    column_ref, result_ref,
):
    levels, blocks, channels, cells = post_ref.shape
    _, _, speeds = lattice_tables()
    front = 8
    grid_row = lax.broadcasted_iota(jnp.int32, (BE, cells), 0)
    grid_lane = lax.broadcasted_iota(jnp.int32, (BE, cells), 1)
    tile_copy = (grid_lane % BE == grid_row).astype(jnp.float32)
    group_copy = (grid_lane // BE == grid_row).astype(jnp.float32)
    column_count = left_ref.shape[0]
    if part == 1:
        row_count = below_ref.shape[0]
        for slot, source in enumerate((below_ref, above_ref)):
            spread_ref[slot, front:front + row_count, :] = jnp.dot(
                source[...], tile_copy, precision=HIGHEST, preferred_element_type=jnp.float32
            )
        result_ref[...] = partial_ref[...]
    for slot, source in enumerate((left_ref, right_ref)):
        column_ref[slot, front:front + column_count, :] = jnp.dot(
            source[...], group_copy, precision=HIGHEST, preferred_element_type=jnp.float32
        )
    lane = lax.broadcasted_iota(jnp.int32, (blocks, cells), 1)
    seat = lax.broadcasted_iota(jnp.int32, (blocks, cells), 0)
    q = lane % BE
    r = lane // BE
    py = seat // TX

    solid_plane = jnp.zeros((blocks, cells), jnp.float32)
    for block in range(blocks):
        found = False
        for seat_number in range(keys_ref.shape[0]):
            found = jnp.logical_or(found, keys_ref[seat_number] == block)
        solid_plane = jnp.where(seat == block, jnp.where(found, 0.0, 1.0), solid_plane)

    def own(channel, level):
        if channel == channels:
            return solid_plane
        return post_ref[level, :, channel, :]

    def moved(plane, shift):
        shift = shift % cells
        if shift == 0:
            return plane
        return pltpu.roll(plane, shift, 1)

    def gathered(channel, level, cx, cy):
        shift = cy * BE + cx
        entry = channel * levels + level
        first = front + entry * (TX + 2)
        first_column = front + entry * TY
        base = own(channel, level)
        if cy != 0:
            stepped = pltpu.roll(base, TX, 0)
            if cy == 1:
                halo = spread_ref[0, first + 1:first + 1 + blocks, :]
                yplane = jnp.where(py == 0, halo, stepped)
            else:
                halo = spread_ref[1, first + 1 - TX:first + 1 - TX + blocks, :]
                yplane = jnp.where(py == TY - 1, halo, stepped)

        def side_row(k, dx):
            corner_at = first if dx == 1 else first + TX + 1
            if k == 0:
                return spread_ref[0, corner_at:corner_at + 1, :]
            if k == TY + 1:
                return spread_ref[1, corner_at:corner_at + 1, :]
            at = first_column + k - 1
            return column_ref[0 if dx == 1 else 1, at:at + 1, :]

        def sideways(plane, dy, dx):
            plane = pltpu.roll(plane, dx % blocks, 0)
            edge = 0 if dx == 1 else TX - 1
            return jnp.where(
                seat == edge,
                side_row(1 - dy, dx),
                jnp.where(seat == edge + TX, side_row(2 - dy, dx), plane),
            )
        value = moved(base, shift)
        if cy != 0:
            ycross = r == (0 if cy == 1 else BE - 1)
            value = jnp.where(ycross, moved(yplane, shift), value)
        if cx != 0:
            xcross = q == (0 if cx == 1 else BE - 1)
            xvalue = moved(sideways(base, 0, cx), shift - BE * cx)
            if cy != 0:
                xvalue = jnp.where(ycross, moved(sideways(yplane, cy, cx), shift - BE * cx), xvalue)
            value = jnp.where(xcross, xvalue, value)
        return value

    blocked_of = {}
    for heading in range(27):
        cx, cy, cz = (int(v) for v in speeds[heading])
        if (cy == 0) != (part == 0):
            continue
        if (cx, cy) not in blocked_of:
            blocked_of[(cx, cy)] = gathered(channels, 0, cx, cy) > 0.5
        blocked = blocked_of[(cx, cy)]
        for level in range(levels):
            bounced = post_ref[level, :, 26 - heading, :]
            window = pl.ds(level * cells, cells)
            if cz == 1 and level == 0:
                result_ref[:, heading, window] = bounced
                continue
            if cz == 0:
                source = gathered(heading, level, cx, cy)
            elif cz == 1:
                source = gathered(heading, 0, cx, cy)
            elif level == 0:
                source = gathered(heading, 1, cx, cy)
            else:
                source = gathered(heading + 2, 1, cx, cy)
            result_ref[:, heading, window] = jnp.where(blocked, bounced, source)
    if part == 0:
        return
    chunks = levels * cells // 128
    for seat_number in range(keys_ref.shape[0]):
        key = keys_ref[seat_number]
        for chunk in range(chunks):
            picked = result_ref[jnp.maximum(key, 0), :, chunk * 128:(chunk + 1) * 128]
            rows = pl.ds(seat_number * channels * chunks + chunk, channels, stride=chunks)
            out_ref[rows, :] = jnp.where(key >= 0, picked, 0.0)


def stream(keys, post, below, above, from_left, from_right):
    channels, levels, blocks, cells = post.shape
    seats = keys.shape[0]
    row_count = below.shape[0]
    column_count = from_left.shape[0]
    vmem = pl.BlockSpec(memory_space=pltpu.VMEM)
    smem = pl.BlockSpec(memory_space=pltpu.SMEM)
    by_level = post.transpose(1, 2, 0, 3)
    partial = pl.pallas_call(
        level_steps_kernel,
        out_shape=jax.ShapeDtypeStruct((blocks, channels, levels * cells), jnp.float32),
        in_specs=[smem] + [vmem] * 3,
        out_specs=vmem,
        scratch_shapes=[pltpu.VMEM((2, column_count + 16, cells), jnp.float32)],
    )(keys, by_level, from_left, from_right)
    return pl.pallas_call(
        stream_kernel,
        out_shape=jax.ShapeDtypeStruct((seats * channels * levels * cells // 128, 128), jnp.float32),
        in_specs=[smem] + [vmem] * 6,
        out_specs=vmem,
        scratch_shapes=[
            pltpu.VMEM((2, row_count + 16, cells), jnp.float32),
            pltpu.VMEM((2, column_count + 16, cells), jnp.float32),
            pltpu.VMEM((blocks, channels, levels * cells), jnp.float32),
        ],
    )(keys, by_level, below, above, from_left, from_right, partial)


def on_device(
    scaled_distributions,
    remaining_brick_places,
    retained_wavenumbers,
    regional_amplitudes,
    relaxation_frequencies,
):
    forward, backward, speeds = lattice_tables()
    slot_state = scaled_distributions[0, 0]
    living_brick_keys = remaining_brick_places[0, 0]
    seats = living_brick_keys.shape[0]
    channels = slot_state.shape[1]
    cells = BE * BE
    levels = slot_state.shape[2] // cells
    blocks = TX * TY
    rows_tile = TY * BE
    cols_tile = TX * BE
    rows = slot_state.reshape(-1, 128)
    moments, wind = cell_moments(living_brick_keys, forward, rows, seats, levels)
    moments = moments.transpose(2, 0, 1, 3)
    line_length = lax.axis_size("line") * cols_tile
    own_columns = lax.axis_index("line") * cols_tile + jnp.arange(cols_tile, dtype=jnp.int32)
    mode_basis = mode_basis_at(retained_wavenumbers, own_columns, line_length).reshape(TX, BE, -1)
    partial = jnp.einsum(
        "kzyxrq,xqm->kzyrm", wind.reshape(3, levels, TY, TX, BE, BE), mode_basis,
        precision=HIGHEST,
    ).reshape(3, levels, rows_tile, -1)
    coefficients = butterfly_sum(partial, "line")
    misfit = regional_amplitudes - 2.0 / line_length * coefficients
    nudge = NUDGE_GAIN * jnp.einsum(
        "kzyrm,xqm->kzyxrq", misfit.reshape(3, levels, TY, BE, -1), mode_basis,
        precision=HIGHEST,
    ).reshape(3, levels, blocks, cells)
    post = collide_blocks(moments, wind, nudge, backward, relaxation_frequencies)
    present = jnp.any(living_brick_keys[None, :] == jnp.arange(blocks, dtype=jnp.int32)[:, None], axis=1)
    fluid = present.astype(jnp.float32)
    solid = jnp.broadcast_to((1.0 - fluid)[None, None, :, None], (1, levels, blocks, cells))
    extended = jnp.concatenate([post, solid], axis=0)
    width = channels + 1
    flat = lambda halo: halo.reshape(-1, BE)
    ahead, behind = ring_pairs("line")
    by_rows = extended.reshape(width, levels, TY, TX, BE, BE)
    column_shape = (width, levels, TY, BE)
    left_cols = lax.ppermute(flat(by_rows[:, :, :, TX - 1, :, BE - 1]), "line", ahead).reshape(column_shape)
    right_cols = lax.ppermute(flat(by_rows[:, :, :, 0, :, 0]), "line", behind).reshape(column_shape)
    corner = lambda cols, py, r: jnp.broadcast_to(cols[:, :, py:py + 1, r:r + 1], (width, levels, 1, BE))
    top_row = jnp.concatenate(
        [
            corner(left_cols, TY - 1, BE - 1),
            extended[:, :, blocks - TX:, cells - BE:],
            corner(right_cols, TY - 1, BE - 1),
        ],
        axis=2,
    )
    bottom_row = jnp.concatenate(
        [corner(left_cols, 0, 0), extended[:, :, :TX, :BE], corner(right_cols, 0, 0)], axis=2
    )
    ahead, behind = ring_pairs("curve")
    row_shape = (width, levels, TX + 2, BE)
    below = lax.ppermute(flat(top_row), "curve", ahead).reshape(row_shape)
    above = lax.ppermute(flat(bottom_row), "curve", behind).reshape(row_shape)
    below_flat = flat(below)
    above_flat = flat(above)
    from_left = flat(left_cols)
    from_right = flat(right_cols)
    new_state = stream(living_brick_keys, post, below_flat, above_flat, from_left, from_right)
    return new_state.reshape((1, 1, seats, channels, levels * cells))


def solution(mesh):
    return jax.shard_map(
        on_device,
        mesh=mesh,
        in_specs=(
            P("curve", "line", None, None, None),
            P("curve", "line", None),
            P(),
            P(None, None, "curve", None),
            P(),
        ),
        out_specs=P("curve", "line", None, None, None),
        check_vma=False,
    )
```

```python
import jax
import jax.numpy as jnp
import numpy as np
from jax import lax
from jax.experimental import pallas as pl
from jax.experimental.pallas import tpu as pltpu
from jax.sharding import PartitionSpec as P

BE = 16
TX = 4
TY = 2


NUDGE_GAIN = 0.5
TWO_PI = 6.283185307179586
HIGHEST = lax.Precision.HIGHEST


def butterfly_sum(value, axis):
    count = lax.axis_size(axis)
    stride = 1
    while stride < count:
        value = value + lax.ppermute(value, axis, [(i, i ^ stride) for i in range(count)])
        stride *= 2
    return value


def ring_pairs(axis):
    count = lax.axis_size(axis)
    forward = [(i, (i + 1) % count) for i in range(count)]
    backward = [(target, source) for source, target in forward]
    return forward, backward


def lattice_tables():
    one_weights = np.array([1.0 / 6.0, 2.0 / 3.0, 1.0 / 6.0])
    speeds = np.array(
        [
            [along_x - 1, along_y - 1, along_z - 1]
            for along_x in range(3)
            for along_y in range(3)
            for along_z in range(3)
        ]
    )
    weights = np.array(
        [
            one_weights[along_x] * one_weights[along_y] * one_weights[along_z]
            for along_x in range(3)
            for along_y in range(3)
            for along_z in range(3)
        ]
    )
    vander = np.array([[1.0, 1.0, 1.0], [-1.0, 0.0, 1.0], [1.0, 0.0, 1.0]])
    undo_vander = np.array([[0.0, -0.5, 0.5], [1.0, 0.0, -1.0], [0.0, 0.5, 0.5]])
    moment_matrix = np.kron(vander, np.kron(vander, vander))
    inverse = np.kron(undo_vander, np.kron(undo_vander, undo_vander))
    forward = jnp.asarray(moment_matrix * weights[None, :], dtype=jnp.float32)
    backward = jnp.asarray(inverse / weights[:, None], dtype=jnp.float32)
    return (forward, backward, speeds)


def mode_basis_at(mode_ids, positions, length):
    phase_ids = positions[:, None] * mode_ids[None, :] % length
    angles = phase_ids.astype(jnp.float32) * (TWO_PI / length)
    return jnp.concatenate([jnp.cos(angles), jnp.sin(angles)], axis=1)


def collide_blocks(moments, velocity, nudge, backward, relaxation_frequencies):
    density = moments[0]
    shifted = velocity + nudge
    powers = jnp.stack([jnp.ones_like(shifted), shifted, shifted * shifted + 1.0 / 3.0], axis=0)
    equilibrium = (
        density[None, None, None]
        * powers[:, None, None, 0]
        * powers[None, :, None, 1]
        * powers[None, None, :, 2]
    )
    equilibrium = equilibrium.reshape(moments.shape)
    relaxed = moments - relaxation_frequencies[:, None, None, None] * (moments - equilibrium)
    return jnp.einsum("ij,jzpl->izpl", backward, relaxed, precision=HIGHEST)


def moments_kernel(keys_ref, forward_ref, state_ref, out_ref, wind_ref, scratch_ref):
    levels, blocks, channels, cells = out_ref.shape
    seats = scratch_ref.shape[0]
    chunks = levels * cells // 128
    forward = forward_ref[...]
    for seat_number in range(seats):
        pieces = [
            state_ref[pl.ds(seat_number * channels * chunks + chunk, channels, stride=chunks), :]
            for chunk in range(chunks)
        ]
        scratch_ref[seat_number] = jnp.dot(
            forward, jnp.concatenate(pieces, axis=1), precision=HIGHEST,
            preferred_element_type=jnp.float32,
        )
    for block in range(blocks):
        slot = 0
        found = False
        for seat_number in range(seats):
            hit = keys_ref[seat_number] == block
            slot = jnp.where(hit, seat_number, slot)
            found = jnp.logical_or(found, hit)
        keep = jnp.where(found, 1.0, 0.0)
        for level in range(levels):
            values = scratch_ref[slot, :, level * cells:(level + 1) * cells] * keep
            out_ref[level, block] = values
            density = jnp.where(found, values[0:1], 1.0)
            for component, row in enumerate((9, 3, 1)):
                wind_ref[component, level, block:block + 1, :] = values[row:row + 1] / density


def cell_moments(keys, forward, rows, seats, levels):
    channels = forward.shape[0]
    blocks = TX * TY
    cells = rows.size // (seats * channels * levels)
    vmem = pl.BlockSpec(memory_space=pltpu.VMEM)
    smem = pl.BlockSpec(memory_space=pltpu.SMEM)
    return pl.pallas_call(
        moments_kernel,
        out_shape=(
            jax.ShapeDtypeStruct((levels, blocks, channels, cells), jnp.float32),
            jax.ShapeDtypeStruct((3, levels, blocks, cells), jnp.float32),
        ),
        in_specs=[smem, vmem, vmem],
        out_specs=(vmem, vmem),
        scratch_shapes=[pltpu.VMEM((seats, channels, levels * cells), jnp.float32)],
    )(keys, forward, rows)


def stream_kernel(
    keys_ref, post_ref, below_ref, above_ref, left_ref, right_ref, out_ref, spread_ref, column_ref, result_ref
):
    levels, blocks, channels, cells = post_ref.shape
    _, _, speeds = lattice_tables()
    front = 8
    grid_row = lax.broadcasted_iota(jnp.int32, (BE, cells), 0)
    grid_lane = lax.broadcasted_iota(jnp.int32, (BE, cells), 1)
    tile_copy = (grid_lane % BE == grid_row).astype(jnp.float32)
    group_copy = (grid_lane // BE == grid_row).astype(jnp.float32)
    row_count = below_ref.shape[0]
    column_count = left_ref.shape[0]
    for slot, source in enumerate((below_ref, above_ref)):
        spread_ref[slot, front:front + row_count, :] = jnp.dot(
            source[...], tile_copy, precision=HIGHEST, preferred_element_type=jnp.float32
        )
    for slot, source in enumerate((left_ref, right_ref)):
        column_ref[slot, front:front + column_count, :] = jnp.dot(
            source[...], group_copy, precision=HIGHEST, preferred_element_type=jnp.float32
        )
    lane = lax.broadcasted_iota(jnp.int32, (blocks, cells), 1)
    seat = lax.broadcasted_iota(jnp.int32, (blocks, cells), 0)
    q = lane % BE
    r = lane // BE
    py = seat // TX

    solid_plane = jnp.zeros((blocks, cells), jnp.float32)
    for block in range(blocks):
        found = False
        for seat_number in range(keys_ref.shape[0]):
            found = jnp.logical_or(found, keys_ref[seat_number] == block)
        solid_plane = jnp.where(seat == block, jnp.where(found, 0.0, 1.0), solid_plane)

    def own(channel, level):
        if channel == channels:
            return solid_plane
        return post_ref[level, :, channel, :]

    def moved(plane, shift):
        shift = shift % cells
        if shift == 0:
            return plane
        return pltpu.roll(plane, shift, 1)

    def gathered(channel, level, cx, cy):
        shift = cy * BE + cx
        entry = channel * levels + level
        first = front + entry * (TX + 2)
        first_column = front + entry * TY
        base = own(channel, level)
        if cy != 0:
            stepped = pltpu.roll(base, TX, 0)
            if cy == 1:
                halo = spread_ref[0, first + 1:first + 1 + blocks, :]
                yplane = jnp.where(py == 0, halo, stepped)
            else:
                halo = spread_ref[1, first + 1 - TX:first + 1 - TX + blocks, :]
                yplane = jnp.where(py == TY - 1, halo, stepped)

        def side_row(k, dx):
            corner_at = first if dx == 1 else first + TX + 1
            if k == 0:
                return spread_ref[0, corner_at:corner_at + 1, :]
            if k == TY + 1:
                return spread_ref[1, corner_at:corner_at + 1, :]
            at = first_column + k - 1
            return column_ref[0 if dx == 1 else 1, at:at + 1, :]

        def sideways(plane, dy, dx):
            plane = pltpu.roll(plane, dx % blocks, 0)
            edge = 0 if dx == 1 else TX - 1
            return jnp.where(
                seat == edge,
                side_row(1 - dy, dx),
                jnp.where(seat == edge + TX, side_row(2 - dy, dx), plane),
            )
        value = moved(base, shift)
        if cy != 0:
            ycross = r == (0 if cy == 1 else BE - 1)
            value = jnp.where(ycross, moved(yplane, shift), value)
        if cx != 0:
            xcross = q == (0 if cx == 1 else BE - 1)
            xvalue = moved(sideways(base, 0, cx), shift - BE * cx)
            if cy != 0:
                xvalue = jnp.where(ycross, moved(sideways(yplane, cy, cx), shift - BE * cx), xvalue)
            value = jnp.where(xcross, xvalue, value)
        return value

    blocked_of = {}
    for cx in (-1, 0, 1):
        for cy in (-1, 0, 1):
            blocked_of[(cx, cy)] = gathered(channels, 0, cx, cy) > 0.5
    for heading in range(27):
        cx, cy, cz = (int(v) for v in speeds[heading])
        blocked = blocked_of[(cx, cy)]
        for level in range(levels):
            bounced = post_ref[level, :, 26 - heading, :]
            window = pl.ds(level * cells, cells)
            if cz == 1 and level == 0:
                result_ref[:, heading, window] = bounced
                continue
            if cz == 0:
                source = gathered(heading, level, cx, cy)
            elif cz == 1:
                source = gathered(heading, 0, cx, cy)
            elif level == 0:
                source = gathered(heading, 1, cx, cy)
            else:
                source = gathered(heading + 2, 1, cx, cy)
            result_ref[:, heading, window] = jnp.where(blocked, bounced, source)
    chunks = levels * cells // 128
    for seat_number in range(keys_ref.shape[0]):
        key = keys_ref[seat_number]
        for chunk in range(chunks):
            picked = result_ref[jnp.maximum(key, 0), :, chunk * 128:(chunk + 1) * 128]
            rows = pl.ds(seat_number * channels * chunks + chunk, channels, stride=chunks)
            out_ref[rows, :] = jnp.where(key >= 0, picked, 0.0)


def stream(keys, post, below, above, from_left, from_right):
    channels, levels, blocks, cells = post.shape
    seats = keys.shape[0]
    row_count = below.shape[0]
    column_count = from_left.shape[0]
    vmem = pl.BlockSpec(memory_space=pltpu.VMEM)
    smem = pl.BlockSpec(memory_space=pltpu.SMEM)
    return pl.pallas_call(
        stream_kernel,
        out_shape=jax.ShapeDtypeStruct((seats * channels * levels * cells // 128, 128), jnp.float32),
        in_specs=[smem] + [vmem] * 5,
        out_specs=vmem,
        scratch_shapes=[
            pltpu.VMEM((2, row_count + 16, cells), jnp.float32),
            pltpu.VMEM((2, column_count + 16, cells), jnp.float32),
            pltpu.VMEM((blocks, channels, levels * cells), jnp.float32),
        ],
    )(keys, post.transpose(1, 2, 0, 3), below, above, from_left, from_right)


def on_device(
    scaled_distributions,
    remaining_brick_places,
    retained_wavenumbers,
    regional_amplitudes,
    relaxation_frequencies,
):
    forward, backward, speeds = lattice_tables()
    slot_state = scaled_distributions[0, 0]
    living_brick_keys = remaining_brick_places[0, 0]
    seats = living_brick_keys.shape[0]
    channels = slot_state.shape[1]
    cells = BE * BE
    levels = slot_state.shape[2] // cells
    blocks = TX * TY
    rows_tile = TY * BE
    cols_tile = TX * BE
    rows = slot_state.reshape(-1, 128)
    moments, wind = cell_moments(living_brick_keys, forward, rows, seats, levels)
    moments = moments.transpose(2, 0, 1, 3)
    line_length = lax.axis_size("line") * cols_tile
    own_columns = lax.axis_index("line") * cols_tile + jnp.arange(cols_tile, dtype=jnp.int32)
    mode_basis = mode_basis_at(retained_wavenumbers, own_columns, line_length).reshape(TX, BE, -1)
    partial = jnp.einsum(
        "kzyxrq,xqm->kzyrm", wind.reshape(3, levels, TY, TX, BE, BE), mode_basis,
        precision=lax.Precision.HIGH,
    ).reshape(3, levels, rows_tile, -1)
    coefficients = butterfly_sum(partial, "line")
    misfit = regional_amplitudes - 2.0 / line_length * coefficients
    nudge = NUDGE_GAIN * jnp.einsum(
        "kzyrm,xqm->kzyxrq", misfit.reshape(3, levels, TY, BE, -1), mode_basis,
        precision=lax.Precision.HIGH,
    ).reshape(3, levels, blocks, cells)
    post = collide_blocks(moments, wind, nudge, backward, relaxation_frequencies)
    present = jnp.any(living_brick_keys[None, :] == jnp.arange(blocks, dtype=jnp.int32)[:, None], axis=1)
    fluid = present.astype(jnp.float32)
    solid = jnp.broadcast_to((1.0 - fluid)[None, None, :, None], (1, levels, blocks, cells))
    extended = jnp.concatenate([post, solid], axis=0)
    width = channels + 1
    flat = lambda halo: halo.reshape(-1, BE)
    ahead, behind = ring_pairs("line")
    by_rows = extended.reshape(width, levels, TY, TX, BE, BE)
    column_shape = (width, levels, TY, BE)
    left_cols = lax.ppermute(flat(by_rows[:, :, :, TX - 1, :, BE - 1]), "line", ahead).reshape(column_shape)
    right_cols = lax.ppermute(flat(by_rows[:, :, :, 0, :, 0]), "line", behind).reshape(column_shape)
    corner = lambda cols, py, r: jnp.broadcast_to(cols[:, :, py:py + 1, r:r + 1], (width, levels, 1, BE))
    top_row = jnp.concatenate(
        [
            corner(left_cols, TY - 1, BE - 1),
            extended[:, :, blocks - TX:, cells - BE:],
            corner(right_cols, TY - 1, BE - 1),
        ],
        axis=2,
    )
    bottom_row = jnp.concatenate(
        [corner(left_cols, 0, 0), extended[:, :, :TX, :BE], corner(right_cols, 0, 0)], axis=2
    )
    ahead, behind = ring_pairs("curve")
    row_shape = (width, levels, TX + 2, BE)
    below = lax.ppermute(flat(top_row), "curve", ahead).reshape(row_shape)
    above = lax.ppermute(flat(bottom_row), "curve", behind).reshape(row_shape)
    below_flat = flat(below)
    above_flat = flat(above)
    from_left = flat(left_cols)
    from_right = flat(right_cols)
    new_state = stream(living_brick_keys, post, below_flat, above_flat, from_left, from_right)
    return new_state.reshape((1, 1, seats, channels, levels * cells))


def solution(mesh):
    return jax.shard_map(
        on_device,
        mesh=mesh,
        in_specs=(
            P("curve", "line", None, None, None),
            P("curve", "line", None),
            P(),
            P(None, None, "curve", None),
            P(),
        ),
        out_specs=P("curve", "line", None, None, None),
        check_vma=False,
    )
```

```python
import jax
import jax.numpy as jnp
import numpy as np
from jax import lax
from jax.experimental import pallas as pl
from jax.experimental.pallas import tpu as pltpu
from jax.sharding import PartitionSpec as P

BE = 16
TX = 4
TY = 2


NUDGE_GAIN = 0.5
TWO_PI = 6.283185307179586
HIGHEST = lax.Precision.HIGHEST


def butterfly_sum(value, axis):
    count = lax.axis_size(axis)
    stride = 1
    while stride < count:
        value = value + lax.ppermute(value, axis, [(i, i ^ stride) for i in range(count)])
        stride *= 2
    return value


def ring_pairs(axis):
    count = lax.axis_size(axis)
    forward = [(i, (i + 1) % count) for i in range(count)]
    backward = [(target, source) for source, target in forward]
    return forward, backward


def lattice_tables():
    one_weights = np.array([1.0 / 6.0, 2.0 / 3.0, 1.0 / 6.0])
    speeds = np.array(
        [
            [along_x - 1, along_y - 1, along_z - 1]
            for along_x in range(3)
            for along_y in range(3)
            for along_z in range(3)
        ]
    )
    weights = np.array(
        [
            one_weights[along_x] * one_weights[along_y] * one_weights[along_z]
            for along_x in range(3)
            for along_y in range(3)
            for along_z in range(3)
        ]
    )
    vander = np.array([[1.0, 1.0, 1.0], [-1.0, 0.0, 1.0], [1.0, 0.0, 1.0]])
    undo_vander = np.array([[0.0, -0.5, 0.5], [1.0, 0.0, -1.0], [0.0, 0.5, 0.5]])
    moment_matrix = np.kron(vander, np.kron(vander, vander))
    inverse = np.kron(undo_vander, np.kron(undo_vander, undo_vander))
    forward = jnp.asarray(moment_matrix * weights[None, :], dtype=jnp.float32)
    backward = jnp.asarray(inverse / weights[:, None], dtype=jnp.float32)
    return (forward, backward, speeds)


def mode_basis_at(mode_ids, positions, length):
    phase_ids = positions[:, None] * mode_ids[None, :] % length
    angles = phase_ids.astype(jnp.float32) * (TWO_PI / length)
    return jnp.concatenate([jnp.cos(angles), jnp.sin(angles)], axis=1)


def collide_blocks(moments, velocity, nudge, backward, relaxation_frequencies):
    density = moments[0]
    shifted = velocity + nudge
    powers = jnp.stack([jnp.ones_like(shifted), shifted, shifted * shifted + 1.0 / 3.0], axis=0)
    equilibrium = (
        density[None, None, None]
        * powers[:, None, None, 0]
        * powers[None, :, None, 1]
        * powers[None, None, :, 2]
    )
    equilibrium = equilibrium.reshape(moments.shape)
    relaxed = moments - relaxation_frequencies[:, None, None, None] * (moments - equilibrium)
    return jnp.einsum("ij,jzpl->izpl", backward, relaxed, precision=HIGHEST)


def moments_kernel(keys_ref, forward_ref, state_ref, out_ref, wind_ref, scratch_ref):
    levels, blocks, channels, cells = out_ref.shape
    seats = scratch_ref.shape[0]
    chunks = levels * cells // 128
    forward = forward_ref[...]
    for seat_number in range(seats):
        pieces = [
            state_ref[pl.ds(seat_number * channels * chunks + chunk, channels, stride=chunks), :]
            for chunk in range(chunks)
        ]
        scratch_ref[seat_number] = jnp.dot(
            forward, jnp.concatenate(pieces, axis=1), precision=HIGHEST,
            preferred_element_type=jnp.float32,
        )
    for block in range(blocks):
        slot = 0
        found = False
        for seat_number in range(seats):
            hit = keys_ref[seat_number] == block
            slot = jnp.where(hit, seat_number, slot)
            found = jnp.logical_or(found, hit)
        keep = jnp.where(found, 1.0, 0.0)
        for level in range(levels):
            values = scratch_ref[slot, :, level * cells:(level + 1) * cells] * keep
            out_ref[level, block] = values
            density = jnp.where(found, values[0:1], 1.0)
            for component, row in enumerate((9, 3, 1)):
                wind_ref[component, level, block:block + 1, :] = values[row:row + 1] / density


def cell_moments(keys, forward, rows, seats, levels):
    channels = forward.shape[0]
    blocks = TX * TY
    cells = rows.size // (seats * channels * levels)
    vmem = pl.BlockSpec(memory_space=pltpu.VMEM)
    smem = pl.BlockSpec(memory_space=pltpu.SMEM)
    return pl.pallas_call(
        moments_kernel,
        out_shape=(
            jax.ShapeDtypeStruct((levels, blocks, channels, cells), jnp.float32),
            jax.ShapeDtypeStruct((3, levels, blocks, cells), jnp.float32),
        ),
        in_specs=[smem, vmem, vmem],
        out_specs=(vmem, vmem),
        scratch_shapes=[pltpu.VMEM((seats, channels, levels * cells), jnp.float32)],
    )(keys, forward, rows)


def stream_kernel(
    keys_ref, post_ref, below_ref, above_ref, left_ref, right_ref, out_ref, spread_ref, column_ref, result_ref
):
    levels, blocks, channels, cells = post_ref.shape
    _, _, speeds = lattice_tables()
    front = 8
    grid_row = lax.broadcasted_iota(jnp.int32, (BE, cells), 0)
    grid_lane = lax.broadcasted_iota(jnp.int32, (BE, cells), 1)
    tile_copy = (grid_lane % BE == grid_row).astype(jnp.float32)
    group_copy = (grid_lane // BE == grid_row).astype(jnp.float32)
    row_count = below_ref.shape[0]
    column_count = left_ref.shape[0]
    for slot, source in enumerate((below_ref, above_ref)):
        spread_ref[slot, front:front + row_count, :] = jnp.dot(
            source[...], tile_copy, precision=lax.Precision.HIGH, preferred_element_type=jnp.float32
        )
    for slot, source in enumerate((left_ref, right_ref)):
        column_ref[slot, front:front + column_count, :] = jnp.dot(
            source[...], group_copy, precision=lax.Precision.HIGH, preferred_element_type=jnp.float32
        )
    lane = lax.broadcasted_iota(jnp.int32, (blocks, cells), 1)
    seat = lax.broadcasted_iota(jnp.int32, (blocks, cells), 0)
    q = lane % BE
    r = lane // BE
    py = seat // TX

    solid_plane = jnp.zeros((blocks, cells), jnp.float32)
    for block in range(blocks):
        found = False
        for seat_number in range(keys_ref.shape[0]):
            found = jnp.logical_or(found, keys_ref[seat_number] == block)
        solid_plane = jnp.where(seat == block, jnp.where(found, 0.0, 1.0), solid_plane)

    def own(channel, level):
        if channel == channels:
            return solid_plane
        return post_ref[level, :, channel, :]

    def moved(plane, shift):
        shift = shift % cells
        if shift == 0:
            return plane
        return pltpu.roll(plane, shift, 1)

    def gathered(channel, level, cx, cy):
        shift = cy * BE + cx
        entry = channel * levels + level
        first = front + entry * (TX + 2)
        first_column = front + entry * TY
        base = own(channel, level)
        if cy != 0:
            stepped = pltpu.roll(base, TX, 0)
            if cy == 1:
                halo = spread_ref[0, first + 1:first + 1 + blocks, :]
                yplane = jnp.where(py == 0, halo, stepped)
            else:
                halo = spread_ref[1, first + 1 - TX:first + 1 - TX + blocks, :]
                yplane = jnp.where(py == TY - 1, halo, stepped)

        def side_row(k, dx):
            corner_at = first if dx == 1 else first + TX + 1
            if k == 0:
                return spread_ref[0, corner_at:corner_at + 1, :]
            if k == TY + 1:
                return spread_ref[1, corner_at:corner_at + 1, :]
            at = first_column + k - 1
            return column_ref[0 if dx == 1 else 1, at:at + 1, :]

        def sideways(plane, dy, dx):
            plane = pltpu.roll(plane, dx % blocks, 0)
            edge = 0 if dx == 1 else TX - 1
            return jnp.where(
                seat == edge,
                side_row(1 - dy, dx),
                jnp.where(seat == edge + TX, side_row(2 - dy, dx), plane),
            )
        value = moved(base, shift)
        if cy != 0:
            ycross = r == (0 if cy == 1 else BE - 1)
            value = jnp.where(ycross, moved(yplane, shift), value)
        if cx != 0:
            xcross = q == (0 if cx == 1 else BE - 1)
            xvalue = moved(sideways(base, 0, cx), shift - BE * cx)
            if cy != 0:
                xvalue = jnp.where(ycross, moved(sideways(yplane, cy, cx), shift - BE * cx), xvalue)
            value = jnp.where(xcross, xvalue, value)
        return value

    blocked_of = {}
    for cx in (-1, 0, 1):
        for cy in (-1, 0, 1):
            blocked_of[(cx, cy)] = gathered(channels, 0, cx, cy) > 0.5
    for heading in range(27):
        cx, cy, cz = (int(v) for v in speeds[heading])
        blocked = blocked_of[(cx, cy)]
        for level in range(levels):
            bounced = post_ref[level, :, 26 - heading, :]
            window = pl.ds(level * cells, cells)
            if cz == 1 and level == 0:
                result_ref[:, heading, window] = bounced
                continue
            if cz == 0:
                source = gathered(heading, level, cx, cy)
            elif cz == 1:
                source = gathered(heading, 0, cx, cy)
            elif level == 0:
                source = gathered(heading, 1, cx, cy)
            else:
                source = gathered(heading + 2, 1, cx, cy)
            result_ref[:, heading, window] = jnp.where(blocked, bounced, source)
    chunks = levels * cells // 128
    for seat_number in range(keys_ref.shape[0]):
        key = keys_ref[seat_number]
        for chunk in range(chunks):
            picked = result_ref[jnp.maximum(key, 0), :, chunk * 128:(chunk + 1) * 128]
            rows = pl.ds(seat_number * channels * chunks + chunk, channels, stride=chunks)
            out_ref[rows, :] = jnp.where(key >= 0, picked, 0.0)


def stream(keys, post, below, above, from_left, from_right):
    channels, levels, blocks, cells = post.shape
    seats = keys.shape[0]
    row_count = below.shape[0]
    column_count = from_left.shape[0]
    vmem = pl.BlockSpec(memory_space=pltpu.VMEM)
    smem = pl.BlockSpec(memory_space=pltpu.SMEM)
    return pl.pallas_call(
        stream_kernel,
        out_shape=jax.ShapeDtypeStruct((seats * channels * levels * cells // 128, 128), jnp.float32),
        in_specs=[smem] + [vmem] * 5,
        out_specs=vmem,
        scratch_shapes=[
            pltpu.VMEM((2, row_count + 16, cells), jnp.float32),
            pltpu.VMEM((2, column_count + 16, cells), jnp.float32),
            pltpu.VMEM((blocks, channels, levels * cells), jnp.float32),
        ],
    )(keys, post.transpose(1, 2, 0, 3), below, above, from_left, from_right)


def on_device(
    scaled_distributions,
    remaining_brick_places,
    retained_wavenumbers,
    regional_amplitudes,
    relaxation_frequencies,
):
    forward, backward, speeds = lattice_tables()
    slot_state = scaled_distributions[0, 0]
    living_brick_keys = remaining_brick_places[0, 0]
    seats = living_brick_keys.shape[0]
    channels = slot_state.shape[1]
    cells = BE * BE
    levels = slot_state.shape[2] // cells
    blocks = TX * TY
    rows_tile = TY * BE
    cols_tile = TX * BE
    rows = slot_state.reshape(-1, 128)
    moments, wind = cell_moments(living_brick_keys, forward, rows, seats, levels)
    moments = moments.transpose(2, 0, 1, 3)
    line_length = lax.axis_size("line") * cols_tile
    own_columns = lax.axis_index("line") * cols_tile + jnp.arange(cols_tile, dtype=jnp.int32)
    mode_basis = mode_basis_at(retained_wavenumbers, own_columns, line_length).reshape(TX, BE, -1)
    partial = jnp.einsum(
        "kzyxrq,xqm->kzyrm", wind.reshape(3, levels, TY, TX, BE, BE), mode_basis,
        precision=lax.Precision.HIGH,
    ).reshape(3, levels, rows_tile, -1)
    coefficients = butterfly_sum(partial, "line")
    misfit = regional_amplitudes - 2.0 / line_length * coefficients
    nudge = NUDGE_GAIN * jnp.einsum(
        "kzyrm,xqm->kzyxrq", misfit.reshape(3, levels, TY, BE, -1), mode_basis,
        precision=lax.Precision.HIGH,
    ).reshape(3, levels, blocks, cells)
    post = collide_blocks(moments, wind, nudge, backward, relaxation_frequencies)
    present = jnp.any(living_brick_keys[None, :] == jnp.arange(blocks, dtype=jnp.int32)[:, None], axis=1)
    fluid = present.astype(jnp.float32)
    solid = jnp.broadcast_to((1.0 - fluid)[None, None, :, None], (1, levels, blocks, cells))
    extended = jnp.concatenate([post, solid], axis=0)
    width = channels + 1
    flat = lambda halo: halo.reshape(-1, BE)
    ahead, behind = ring_pairs("line")
    by_rows = extended.reshape(width, levels, TY, TX, BE, BE)
    column_shape = (width, levels, TY, BE)
    left_cols = lax.ppermute(flat(by_rows[:, :, :, TX - 1, :, BE - 1]), "line", ahead).reshape(column_shape)
    right_cols = lax.ppermute(flat(by_rows[:, :, :, 0, :, 0]), "line", behind).reshape(column_shape)
    corner = lambda cols, py, r: jnp.broadcast_to(cols[:, :, py:py + 1, r:r + 1], (width, levels, 1, BE))
    top_row = jnp.concatenate(
        [
            corner(left_cols, TY - 1, BE - 1),
            extended[:, :, blocks - TX:, cells - BE:],
            corner(right_cols, TY - 1, BE - 1),
        ],
        axis=2,
    )
    bottom_row = jnp.concatenate(
        [corner(left_cols, 0, 0), extended[:, :, :TX, :BE], corner(right_cols, 0, 0)], axis=2
    )
    ahead, behind = ring_pairs("curve")
    row_shape = (width, levels, TX + 2, BE)
    below = lax.ppermute(flat(top_row), "curve", ahead).reshape(row_shape)
    above = lax.ppermute(flat(bottom_row), "curve", behind).reshape(row_shape)
    below_flat = flat(below)
    above_flat = flat(above)
    from_left = flat(left_cols)
    from_right = flat(right_cols)
    new_state = stream(living_brick_keys, post, below_flat, above_flat, from_left, from_right)
    return new_state.reshape((1, 1, seats, channels, levels * cells))


def solution(mesh):
    return jax.shard_map(
        on_device,
        mesh=mesh,
        in_specs=(
            P("curve", "line", None, None, None),
            P("curve", "line", None),
            P(),
            P(None, None, "curve", None),
            P(),
        ),
        out_specs=P("curve", "line", None, None, None),
        check_vma=False,
    )
```

```python
import jax
import jax.numpy as jnp
import numpy as np
from jax import lax
from jax.experimental import pallas as pl
from jax.experimental.pallas import tpu as pltpu
from jax.sharding import PartitionSpec as P

BE = 16
TX = 4
TY = 2


NUDGE_GAIN = 0.5
TWO_PI = 6.283185307179586
HIGHEST = lax.Precision.HIGHEST


def butterfly_sum(value, axis):
    count = lax.axis_size(axis)
    stride = 1
    while stride < count:
        value = value + lax.ppermute(value, axis, [(i, i ^ stride) for i in range(count)])
        stride *= 2
    return value


def ring_pairs(axis):
    count = lax.axis_size(axis)
    forward = [(i, (i + 1) % count) for i in range(count)]
    backward = [(target, source) for source, target in forward]
    return forward, backward


def lattice_tables():
    one_weights = np.array([1.0 / 6.0, 2.0 / 3.0, 1.0 / 6.0])
    speeds = np.array(
        [
            [along_x - 1, along_y - 1, along_z - 1]
            for along_x in range(3)
            for along_y in range(3)
            for along_z in range(3)
        ]
    )
    weights = np.array(
        [
            one_weights[along_x] * one_weights[along_y] * one_weights[along_z]
            for along_x in range(3)
            for along_y in range(3)
            for along_z in range(3)
        ]
    )
    vander = np.array([[1.0, 1.0, 1.0], [-1.0, 0.0, 1.0], [1.0, 0.0, 1.0]])
    undo_vander = np.array([[0.0, -0.5, 0.5], [1.0, 0.0, -1.0], [0.0, 0.5, 0.5]])
    moment_matrix = np.kron(vander, np.kron(vander, vander))
    inverse = np.kron(undo_vander, np.kron(undo_vander, undo_vander))
    forward = jnp.asarray(moment_matrix * weights[None, :], dtype=jnp.float32)
    backward = jnp.asarray(inverse / weights[:, None], dtype=jnp.float32)
    return (forward, backward, speeds)


def mode_basis_at(mode_ids, positions, length):
    phase_ids = positions[:, None] * mode_ids[None, :] % length
    angles = phase_ids.astype(jnp.float32) * (TWO_PI / length)
    return jnp.concatenate([jnp.cos(angles), jnp.sin(angles)], axis=1)


def collide_blocks(moments, velocity, nudge, backward, relaxation_frequencies):
    density = moments[0]
    shifted = velocity + nudge
    powers = jnp.stack([jnp.ones_like(shifted), shifted, shifted * shifted + 1.0 / 3.0], axis=0)
    equilibrium = (
        density[None, None, None]
        * powers[:, None, None, 0]
        * powers[None, :, None, 1]
        * powers[None, None, :, 2]
    )
    equilibrium = equilibrium.reshape(moments.shape)
    relaxed = moments - relaxation_frequencies[:, None, None, None] * (moments - equilibrium)
    return jnp.einsum("ij,jzpl->izpl", backward, relaxed, precision=lax.Precision.HIGH)


def moments_kernel(keys_ref, forward_ref, state_ref, out_ref, wind_ref, scratch_ref):
    levels, blocks, channels, cells = out_ref.shape
    seats = scratch_ref.shape[0]
    chunks = levels * cells // 128
    forward = forward_ref[...]
    for seat_number in range(seats):
        pieces = [
            state_ref[pl.ds(seat_number * channels * chunks + chunk, channels, stride=chunks), :]
            for chunk in range(chunks)
        ]
        scratch_ref[seat_number] = jnp.dot(
            forward, jnp.concatenate(pieces, axis=1), precision=HIGHEST,
            preferred_element_type=jnp.float32,
        )
    for block in range(blocks):
        slot = 0
        found = False
        for seat_number in range(seats):
            hit = keys_ref[seat_number] == block
            slot = jnp.where(hit, seat_number, slot)
            found = jnp.logical_or(found, hit)
        keep = jnp.where(found, 1.0, 0.0)
        for level in range(levels):
            values = scratch_ref[slot, :, level * cells:(level + 1) * cells] * keep
            out_ref[level, block] = values
            density = jnp.where(found, values[0:1], 1.0)
            for component, row in enumerate((9, 3, 1)):
                wind_ref[component, level, block:block + 1, :] = values[row:row + 1] / density


def cell_moments(keys, forward, rows, seats, levels):
    channels = forward.shape[0]
    blocks = TX * TY
    cells = rows.size // (seats * channels * levels)
    vmem = pl.BlockSpec(memory_space=pltpu.VMEM)
    smem = pl.BlockSpec(memory_space=pltpu.SMEM)
    return pl.pallas_call(
        moments_kernel,
        out_shape=(
            jax.ShapeDtypeStruct((levels, blocks, channels, cells), jnp.float32),
            jax.ShapeDtypeStruct((3, levels, blocks, cells), jnp.float32),
        ),
        in_specs=[smem, vmem, vmem],
        out_specs=(vmem, vmem),
        scratch_shapes=[pltpu.VMEM((seats, channels, levels * cells), jnp.float32)],
    )(keys, forward, rows)


def stream_kernel(
    keys_ref, post_ref, below_ref, above_ref, left_ref, right_ref, out_ref, spread_ref, column_ref, result_ref
):
    levels, blocks, channels, cells = post_ref.shape
    _, _, speeds = lattice_tables()
    front = 8
    grid_row = lax.broadcasted_iota(jnp.int32, (BE, cells), 0)
    grid_lane = lax.broadcasted_iota(jnp.int32, (BE, cells), 1)
    tile_copy = (grid_lane % BE == grid_row).astype(jnp.float32)
    group_copy = (grid_lane // BE == grid_row).astype(jnp.float32)
    row_count = below_ref.shape[0]
    column_count = left_ref.shape[0]
    for slot, source in enumerate((below_ref, above_ref)):
        spread_ref[slot, front:front + row_count, :] = jnp.dot(
            source[...], tile_copy, precision=lax.Precision.HIGH, preferred_element_type=jnp.float32
        )
    for slot, source in enumerate((left_ref, right_ref)):
        column_ref[slot, front:front + column_count, :] = jnp.dot(
            source[...], group_copy, precision=lax.Precision.HIGH, preferred_element_type=jnp.float32
        )
    lane = lax.broadcasted_iota(jnp.int32, (blocks, cells), 1)
    seat = lax.broadcasted_iota(jnp.int32, (blocks, cells), 0)
    q = lane % BE
    r = lane // BE
    py = seat // TX

    solid_plane = jnp.zeros((blocks, cells), jnp.float32)
    for block in range(blocks):
        found = False
        for seat_number in range(keys_ref.shape[0]):
            found = jnp.logical_or(found, keys_ref[seat_number] == block)
        solid_plane = jnp.where(seat == block, jnp.where(found, 0.0, 1.0), solid_plane)

    def own(channel, level):
        if channel == channels:
            return solid_plane
        return post_ref[level, :, channel, :]

    def moved(plane, shift):
        shift = shift % cells
        if shift == 0:
            return plane
        return pltpu.roll(plane, shift, 1)

    def gathered(channel, level, cx, cy):
        shift = cy * BE + cx
        entry = channel * levels + level
        first = front + entry * (TX + 2)
        first_column = front + entry * TY
        base = own(channel, level)
        if cy != 0:
            stepped = pltpu.roll(base, TX, 0)
            if cy == 1:
                halo = spread_ref[0, first + 1:first + 1 + blocks, :]
                yplane = jnp.where(py == 0, halo, stepped)
            else:
                halo = spread_ref[1, first + 1 - TX:first + 1 - TX + blocks, :]
                yplane = jnp.where(py == TY - 1, halo, stepped)

        def side_row(k, dx):
            corner_at = first if dx == 1 else first + TX + 1
            if k == 0:
                return spread_ref[0, corner_at:corner_at + 1, :]
            if k == TY + 1:
                return spread_ref[1, corner_at:corner_at + 1, :]
            at = first_column + k - 1
            return column_ref[0 if dx == 1 else 1, at:at + 1, :]

        def sideways(plane, dy, dx):
            plane = pltpu.roll(plane, dx % blocks, 0)
            edge = 0 if dx == 1 else TX - 1
            return jnp.where(
                seat == edge,
                side_row(1 - dy, dx),
                jnp.where(seat == edge + TX, side_row(2 - dy, dx), plane),
            )
        value = moved(base, shift)
        if cy != 0:
            ycross = r == (0 if cy == 1 else BE - 1)
            value = jnp.where(ycross, moved(yplane, shift), value)
        if cx != 0:
            xcross = q == (0 if cx == 1 else BE - 1)
            xvalue = moved(sideways(base, 0, cx), shift - BE * cx)
            if cy != 0:
                xvalue = jnp.where(ycross, moved(sideways(yplane, cy, cx), shift - BE * cx), xvalue)
            value = jnp.where(xcross, xvalue, value)
        return value

    blocked_of = {}
    for cx in (-1, 0, 1):
        for cy in (-1, 0, 1):
            blocked_of[(cx, cy)] = gathered(channels, 0, cx, cy) > 0.5
    for heading in range(27):
        cx, cy, cz = (int(v) for v in speeds[heading])
        blocked = blocked_of[(cx, cy)]
        for level in range(levels):
            bounced = post_ref[level, :, 26 - heading, :]
            window = pl.ds(level * cells, cells)
            if cz == 1 and level == 0:
                result_ref[:, heading, window] = bounced
                continue
            if cz == 0:
                source = gathered(heading, level, cx, cy)
            elif cz == 1:
                source = gathered(heading, 0, cx, cy)
            elif level == 0:
                source = gathered(heading, 1, cx, cy)
            else:
                source = gathered(heading + 2, 1, cx, cy)
            result_ref[:, heading, window] = jnp.where(blocked, bounced, source)
    chunks = levels * cells // 128
    for seat_number in range(keys_ref.shape[0]):
        key = keys_ref[seat_number]
        for chunk in range(chunks):
            picked = result_ref[jnp.maximum(key, 0), :, chunk * 128:(chunk + 1) * 128]
            rows = pl.ds(seat_number * channels * chunks + chunk, channels, stride=chunks)
            out_ref[rows, :] = jnp.where(key >= 0, picked, 0.0)


def stream(keys, post, below, above, from_left, from_right):
    channels, levels, blocks, cells = post.shape
    seats = keys.shape[0]
    row_count = below.shape[0]
    column_count = from_left.shape[0]
    vmem = pl.BlockSpec(memory_space=pltpu.VMEM)
    smem = pl.BlockSpec(memory_space=pltpu.SMEM)
    return pl.pallas_call(
        stream_kernel,
        out_shape=jax.ShapeDtypeStruct((seats * channels * levels * cells // 128, 128), jnp.float32),
        in_specs=[smem] + [vmem] * 5,
        out_specs=vmem,
        scratch_shapes=[
            pltpu.VMEM((2, row_count + 16, cells), jnp.float32),
            pltpu.VMEM((2, column_count + 16, cells), jnp.float32),
            pltpu.VMEM((blocks, channels, levels * cells), jnp.float32),
        ],
    )(keys, post.transpose(1, 2, 0, 3), below, above, from_left, from_right)


def on_device(
    scaled_distributions,
    remaining_brick_places,
    retained_wavenumbers,
    regional_amplitudes,
    relaxation_frequencies,
):
    forward, backward, speeds = lattice_tables()
    slot_state = scaled_distributions[0, 0]
    living_brick_keys = remaining_brick_places[0, 0]
    seats = living_brick_keys.shape[0]
    channels = slot_state.shape[1]
    cells = BE * BE
    levels = slot_state.shape[2] // cells
    blocks = TX * TY
    rows_tile = TY * BE
    cols_tile = TX * BE
    rows = slot_state.reshape(-1, 128)
    moments, wind = cell_moments(living_brick_keys, forward, rows, seats, levels)
    moments = moments.transpose(2, 0, 1, 3)
    line_length = lax.axis_size("line") * cols_tile
    own_columns = lax.axis_index("line") * cols_tile + jnp.arange(cols_tile, dtype=jnp.int32)
    mode_basis = mode_basis_at(retained_wavenumbers, own_columns, line_length).reshape(TX, BE, -1)
    partial = jnp.einsum(
        "kzyxrq,xqm->kzyrm", wind.reshape(3, levels, TY, TX, BE, BE), mode_basis,
        precision=lax.Precision.HIGH,
    ).reshape(3, levels, rows_tile, -1)
    coefficients = butterfly_sum(partial, "line")
    misfit = regional_amplitudes - 2.0 / line_length * coefficients
    nudge = NUDGE_GAIN * jnp.einsum(
        "kzyrm,xqm->kzyxrq", misfit.reshape(3, levels, TY, BE, -1), mode_basis,
        precision=lax.Precision.HIGH,
    ).reshape(3, levels, blocks, cells)
    post = collide_blocks(moments, wind, nudge, backward, relaxation_frequencies)
    present = jnp.any(living_brick_keys[None, :] == jnp.arange(blocks, dtype=jnp.int32)[:, None], axis=1)
    fluid = present.astype(jnp.float32)
    solid = jnp.broadcast_to((1.0 - fluid)[None, None, :, None], (1, levels, blocks, cells))
    extended = jnp.concatenate([post, solid], axis=0)
    width = channels + 1
    flat = lambda halo: halo.reshape(-1, BE)
    ahead, behind = ring_pairs("line")
    by_rows = extended.reshape(width, levels, TY, TX, BE, BE)
    column_shape = (width, levels, TY, BE)
    left_cols = lax.ppermute(flat(by_rows[:, :, :, TX - 1, :, BE - 1]), "line", ahead).reshape(column_shape)
    right_cols = lax.ppermute(flat(by_rows[:, :, :, 0, :, 0]), "line", behind).reshape(column_shape)
    corner = lambda cols, py, r: jnp.broadcast_to(cols[:, :, py:py + 1, r:r + 1], (width, levels, 1, BE))
    top_row = jnp.concatenate(
        [
            corner(left_cols, TY - 1, BE - 1),
            extended[:, :, blocks - TX:, cells - BE:],
            corner(right_cols, TY - 1, BE - 1),
        ],
        axis=2,
    )
    bottom_row = jnp.concatenate(
        [corner(left_cols, 0, 0), extended[:, :, :TX, :BE], corner(right_cols, 0, 0)], axis=2
    )
    ahead, behind = ring_pairs("curve")
    row_shape = (width, levels, TX + 2, BE)
    below = lax.ppermute(flat(top_row), "curve", ahead).reshape(row_shape)
    above = lax.ppermute(flat(bottom_row), "curve", behind).reshape(row_shape)
    below_flat = flat(below)
    above_flat = flat(above)
    from_left = flat(left_cols)
    from_right = flat(right_cols)
    new_state = stream(living_brick_keys, post, below_flat, above_flat, from_left, from_right)
    return new_state.reshape((1, 1, seats, channels, levels * cells))


def solution(mesh):
    return jax.shard_map(
        on_device,
        mesh=mesh,
        in_specs=(
            P("curve", "line", None, None, None),
            P("curve", "line", None),
            P(),
            P(None, None, "curve", None),
            P(),
        ),
        out_specs=P("curve", "line", None, None, None),
        check_vma=False,
    )
```

```python
import jax
import jax.numpy as jnp
import numpy as np
from jax import lax
from jax.experimental import pallas as pl
from jax.experimental.pallas import tpu as pltpu
from jax.sharding import PartitionSpec as P

BE = 16
TX = 4
TY = 2


NUDGE_GAIN = 0.5
TWO_PI = 6.283185307179586
HIGHEST = lax.Precision.HIGHEST


def butterfly_sum(value, axis):
    count = lax.axis_size(axis)
    stride = 1
    while stride < count:
        value = value + lax.ppermute(value, axis, [(i, i ^ stride) for i in range(count)])
        stride *= 2
    return value


def ring_pairs(axis):
    count = lax.axis_size(axis)
    forward = [(i, (i + 1) % count) for i in range(count)]
    backward = [(target, source) for source, target in forward]
    return forward, backward


def lattice_tables():
    one_weights = np.array([1.0 / 6.0, 2.0 / 3.0, 1.0 / 6.0])
    speeds = np.array(
        [
            [along_x - 1, along_y - 1, along_z - 1]
            for along_x in range(3)
            for along_y in range(3)
            for along_z in range(3)
        ]
    )
    weights = np.array(
        [
            one_weights[along_x] * one_weights[along_y] * one_weights[along_z]
            for along_x in range(3)
            for along_y in range(3)
            for along_z in range(3)
        ]
    )
    vander = np.array([[1.0, 1.0, 1.0], [-1.0, 0.0, 1.0], [1.0, 0.0, 1.0]])
    undo_vander = np.array([[0.0, -0.5, 0.5], [1.0, 0.0, -1.0], [0.0, 0.5, 0.5]])
    moment_matrix = np.kron(vander, np.kron(vander, vander))
    inverse = np.kron(undo_vander, np.kron(undo_vander, undo_vander))
    forward = jnp.asarray(moment_matrix * weights[None, :], dtype=jnp.float32)
    backward = jnp.asarray(inverse / weights[:, None], dtype=jnp.float32)
    return (forward, backward, speeds)


def mode_basis_at(mode_ids, positions, length):
    phase_ids = positions[:, None] * mode_ids[None, :] % length
    angles = phase_ids.astype(jnp.float32) * (TWO_PI / length)
    return jnp.concatenate([jnp.cos(angles), jnp.sin(angles)], axis=1)


def collide_blocks(moments, velocity, nudge, backward, relaxation_frequencies):
    density = moments[0]
    shifted = velocity + nudge
    powers = jnp.stack([jnp.ones_like(shifted), shifted, shifted * shifted + 1.0 / 3.0], axis=0)
    equilibrium = (
        density[None, None, None]
        * powers[:, None, None, 0]
        * powers[None, :, None, 1]
        * powers[None, None, :, 2]
    )
    equilibrium = equilibrium.reshape(moments.shape)
    relaxed = moments - relaxation_frequencies[:, None, None, None] * (moments - equilibrium)
    return jnp.einsum("ij,jzpl->izpl", backward, relaxed, precision=lax.Precision.HIGH)


def moments_kernel(keys_ref, forward_ref, state_ref, out_ref, wind_ref, scratch_ref):
    levels, blocks, channels, cells = out_ref.shape
    seats = scratch_ref.shape[0]
    chunks = levels * cells // 128
    forward = forward_ref[...]
    for seat_number in range(seats):
        pieces = [
            state_ref[pl.ds(seat_number * channels * chunks + chunk, channels, stride=chunks), :]
            for chunk in range(chunks)
        ]
        scratch_ref[seat_number] = jnp.dot(
            forward, jnp.concatenate(pieces, axis=1), precision=lax.Precision.HIGH,
            preferred_element_type=jnp.float32,
        )
    for block in range(blocks):
        slot = 0
        found = False
        for seat_number in range(seats):
            hit = keys_ref[seat_number] == block
            slot = jnp.where(hit, seat_number, slot)
            found = jnp.logical_or(found, hit)
        keep = jnp.where(found, 1.0, 0.0)
        for level in range(levels):
            values = scratch_ref[slot, :, level * cells:(level + 1) * cells] * keep
            out_ref[level, block] = values
            density = jnp.where(found, values[0:1], 1.0)
            for component, row in enumerate((9, 3, 1)):
                wind_ref[component, level, block:block + 1, :] = values[row:row + 1] / density


def cell_moments(keys, forward, rows, seats, levels):
    channels = forward.shape[0]
    blocks = TX * TY
    cells = rows.size // (seats * channels * levels)
    vmem = pl.BlockSpec(memory_space=pltpu.VMEM)
    smem = pl.BlockSpec(memory_space=pltpu.SMEM)
    return pl.pallas_call(
        moments_kernel,
        out_shape=(
            jax.ShapeDtypeStruct((levels, blocks, channels, cells), jnp.float32),
            jax.ShapeDtypeStruct((3, levels, blocks, cells), jnp.float32),
        ),
        in_specs=[smem, vmem, vmem],
        out_specs=(vmem, vmem),
        scratch_shapes=[pltpu.VMEM((seats, channels, levels * cells), jnp.float32)],
    )(keys, forward, rows)


def stream_kernel(
    keys_ref, post_ref, below_ref, above_ref, left_ref, right_ref, out_ref, spread_ref, column_ref, result_ref
):
    levels, blocks, channels, cells = post_ref.shape
    _, _, speeds = lattice_tables()
    front = 8
    grid_row = lax.broadcasted_iota(jnp.int32, (BE, cells), 0)
    grid_lane = lax.broadcasted_iota(jnp.int32, (BE, cells), 1)
    tile_copy = (grid_lane % BE == grid_row).astype(jnp.float32)
    group_copy = (grid_lane // BE == grid_row).astype(jnp.float32)
    row_count = below_ref.shape[0]
    column_count = left_ref.shape[0]
    for slot, source in enumerate((below_ref, above_ref)):
        spread_ref[slot, front:front + row_count, :] = jnp.dot(
            source[...], tile_copy, precision=lax.Precision.HIGH, preferred_element_type=jnp.float32
        )
    for slot, source in enumerate((left_ref, right_ref)):
        column_ref[slot, front:front + column_count, :] = jnp.dot(
            source[...], group_copy, precision=lax.Precision.HIGH, preferred_element_type=jnp.float32
        )
    lane = lax.broadcasted_iota(jnp.int32, (blocks, cells), 1)
    seat = lax.broadcasted_iota(jnp.int32, (blocks, cells), 0)
    q = lane % BE
    r = lane // BE
    py = seat // TX

    solid_plane = jnp.zeros((blocks, cells), jnp.float32)
    for block in range(blocks):
        found = False
        for seat_number in range(keys_ref.shape[0]):
            found = jnp.logical_or(found, keys_ref[seat_number] == block)
        solid_plane = jnp.where(seat == block, jnp.where(found, 0.0, 1.0), solid_plane)

    def own(channel, level):
        if channel == channels:
            return solid_plane
        return post_ref[level, :, channel, :]

    def moved(plane, shift):
        shift = shift % cells
        if shift == 0:
            return plane
        return pltpu.roll(plane, shift, 1)

    def gathered(channel, level, cx, cy):
        shift = cy * BE + cx
        entry = channel * levels + level
        first = front + entry * (TX + 2)
        first_column = front + entry * TY
        base = own(channel, level)
        if cy != 0:
            stepped = pltpu.roll(base, TX, 0)
            if cy == 1:
                halo = spread_ref[0, first + 1:first + 1 + blocks, :]
                yplane = jnp.where(py == 0, halo, stepped)
            else:
                halo = spread_ref[1, first + 1 - TX:first + 1 - TX + blocks, :]
                yplane = jnp.where(py == TY - 1, halo, stepped)

        def side_row(k, dx):
            corner_at = first if dx == 1 else first + TX + 1
            if k == 0:
                return spread_ref[0, corner_at:corner_at + 1, :]
            if k == TY + 1:
                return spread_ref[1, corner_at:corner_at + 1, :]
            at = first_column + k - 1
            return column_ref[0 if dx == 1 else 1, at:at + 1, :]

        def sideways(plane, dy, dx):
            plane = pltpu.roll(plane, dx % blocks, 0)
            edge = 0 if dx == 1 else TX - 1
            return jnp.where(
                seat == edge,
                side_row(1 - dy, dx),
                jnp.where(seat == edge + TX, side_row(2 - dy, dx), plane),
            )
        value = moved(base, shift)
        if cy != 0:
            ycross = r == (0 if cy == 1 else BE - 1)
            value = jnp.where(ycross, moved(yplane, shift), value)
        if cx != 0:
            xcross = q == (0 if cx == 1 else BE - 1)
            xvalue = moved(sideways(base, 0, cx), shift - BE * cx)
            if cy != 0:
                xvalue = jnp.where(ycross, moved(sideways(yplane, cy, cx), shift - BE * cx), xvalue)
            value = jnp.where(xcross, xvalue, value)
        return value

    blocked_of = {}
    for cx in (-1, 0, 1):
        for cy in (-1, 0, 1):
            blocked_of[(cx, cy)] = gathered(channels, 0, cx, cy) > 0.5
    for heading in range(27):
        cx, cy, cz = (int(v) for v in speeds[heading])
        blocked = blocked_of[(cx, cy)]
        for level in range(levels):
            bounced = post_ref[level, :, 26 - heading, :]
            window = pl.ds(level * cells, cells)
            if cz == 1 and level == 0:
                result_ref[:, heading, window] = bounced
                continue
            if cz == 0:
                source = gathered(heading, level, cx, cy)
            elif cz == 1:
                source = gathered(heading, 0, cx, cy)
            elif level == 0:
                source = gathered(heading, 1, cx, cy)
            else:
                source = gathered(heading + 2, 1, cx, cy)
            result_ref[:, heading, window] = jnp.where(blocked, bounced, source)
    chunks = levels * cells // 128
    for seat_number in range(keys_ref.shape[0]):
        key = keys_ref[seat_number]
        for chunk in range(chunks):
            picked = result_ref[jnp.maximum(key, 0), :, chunk * 128:(chunk + 1) * 128]
            rows = pl.ds(seat_number * channels * chunks + chunk, channels, stride=chunks)
            out_ref[rows, :] = jnp.where(key >= 0, picked, 0.0)


def stream(keys, post, below, above, from_left, from_right):
    channels, levels, blocks, cells = post.shape
    seats = keys.shape[0]
    row_count = below.shape[0]
    column_count = from_left.shape[0]
    vmem = pl.BlockSpec(memory_space=pltpu.VMEM)
    smem = pl.BlockSpec(memory_space=pltpu.SMEM)
    return pl.pallas_call(
        stream_kernel,
        out_shape=jax.ShapeDtypeStruct((seats * channels * levels * cells // 128, 128), jnp.float32),
        in_specs=[smem] + [vmem] * 5,
        out_specs=vmem,
        scratch_shapes=[
            pltpu.VMEM((2, row_count + 16, cells), jnp.float32),
            pltpu.VMEM((2, column_count + 16, cells), jnp.float32),
            pltpu.VMEM((blocks, channels, levels * cells), jnp.float32),
        ],
    )(keys, post.transpose(1, 2, 0, 3), below, above, from_left, from_right)


def on_device(
    scaled_distributions,
    remaining_brick_places,
    retained_wavenumbers,
    regional_amplitudes,
    relaxation_frequencies,
):
    forward, backward, speeds = lattice_tables()
    slot_state = scaled_distributions[0, 0]
    living_brick_keys = remaining_brick_places[0, 0]
    seats = living_brick_keys.shape[0]
    channels = slot_state.shape[1]
    cells = BE * BE
    levels = slot_state.shape[2] // cells
    blocks = TX * TY
    rows_tile = TY * BE
    cols_tile = TX * BE
    rows = slot_state.reshape(-1, 128)
    moments, wind = cell_moments(living_brick_keys, forward, rows, seats, levels)
    moments = moments.transpose(2, 0, 1, 3)
    line_length = lax.axis_size("line") * cols_tile
    own_columns = lax.axis_index("line") * cols_tile + jnp.arange(cols_tile, dtype=jnp.int32)
    mode_basis = mode_basis_at(retained_wavenumbers, own_columns, line_length).reshape(TX, BE, -1)
    partial = jnp.einsum(
        "kzyxrq,xqm->kzyrm", wind.reshape(3, levels, TY, TX, BE, BE), mode_basis,
        precision=lax.Precision.HIGH,
    ).reshape(3, levels, rows_tile, -1)
    coefficients = butterfly_sum(partial, "line")
    misfit = regional_amplitudes - 2.0 / line_length * coefficients
    nudge = NUDGE_GAIN * jnp.einsum(
        "kzyrm,xqm->kzyxrq", misfit.reshape(3, levels, TY, BE, -1), mode_basis,
        precision=lax.Precision.HIGH,
    ).reshape(3, levels, blocks, cells)
    post = collide_blocks(moments, wind, nudge, backward, relaxation_frequencies)
    present = jnp.any(living_brick_keys[None, :] == jnp.arange(blocks, dtype=jnp.int32)[:, None], axis=1)
    fluid = present.astype(jnp.float32)
    solid = jnp.broadcast_to((1.0 - fluid)[None, None, :, None], (1, levels, blocks, cells))
    extended = jnp.concatenate([post, solid], axis=0)
    width = channels + 1
    flat = lambda halo: halo.reshape(-1, BE)
    ahead, behind = ring_pairs("line")
    by_rows = extended.reshape(width, levels, TY, TX, BE, BE)
    column_shape = (width, levels, TY, BE)
    left_cols = lax.ppermute(flat(by_rows[:, :, :, TX - 1, :, BE - 1]), "line", ahead).reshape(column_shape)
    right_cols = lax.ppermute(flat(by_rows[:, :, :, 0, :, 0]), "line", behind).reshape(column_shape)
    corner = lambda cols, py, r: jnp.broadcast_to(cols[:, :, py:py + 1, r:r + 1], (width, levels, 1, BE))
    top_row = jnp.concatenate(
        [
            corner(left_cols, TY - 1, BE - 1),
            extended[:, :, blocks - TX:, cells - BE:],
            corner(right_cols, TY - 1, BE - 1),
        ],
        axis=2,
    )
    bottom_row = jnp.concatenate(
        [corner(left_cols, 0, 0), extended[:, :, :TX, :BE], corner(right_cols, 0, 0)], axis=2
    )
    ahead, behind = ring_pairs("curve")
    row_shape = (width, levels, TX + 2, BE)
    below = lax.ppermute(flat(top_row), "curve", ahead).reshape(row_shape)
    above = lax.ppermute(flat(bottom_row), "curve", behind).reshape(row_shape)
    below_flat = flat(below)
    above_flat = flat(above)
    from_left = flat(left_cols)
    from_right = flat(right_cols)
    new_state = stream(living_brick_keys, post, below_flat, above_flat, from_left, from_right)
    return new_state.reshape((1, 1, seats, channels, levels * cells))


def solution(mesh):
    return jax.shard_map(
        on_device,
        mesh=mesh,
        in_specs=(
            P("curve", "line", None, None, None),
            P("curve", "line", None),
            P(),
            P(None, None, "curve", None),
            P(),
        ),
        out_specs=P("curve", "line", None, None, None),
        check_vma=False,
    )
```
